128 devices in a mesh: lat: 4 (over z), lon: 32 (over x, y, core).
Axes of the slice: x: 4, y: 4, z: 4, core: 2. Of those that a mesh axis runs over, the one named last changes fastest.
Arguments:
- column_state: float32 [4, 32, 128, 4096], P(None, None, 'lat', 'lon'), may hold values from -6 to 6
- wind_speed: float32 [2, 32, 128, 4096], P(None, None, 'lat', 'lon'), may hold values from -0.4 to 0.4
- diffusivity: float32 [32, 128, 4096], P(None, 'lat', 'lon'), may hold values from 0.02 to 0.2
- batch_index: int32 [4, 131072, 1], P('lat', 'lon'), may hold values from 0 to 31; in each aligned block of 4096 rows (0 to 4095, 4096 to 8191, ..., all dimensions but the last counted through in order) at most 256 rows name the same one
- input_weight: bfloat16 [32, 512, 128], P('lon'), may hold values from -0.5 to 0.5
- middle_weight: bfloat16 [32, 3, 512, 512], P('lon'), may hold values from -0.25 to 0.25
- output_weight: bfloat16 [32, 128, 512], P('lon'), may hold values from -0.25 to 0.25
Outputs:
- new_state: float32 [4, 32, 128, 4096], P(None, None, 'lat', 'lon')
The draws below stay inside these ranges and needn't reach their ends.
Inputs may be any that keep to these rules, and one draw needn't show every extreme that they name: `batch_index`: within the columns of one device no batch is named more than 256 times; some device names some batch exactly 256 times.
All inputs are finite; a program needn't handle non-finite values.
Results may differ from the reference program's by a relative error of at most 0.0012.
Values may be sent and summed in bfloat16 or wider, within the bound.
No kernel may reach another device: no remote copies, remote signals or barrier semaphores. Data moves between devices by JAX's collectives and lax.ppermute only.
A program may use at most 128 MiB of HBM per device.

```python
import math
import jax
import jax.numpy as jnp
import numpy as np
from jax import lax

VARS = 4
LEV = 32
HID = 512
LAYERS = 5
CLAT = 32
CLON = 128
FEAT = 128
COLS = 4096
EXPERTS = 32
CAP = 256
GLAT = 128
GLON = 4096
N_LAT = 4
N_LON = 32


def levels(own_key, dims, split, least, top_value):
    level = 1.0
    for dim, shards_of in split:
        steps = jax.random.uniform(jax.random.fold_in(jax.random.fold_in(own_key, 6), dim), (shards_of,), jnp.float32, least / len(split), top_value / len(split))
        level = level * jnp.repeat(jnp.exp(steps), dims[dim] // shards_of).reshape((-1,) + (1,) * (len(dims) - 1 - dim))
    return level


def shared_out(own_key, own, number, rows, count, top, limit, skew):
    order = jax.random.permutation(own_key, count)
    heavy_load, usual = shares(count, rows * top, limit, skew, True), shares(count, rows * top, limit, skew, False)
    places = jnp.arange(count)

    def named(lengths, rotation):
        used = int((lengths > 0).sum())
        fixed = max(1, used // 4)
        passed = fixed + (places - fixed + rotation * (used - fixed)) % max(1, count - fixed)
        return jnp.zeros((count,), jnp.int32).at[order[jnp.where(places < fixed, places, passed)]].set(jnp.asarray(lengths, jnp.int32))

    lengths = jnp.where(number % 4 == 0, named(heavy_load, number // 4), named(usual, number - number // 4 - 1))
    mixed = jax.random.permutation(jax.random.fold_in(own, 3), count)
    giver, receiver = mixed[0:count // 2 * 2:2], mixed[1:count // 2 * 2:2]
    room = jnp.minimum(lengths[giver] - 1, limit - lengths[receiver]) // 2
    room = jnp.where((giver == order[0]) | (receiver == order[0]) | (lengths[receiver] == 0), 0, jnp.maximum(room, 0))
    passed = jax.random.randint(jax.random.fold_in(own, 4), (count // 2,), 0, 1 << 20) % (room + 1)
    lengths = lengths.at[giver].add(-passed).at[receiver].add(passed)
    items = jnp.searchsorted(jnp.cumsum(lengths), jnp.arange(rows * top), side="right").astype(jnp.int32)
    grid = items.reshape(top, rows).T
    grid = grid[jax.random.permutation(jax.random.fold_in(own, 1), rows)]
    rotation = jax.random.randint(jax.random.fold_in(own, 2), (rows, 1), 0, top)
    return jnp.take_along_axis(grid, (jnp.arange(top)[None, :] + rotation) % top, axis=1)


def shares(number_of, total, most, slope, full):
    weights = [(1 << 20) // math.isqrt(standing ** slope) + 1 for standing in range(1, number_of + 1)]
    largest = most if full else min(most, max(-(-total // number_of), total * weights[0] // sum(weights)))
    least = 1 if total - largest >= number_of - 1 else 0
    holding, surplus = [largest] + [least] * (number_of - 1), total - largest - least * (number_of - 1)
    while surplus > 0:
        movable = [i for i in range(1, number_of) if holding[i] < largest] or [i for i in range(1, number_of) if holding[i] < most]
        whole, remaining = sum([weights[i] for i in movable]), surplus
        for i in movable:
            more = min(most - holding[i], max(1, remaining * weights[i] // whole), surplus)
            holding[i] = holding[i] + more
            surplus = surplus - more
    return np.array(holding)


def noise(key, shape, width, limit, shards=(), kind=jnp.bfloat16):
    entries = jax.random.normal(key, shape, jnp.float32) * width
    if len(shards) > 0:
        entries = levels(key, shape, shards, -0.22, 0.18) * entries
    return jnp.clip(entries, min=-limit, max=limit).astype(kind)


def setup_inputs(seed: int = 0) -> dict:
    keys = jax.random.split(jax.random.key(seed), 8)
    column_state = noise(keys[0], (VARS, LEV, GLAT, GLON), 1.0, 6.0, ((2, 4), (3, 32)), jnp.float32)
    wind_speed = jnp.clip(jax.random.uniform(keys[1], (2, LEV, GLAT, GLON), jnp.float32, -0.4, 0.4) * levels(keys[1], (2, LEV, GLAT, GLON), ((2, 4), (3, 32)), -0.4, 0.0), -0.4, 0.4)
    diffusivity = jnp.clip(jnp.exp(math.log(0.2) - 2.3025851 * jax.random.uniform(keys[2], (LEV, GLAT, GLON), jnp.float32) ** levels(keys[2], (LEV, GLAT, GLON), ((1, 4), (2, 32)), -0.2, 0.2)), 0.02, 0.2)
    batch_index_keys = jax.random.split(jax.random.fold_in(keys[3], 1), N_LAT * (N_LON * COLS) // COLS)
    batch_index_turns = jax.random.permutation(jax.random.fold_in(keys[3], 3), N_LAT * (N_LON * COLS) // COLS)
    batch_index = jax.vmap(lambda own, number: shared_out(jax.random.fold_in(keys[3], 2), own, number, COLS, EXPERTS, 1, CAP, 2))(batch_index_keys, batch_index_turns).reshape((N_LAT, N_LON * COLS, 1))
    input_weight = noise(keys[4], (EXPERTS, HID, FEAT), FEAT ** -0.5, 0.5, ((0, 32),))
    middle_weight = noise(keys[5], (EXPERTS, LAYERS - 2, HID, HID), HID ** -0.5, 0.25, ((0, 32),))
    output_weight = noise(keys[6], (EXPERTS, FEAT, HID), HID ** -0.5, 0.25, ((0, 32),))
    return dict(column_state=column_state, wind_speed=wind_speed, diffusivity=diffusivity, batch_index=batch_index, input_weight=input_weight, middle_weight=middle_weight, output_weight=output_weight)


def advect(extended, east_wind, north_wind, spread):
    middle = extended[:, :, 1:-1, 1:-1]
    north_cell = extended[:, :, 2:, 1:-1]
    south_cell = extended[:, :, :-2, 1:-1]
    east_cell = extended[:, :, 1:-1, 2:]
    west_cell = extended[:, :, 1:-1, :-2]
    return (middle - 0.5 * east_wind * (east_cell - west_cell)
            - 0.5 * north_wind * (north_cell - south_cell)
            + spread * (east_cell + west_cell + north_cell + south_cell - 4.0 * middle))


def extend(current):
    padded = jnp.pad(current, ((0, 0), (0, 0), (1, 1), (0, 0)))
    return jnp.concatenate([padded[:, :, :, -1:], padded, padded[:, :, :, :1]], axis=3)


def run_network(inputs, first_weight, middle_all, last_weight):
    hidden = jax.nn.silu(jnp.dot(first_weight, inputs, preferred_element_type=jnp.float32)).astype(jnp.bfloat16)
    for layer_index in range(middle_all.shape[0]):
        hidden = jax.nn.silu(jnp.dot(middle_all[layer_index], hidden, preferred_element_type=jnp.float32)).astype(jnp.bfloat16)
    return jnp.dot(last_weight, hidden, preferred_element_type=jnp.float32).astype(jnp.bfloat16)


def place_columns(values, indices):
    return jnp.zeros((FEAT, EXPERTS * CAP), jnp.bfloat16).at[:, indices].set(values)


def reference(column_state, wind_speed, diffusivity, batch_index, input_weight, middle_weight, output_weight):
    current = column_state
    for sweep_index in range(2):
        current = advect(extend(current), wind_speed[0], wind_speed[1], diffusivity)
    swept_state = current
    device_count = N_LAT * N_LON
    tile_values = swept_state.reshape(VARS, LEV, N_LAT, CLAT, N_LON, CLON).transpose(2, 4, 0, 1, 3, 5)
    columns = tile_values.reshape(device_count, FEAT, COLS).astype(jnp.bfloat16)
    targets_all = batch_index.reshape(device_count, COLS).astype(jnp.int32)
    onehot = (targets_all[:, :, None] == jnp.arange(EXPERTS, dtype=jnp.int32)[None, None, :]).astype(jnp.int32)
    position = jnp.sum((jnp.cumsum(onehot, axis=1) - onehot) * onehot, axis=2).astype(jnp.int32)
    targets = (targets_all * CAP + position).astype(jnp.int32)
    buffer = jax.vmap(place_columns)(columns, targets)

    def run_batch(packed):
        number, first_weight, middle_all, last_weight = packed
        selected = lax.dynamic_slice_in_dim(buffer, (number * CAP).astype(jnp.int32), CAP, axis=2)
        inputs = selected.transpose(1, 0, 2).reshape(FEAT, device_count * CAP)
        return run_network(inputs, first_weight, middle_all, last_weight)

    outputs = lax.map(run_batch, (jnp.arange(EXPERTS, dtype=jnp.int32), input_weight, middle_weight, output_weight))
    outputs = outputs.reshape(EXPERTS, FEAT, device_count, CAP).transpose(2, 1, 0, 3).reshape(device_count, FEAT, EXPERTS * CAP)
    tendency = jnp.take_along_axis(outputs, targets[:, None, :], axis=2)
    restored = tendency.astype(jnp.float32).reshape(N_LAT, N_LON, VARS, LEV, CLAT, CLON).transpose(2, 3, 0, 4, 1, 5)
    return swept_state + restored.reshape(VARS, LEV, GLAT, GLON)
```

```python
import jax
import jax.numpy as jnp
from jax import lax
from jax.sharding import PartitionSpec as P


def shifted(axis, pieces, periodic):
    count = lax.axis_size(axis)
    forward = [(i, i + 1) for i in range(count - 1)]
    if periodic:
        forward.append((count - 1, 0))
    backward = [(target, source) for source, target in forward]
    low_parts, high_parts = pieces
    low = lax.ppermute(low_parts, axis, forward)
    high = lax.ppermute(high_parts, axis, backward)
    return low, high


def pack(arrays):
    flat = jnp.concatenate([a.reshape(-1) for a in arrays])
    return flat


def unpack(flat, shapes):
    out, start = [], 0
    for shape in shapes:
        size = 1
        for s in shape:
            size *= s
        out.append(flat[start:start + size].reshape(shape))
        start += size
    return out


def advect(extended, east_wind, north_wind, spread):
    middle = extended[:, :, 1:-1, 1:-1]
    north_cell = extended[:, :, 2:, 1:-1]
    south_cell = extended[:, :, :-2, 1:-1]
    east_cell = extended[:, :, 1:-1, 2:]
    west_cell = extended[:, :, 1:-1, :-2]
    return (
        middle
        - 0.5 * east_wind * (east_cell - west_cell)
        - 0.5 * north_wind * (north_cell - south_cell)
        + spread * (east_cell + west_cell + north_cell + south_cell - 4.0 * middle)
    )


def widen(q, fields):
    v, l, rows, cols = q.shape
    top = [q[:, :, rows - 2:, :]] + [f[:, rows - 1:, :] for f in fields]
    bottom = [q[:, :, :2, :]] + [f[:, :1, :] for f in fields]
    lat_shapes = [a.shape for a in top]
    low, high = shifted("lat", (pack(top), pack(bottom)), False)
    low, high = unpack(low, lat_shapes), unpack(high, lat_shapes)
    q = jnp.concatenate([low[0], q, high[0]], axis=2)
    fields = [jnp.concatenate([lo, f, hi], axis=1) for lo, f, hi in zip(low[1:], fields, high[1:])]
    east = [jnp.swapaxes(q[..., cols - 2:], -1, -2)] + [jnp.swapaxes(f[..., cols - 1:], -1, -2) for f in fields]
    west = [jnp.swapaxes(q[..., :2], -1, -2)] + [jnp.swapaxes(f[..., :1], -1, -2) for f in fields]
    lon_shapes = [a.shape for a in east]
    low, high = shifted("lon", (pack(east), pack(west)), True)
    low, high = unpack(low, lon_shapes), unpack(high, lon_shapes)
    q = jnp.concatenate([jnp.swapaxes(low[0], -1, -2), q, jnp.swapaxes(high[0], -1, -2)], axis=3)
    fields = [
        jnp.concatenate([jnp.swapaxes(lo, -1, -2), f, jnp.swapaxes(hi, -1, -2)], axis=2)
        for lo, f, hi in zip(low[1:], fields, high[1:])
    ]
    return q, fields


def positions(targets_all, experts):
    count = targets_all.shape[0]
    block = 128
    onehot = (targets_all[:, None] == jnp.arange(experts, dtype=jnp.int32)[None, :]).astype(
        jnp.bfloat16
    )
    blocks = onehot.reshape(count // block, block, experts)
    rows = jnp.arange(block, dtype=jnp.int32)
    before = (rows[:, None] > rows[None, :]).astype(jnp.bfloat16)
    within = jnp.einsum("ij,bje->bie", before, blocks, preferred_element_type=jnp.float32)
    totals = jnp.sum(blocks.astype(jnp.float32), axis=1)
    offsets = jnp.cumsum(totals, axis=0) - totals
    ranks = within + offsets[:, None, :]
    position = jnp.sum(ranks * blocks.astype(jnp.float32), axis=2)
    return position.reshape(count).astype(jnp.int32)


def local(
    column_state, wind_speed, diffusivity, batch_index, input_weight, middle_weight, output_weight
):
    num_vars, levels, lat_cells, lon_cells = column_state.shape
    q, (east_wind, north_wind, spread) = widen(
        column_state, [wind_speed[0], wind_speed[1], diffusivity]
    )
    first = advect(q, east_wind, north_wind, spread)
    lat_index = lax.axis_index("lat")
    lat_count = lax.axis_size("lat")
    row = jnp.arange(lat_cells + 2)[None, None, :, None]
    outside = ((row == 0) & (lat_index == 0)) | ((row == lat_cells + 1) & (lat_index == lat_count - 1))
    first = jnp.where(outside, 0.0, first)
    current = advect(first, east_wind[:, 1:-1, 1:-1], north_wind[:, 1:-1, 1:-1], spread[:, 1:-1, 1:-1])
    features = num_vars * levels
    column_count = lat_cells * lon_cells
    columns = current.reshape(features, column_count).astype(jnp.bfloat16)
    experts = lax.axis_size("lon")
    capacity = 2 * column_count // experts
    targets_all = batch_index.reshape(column_count)
    position = positions(targets_all, experts)
    targets = targets_all * capacity + position
    packed = jnp.zeros((features, experts * capacity), jnp.bfloat16).at[:, targets].set(columns)
    packed = packed.reshape(features, experts, capacity)
    received = lax.all_to_all(packed, "lon", split_axis=1, concat_axis=1, tiled=True)
    layout = received.shape
    flattened = received.reshape(layout[0], layout[1] * layout[2])
    hidden = jax.nn.silu(
        jnp.dot(input_weight[0], flattened, preferred_element_type=jnp.float32)
    ).astype(jnp.bfloat16)
    for layer_index in range(middle_weight.shape[1]):
        hidden = jax.nn.silu(
            jnp.dot(middle_weight[0, layer_index], hidden, preferred_element_type=jnp.float32)
        ).astype(jnp.bfloat16)
    result = jnp.dot(output_weight[0], hidden, preferred_element_type=jnp.float32).astype(
        jnp.bfloat16
    )
    answered = result.reshape(layout)
    returned = lax.all_to_all(answered, "lon", split_axis=1, concat_axis=1, tiled=True)
    tendency = returned.reshape(features, -1)[:, targets]
    return current + tendency.astype(jnp.float32).reshape(current.shape)


def solution(mesh):
    in_specs = (
        P(None, None, "lat", "lon"),
        P(None, None, "lat", "lon"),
        P(None, "lat", "lon"),
        P("lat", "lon", None),
        P("lon", None, None),
        P("lon", None, None, None),
        P("lon", None, None),
    )
    out_specs = P(None, None, "lat", "lon")
    return jax.shard_map(local, mesh=mesh, in_specs=in_specs, out_specs=out_specs, check_vma=False)
```

```python
import jax
import jax.numpy as jnp
from jax import lax
from jax.experimental import pallas as pl
from jax.experimental.pallas import tpu as pltpu
from jax.sharding import PartitionSpec as P


def neighbours(axis, periodic):
    count = lax.axis_size(axis)
    forward = [(i, i + 1) for i in range(count - 1)]
    if periodic:
        forward.append((count - 1, 0))
    backward = [(target, source) for source, target in forward]
    return forward, backward


FB = 32

def sweep_kernel(q_ref, hn_ref, hs_ref, he_ref, hw_ref, u_ref, v_ref, k_ref, o_ref):
    rows, cols = q_ref.shape[1], q_ref.shape[2]
    row = lax.broadcasted_iota(jnp.int32, (rows, cols), 0)
    lane = lax.broadcasted_iota(jnp.int32, (rows, cols), 1)
    he = he_ref[0]
    hw = hw_ref[0]
    for f in range(FB):
        q = q_ref[f]
        north = jnp.where(row == rows - 1, jnp.broadcast_to(hn_ref[f], (rows, cols)), pltpu.roll(q, rows - 1, 0))
        south = jnp.where(row == 0, jnp.broadcast_to(hs_ref[f], (rows, cols)), pltpu.roll(q, 1, 0))
        east = jnp.where(lane == cols - 1, jnp.broadcast_to(he[:, f:f + 1], (rows, cols)), pltpu.roll(q, cols - 1, 1))
        west = jnp.where(lane == 0, jnp.broadcast_to(hw[:, f:f + 1], (rows, cols)), pltpu.roll(q, 1, 1))
        u = u_ref[f]
        v = v_ref[f]
        k = k_ref[f]
        o_ref[f] = (q - 0.5 * u * (east - west) - 0.5 * v * (north - south)
                    + k * (east + west + north + south - 4.0 * q))


def sweep(q, hn, hs, he, hw, u, v, k):
    feats, rows, cols = q.shape
    levels = u.shape[0]
    nb = feats // FB
    per = levels // FB
    big = pl.BlockSpec((FB, rows, cols), lambda i: (i, 0, 0))
    field = pl.BlockSpec((FB, rows, cols), lambda i: (i % per, 0, 0))
    edge_row = pl.BlockSpec((FB, 1, cols), lambda i: (i, 0, 0))
    edge_col = pl.BlockSpec((1, rows, FB), lambda i: (i, 0, 0))
    return pl.pallas_call(
        sweep_kernel,
        grid=(nb,),
        in_specs=[big, edge_row, edge_row, edge_col, edge_col, field, field, field],
        out_specs=big,
        out_shape=jax.ShapeDtypeStruct(q.shape, q.dtype),
        cost_estimate=pl.CostEstimate(flops=20 * q.size, bytes_accessed=8 * q.size + 12 * u.size, transcendentals=0),
    )(q, hn, hs, he, hw, u, v, k)


def columns_of(edge):
    feats, rows = edge.shape
    return jnp.swapaxes(edge.reshape(feats // FB, FB, rows), 1, 2)


def step(x, u, v, k):
    feats, rows, cols = x.shape
    lat_forward, lat_backward = neighbours("lat", False)
    lon_forward, lon_backward = neighbours("lon", True)
    hn = lax.ppermute(x[:, :1, :], "lat", lat_backward)
    hs = lax.ppermute(x[:, rows - 1:, :], "lat", lat_forward)
    he = lax.ppermute(columns_of(x[:, :, 0]), "lon", lon_backward)
    hw = lax.ppermute(columns_of(x[:, :, cols - 1]), "lon", lon_forward)
    return sweep(x, hn, hs, he, hw, u, v, k)


def positions(targets_all, experts):
    count = targets_all.shape[0]
    block = 128
    onehot = (targets_all[:, None] == jnp.arange(experts, dtype=jnp.int32)[None, :]).astype(
        jnp.bfloat16
    )
    blocks = onehot.reshape(count // block, block, experts)
    rows = jnp.arange(block, dtype=jnp.int32)
    before = (rows[:, None] > rows[None, :]).astype(jnp.bfloat16)
    within = jnp.einsum("ij,bje->bie", before, blocks, preferred_element_type=jnp.float32)
    totals = jnp.sum(blocks.astype(jnp.float32), axis=1)
    offsets = jnp.cumsum(totals, axis=0) - totals
    ranks = within + offsets[:, None, :]
    position = jnp.sum(ranks * blocks.astype(jnp.float32), axis=2)
    return position.reshape(count).astype(jnp.int32)


def local(
    column_state, wind_speed, diffusivity, batch_index, input_weight, middle_weight, output_weight
):
    num_vars, levels, lat_cells, lon_cells = column_state.shape
    features = num_vars * levels
    current = column_state.reshape(features, lat_cells, lon_cells)
    for sweep_index in range(2):
        current = step(current, wind_speed[0], wind_speed[1], diffusivity)
    column_count = lat_cells * lon_cells
    columns = current.reshape(features, column_count).astype(jnp.bfloat16)
    experts = lax.axis_size("lon")
    capacity = 2 * column_count // experts
    targets_all = batch_index.reshape(column_count)
    position = positions(targets_all, experts)
    targets = targets_all * capacity + position
    packed = jnp.zeros((features, experts * capacity), jnp.bfloat16).at[:, targets].set(columns)
    packed = packed.reshape(features, experts, capacity)
    received = lax.all_to_all(packed, "lon", split_axis=1, concat_axis=1, tiled=True)
    layout = received.shape
    flattened = received.reshape(layout[0], layout[1] * layout[2])
    hidden = jax.nn.silu(
        jnp.dot(input_weight[0], flattened, preferred_element_type=jnp.float32)
    ).astype(jnp.bfloat16)
    for layer_index in range(middle_weight.shape[1]):
        hidden = jax.nn.silu(
            jnp.dot(middle_weight[0, layer_index], hidden, preferred_element_type=jnp.float32)
        ).astype(jnp.bfloat16)
    result = jnp.dot(output_weight[0], hidden, preferred_element_type=jnp.float32).astype(
        jnp.bfloat16
    )
    answered = result.reshape(layout)
    returned = lax.all_to_all(answered, "lon", split_axis=1, concat_axis=1, tiled=True)
    tendency = returned.reshape(features, -1)[:, targets]
    return (current + tendency.astype(jnp.float32).reshape(current.shape)).reshape(column_state.shape)


def solution(mesh):
    in_specs = (
        P(None, None, "lat", "lon"),
        P(None, None, "lat", "lon"),
        P(None, "lat", "lon"),
        P("lat", "lon", None),
        P("lon", None, None),
        P("lon", None, None, None),
        P("lon", None, None),
    )
    out_specs = P(None, None, "lat", "lon")
    return jax.shard_map(local, mesh=mesh, in_specs=in_specs, out_specs=out_specs, check_vma=False)
```

```python
import jax
import jax.numpy as jnp
from jax import lax
from jax.experimental import pallas as pl
from jax.experimental.pallas import tpu as pltpu
from jax.sharding import PartitionSpec as P


def neighbours(axis, periodic):
    count = lax.axis_size(axis)
    forward = [(i, i + 1) for i in range(count - 1)]
    if periodic:
        forward.append((count - 1, 0))
    backward = [(target, source) for source, target in forward]
    return forward, backward


FB = 32

def sweep_kernel(q_ref, hn_ref, hs_ref, he_ref, hw_ref, u_ref, v_ref, k_ref, o_ref):
    rows, cols = q_ref.shape[1], q_ref.shape[2]
    row = lax.broadcasted_iota(jnp.int32, (rows, cols), 0)
    lane = lax.broadcasted_iota(jnp.int32, (rows, cols), 1)
    he = he_ref[0]
    hw = hw_ref[0]
    for f in range(FB):
        q = q_ref[f]
        north = jnp.where(row == rows - 1, jnp.broadcast_to(hn_ref[f], (rows, cols)), pltpu.roll(q, rows - 1, 0))
        south = jnp.where(row == 0, jnp.broadcast_to(hs_ref[f], (rows, cols)), pltpu.roll(q, 1, 0))
        east = jnp.where(lane == cols - 1, jnp.broadcast_to(he[:, f:f + 1], (rows, cols)), pltpu.roll(q, cols - 1, 1))
        west = jnp.where(lane == 0, jnp.broadcast_to(hw[:, f:f + 1], (rows, cols)), pltpu.roll(q, 1, 1))
        u = u_ref[f]
        v = v_ref[f]
        k = k_ref[f]
        o_ref[f] = (q - 0.5 * u * (east - west) - 0.5 * v * (north - south)
                    + k * (east + west + north + south - 4.0 * q))


def sweep(q, hn, hs, he, hw, u, v, k):
    feats, rows, cols = q.shape
    levels = u.shape[0]
    nb = feats // FB
    per = levels // FB
    big = pl.BlockSpec((FB, rows, cols), lambda i: (i, 0, 0))
    field = pl.BlockSpec((FB, rows, cols), lambda i: (i % per, 0, 0))
    edge_row = pl.BlockSpec((FB, 1, cols), lambda i: (i, 0, 0))
    edge_col = pl.BlockSpec((1, rows, FB), lambda i: (i, 0, 0))
    return pl.pallas_call(
        sweep_kernel,
        grid=(nb,),
        in_specs=[big, edge_row, edge_row, edge_col, edge_col, field, field, field],
        out_specs=big,
        out_shape=jax.ShapeDtypeStruct(q.shape, q.dtype),
        cost_estimate=pl.CostEstimate(flops=20 * q.size, bytes_accessed=8 * q.size + 12 * u.size, transcendentals=0),
    )(q, hn, hs, he, hw, u, v, k)


def columns_of(edge):
    feats, rows = edge.shape
    return jnp.swapaxes(edge.reshape(feats // FB, FB, rows), 1, 2)


def step(x, u, v, k):
    feats, rows, cols = x.shape
    lat_forward, lat_backward = neighbours("lat", False)
    lon_forward, lon_backward = neighbours("lon", True)
    hn = lax.ppermute(x[:, :1, :], "lat", lat_backward)
    hs = lax.ppermute(x[:, rows - 1:, :], "lat", lat_forward)
    he = lax.ppermute(columns_of(x[:, :, 0]), "lon", lon_backward)
    hw = lax.ppermute(columns_of(x[:, :, cols - 1]), "lon", lon_forward)
    return sweep(x, hn, hs, he, hw, u, v, k)


def positions(targets_all, experts):
    count = targets_all.shape[0]
    block = 128
    onehot = (targets_all[:, None] == jnp.arange(experts, dtype=jnp.int32)[None, :]).astype(
        jnp.bfloat16
    )
    blocks = onehot.reshape(count // block, block, experts)
    rows = jnp.arange(block, dtype=jnp.int32)
    before = (rows[:, None] > rows[None, :]).astype(jnp.bfloat16)
    within = jnp.einsum("ij,bje->bie", before, blocks, preferred_element_type=jnp.float32)
    totals = jnp.sum(blocks.astype(jnp.float32), axis=1)
    offsets = jnp.cumsum(totals, axis=0) - totals
    ranks = within + offsets[:, None, :]
    position = jnp.sum(ranks * blocks.astype(jnp.float32), axis=2)
    return position.reshape(count).astype(jnp.int32)


def network(flattened, input_weight, middle_weight, output_weight):
    hidden = jax.nn.silu(
        jnp.dot(input_weight[0], flattened, preferred_element_type=jnp.float32)
    ).astype(jnp.bfloat16)
    for layer_index in range(middle_weight.shape[1]):
        hidden = jax.nn.silu(
            jnp.dot(middle_weight[0, layer_index], hidden, preferred_element_type=jnp.float32)
        ).astype(jnp.bfloat16)
    return jnp.dot(output_weight[0], hidden, preferred_element_type=jnp.float32).astype(
        jnp.bfloat16
    )


def local(
    column_state, wind_speed, diffusivity, batch_index, input_weight, middle_weight, output_weight
):
    num_vars, levels, lat_cells, lon_cells = column_state.shape
    features = num_vars * levels
    current = column_state.reshape(features, lat_cells, lon_cells)
    for sweep_index in range(2):
        current = step(current, wind_speed[0], wind_speed[1], diffusivity)
    column_count = lat_cells * lon_cells
    columns = current.reshape(features, column_count).astype(jnp.bfloat16)
    experts = lax.axis_size("lon")
    capacity = 2 * column_count // experts
    targets_all = batch_index.reshape(column_count)
    position = positions(targets_all, experts)
    targets = targets_all * capacity + position
    packed = jnp.zeros((features, experts * capacity), jnp.bfloat16).at[:, targets].set(columns)
    packed = packed.reshape(features, experts, capacity)
    chunks = 2
    width = capacity // chunks
    answers = []
    for chunk in range(chunks):
        part = packed[:, :, chunk * width:(chunk + 1) * width]
        received = lax.all_to_all(part, "lon", split_axis=1, concat_axis=1, tiled=True)
        result = network(received.reshape(features, experts * width), input_weight, middle_weight, output_weight)
        answers.append(
            lax.all_to_all(result.reshape(features, experts, width), "lon", split_axis=1, concat_axis=1, tiled=True)
        )
    returned = jnp.concatenate(answers, axis=2)
    tendency = returned.reshape(features, -1)[:, targets]
    return (current + tendency.astype(jnp.float32).reshape(current.shape)).reshape(column_state.shape)


def solution(mesh):
    in_specs = (
        P(None, None, "lat", "lon"),
        P(None, None, "lat", "lon"),
        P(None, "lat", "lon"),
        P("lat", "lon", None),
        P("lon", None, None),
        P("lon", None, None, None),
        P("lon", None, None),
    )
    out_specs = P(None, None, "lat", "lon")
    return jax.shard_map(local, mesh=mesh, in_specs=in_specs, out_specs=out_specs, check_vma=False)
```

```python
import jax
import jax.numpy as jnp
from jax import lax
from jax.experimental import pallas as pl
from jax.experimental.pallas import tpu as pltpu
from jax.sharding import PartitionSpec as P


def neighbours(axis, periodic):
    count = lax.axis_size(axis)
    forward = [(i, i + 1) for i in range(count - 1)]
    if periodic:
        forward.append((count - 1, 0))
    backward = [(target, source) for source, target in forward]
    return forward, backward


FB = 32

def sweep_kernel(q_ref, hn_ref, hs_ref, he_ref, hw_ref, u_ref, v_ref, k_ref, o_ref):
    rows, cols = q_ref.shape[1], q_ref.shape[2]
    row = lax.broadcasted_iota(jnp.int32, (rows, cols), 0)
    lane = lax.broadcasted_iota(jnp.int32, (rows, cols), 1)
    he = he_ref[0]
    hw = hw_ref[0]
    for f in range(FB):
        q = q_ref[f]
        north = jnp.where(row == rows - 1, jnp.broadcast_to(hn_ref[f], (rows, cols)), pltpu.roll(q, rows - 1, 0))
        south = jnp.where(row == 0, jnp.broadcast_to(hs_ref[f], (rows, cols)), pltpu.roll(q, 1, 0))
        east = jnp.where(lane == cols - 1, jnp.broadcast_to(he[:, f:f + 1], (rows, cols)), pltpu.roll(q, cols - 1, 1))
        west = jnp.where(lane == 0, jnp.broadcast_to(hw[:, f:f + 1], (rows, cols)), pltpu.roll(q, 1, 1))
        u = u_ref[f]
        v = v_ref[f]
        k = k_ref[f]
        o_ref[f] = (q - 0.5 * u * (east - west) - 0.5 * v * (north - south)
                    + k * (east + west + north + south - 4.0 * q))


def sweep(q, hn, hs, he, hw, u, v, k):
    feats, rows, cols = q.shape
    levels = u.shape[0]
    nb = feats // FB
    per = levels // FB
    big = pl.BlockSpec((FB, rows, cols), lambda i: (i, 0, 0))
    field = pl.BlockSpec((FB, rows, cols), lambda i: (i % per, 0, 0))
    edge_row = pl.BlockSpec((FB, 1, cols), lambda i: (i, 0, 0))
    edge_col = pl.BlockSpec((1, rows, FB), lambda i: (i, 0, 0))
    return pl.pallas_call(
        sweep_kernel,
        grid=(nb,),
        in_specs=[big, edge_row, edge_row, edge_col, edge_col, field, field, field],
        out_specs=big,
        out_shape=jax.ShapeDtypeStruct(q.shape, q.dtype),
        cost_estimate=pl.CostEstimate(flops=20 * q.size, bytes_accessed=8 * q.size + 12 * u.size, transcendentals=0),
    )(q, hn, hs, he, hw, u, v, k)


def columns_of(edge):
    feats, rows = edge.shape
    return jnp.swapaxes(edge.reshape(feats // FB, FB, rows), 1, 2)


def step(x, u, v, k):
    feats, rows, cols = x.shape
    lat_forward, lat_backward = neighbours("lat", False)
    lon_forward, lon_backward = neighbours("lon", True)
    hn = lax.ppermute(x[:, :1, :], "lat", lat_backward)
    hs = lax.ppermute(x[:, rows - 1:, :], "lat", lat_forward)
    he = lax.ppermute(columns_of(x[:, :, 0]), "lon", lon_backward)
    hw = lax.ppermute(columns_of(x[:, :, cols - 1]), "lon", lon_forward)
    return sweep(x, hn, hs, he, hw, u, v, k)


def positions(targets_all, experts):
    count = targets_all.shape[0]
    block = 128
    onehot = (targets_all[:, None] == jnp.arange(experts, dtype=jnp.int32)[None, :]).astype(
        jnp.bfloat16
    )
    blocks = onehot.reshape(count // block, block, experts)
    rows = jnp.arange(block, dtype=jnp.int32)
    before = (rows[:, None] > rows[None, :]).astype(jnp.bfloat16)
    within = jnp.einsum("ij,bje->bie", before, blocks, preferred_element_type=jnp.float32)
    totals = jnp.sum(blocks.astype(jnp.float32), axis=1)
    offsets = jnp.cumsum(totals, axis=0) - totals
    ranks = within + offsets[:, None, :]
    position = jnp.sum(ranks * blocks.astype(jnp.float32), axis=2)
    return position.reshape(count).astype(jnp.int32)


ROWS = 256
HALF = ROWS // 2


def silu(t):
    return t * (0.5 * jnp.tanh(0.5 * t) + 0.5)


def layers(x, w_first, w_middle, w_last):
    nt = (((1,), (1,)), ((), ()))
    hidden = silu(lax.dot_general(x, w_first, nt, preferred_element_type=jnp.float32)).astype(jnp.bfloat16)
    for layer_index in range(w_middle.shape[0]):
        hidden = silu(
            lax.dot_general(hidden, w_middle[layer_index], nt, preferred_element_type=jnp.float32)
        ).astype(jnp.bfloat16)
    return lax.dot_general(hidden, w_last, nt, preferred_element_type=jnp.float32).astype(jnp.bfloat16)


def network_kernel(filled_ref, x_ref, first_ref, middle_ref, last_ref, o_ref):
    filled = filled_ref[pl.program_id(0)]

    @pl.when(filled == 2)
    def _():
        o_ref[...] = layers(x_ref[...], first_ref[0], middle_ref[0], last_ref[0])

    @pl.when(filled == 1)
    def _():
        o_ref[:HALF, :] = layers(x_ref[:HALF, :], first_ref[0], middle_ref[0], last_ref[0])
        o_ref[HALF:, :] = jnp.zeros((ROWS - HALF, o_ref.shape[1]), o_ref.dtype)

    @pl.when(filled == 0)
    def _():
        o_ref[...] = jnp.zeros(o_ref.shape, o_ref.dtype)


def network(rows_in, input_weight, middle_weight, output_weight):
    count, feats = rows_in.shape
    blocks = count // ROWS
    hid = input_weight.shape[1]
    nonzero = jnp.any(rows_in.reshape(blocks, 2, HALF * feats) != 0, axis=2)
    filled = jnp.where(nonzero[:, 1], 2, jnp.where(nonzero[:, 0], 1, 0)).astype(jnp.int32)
    mats = 2 * (hid * feats * 2 + middle_weight.shape[1] * hid * hid)
    return pl.pallas_call(
        network_kernel,
        grid_spec=pltpu.PrefetchScalarGridSpec(
            num_scalar_prefetch=1,
            grid=(blocks,),
            in_specs=[
                pl.BlockSpec((ROWS, feats), lambda i, f: (i, 0)),
                pl.BlockSpec(input_weight.shape, lambda i, f: (0, 0, 0)),
                pl.BlockSpec(middle_weight.shape, lambda i, f: (0, 0, 0, 0)),
                pl.BlockSpec(output_weight.shape, lambda i, f: (0, 0, 0)),
            ],
            out_specs=pl.BlockSpec((ROWS, feats), lambda i, f: (i, 0)),
        ),
        out_shape=jax.ShapeDtypeStruct((count, feats), jnp.bfloat16),
        cost_estimate=pl.CostEstimate(
            flops=mats * count,
            bytes_accessed=4 * count * feats + 2 * (mats // 2),
            transcendentals=(1 + middle_weight.shape[1]) * hid * count,
        ),
    )(filled, rows_in, input_weight, middle_weight, output_weight)


def local(
    column_state, wind_speed, diffusivity, batch_index, input_weight, middle_weight, output_weight
):
    num_vars, levels, lat_cells, lon_cells = column_state.shape
    features = num_vars * levels
    current = column_state.reshape(features, lat_cells, lon_cells)
    for sweep_index in range(2):
        current = step(current, wind_speed[0], wind_speed[1], diffusivity)
    column_count = lat_cells * lon_cells
    columns = current.reshape(features, column_count).astype(jnp.bfloat16)
    experts = lax.axis_size("lon")
    capacity = 2 * column_count // experts
    targets_all = batch_index.reshape(column_count)
    position = positions(targets_all, experts)
    targets = targets_all * capacity + position
    packed = jnp.zeros((features, experts * capacity), jnp.bfloat16).at[:, targets].set(columns)
    packed = packed.reshape(features, experts, capacity)
    chunks = 1
    width = capacity // chunks
    answers = []
    for chunk in range(chunks):
        part = packed[:, :, chunk * width:(chunk + 1) * width]
        received = lax.all_to_all(part, "lon", split_axis=1, concat_axis=1, tiled=True)
        rows_in = received.reshape(features, experts * width).T
        result = network(rows_in, input_weight, middle_weight, output_weight).T
        answers.append(
            lax.all_to_all(result.reshape(features, experts, width), "lon", split_axis=1, concat_axis=1, tiled=True)
        )
    returned = jnp.concatenate(answers, axis=2)
    tendency = returned.reshape(features, -1)[:, targets]
    return (current + tendency.astype(jnp.float32).reshape(current.shape)).reshape(column_state.shape)


def solution(mesh):
    in_specs = (
        P(None, None, "lat", "lon"),
        P(None, None, "lat", "lon"),
        P(None, "lat", "lon"),
        P("lat", "lon", None),
        P("lon", None, None),
        P("lon", None, None, None),
        P("lon", None, None),
    )
    out_specs = P(None, None, "lat", "lon")
    return jax.shard_map(local, mesh=mesh, in_specs=in_specs, out_specs=out_specs, check_vma=False)
```

```python
import jax
import jax.numpy as jnp
from jax import lax
from jax.experimental import pallas as pl
from jax.experimental.pallas import tpu as pltpu
from jax.sharding import PartitionSpec as P


def neighbours(axis, periodic):
    count = lax.axis_size(axis)
    forward = [(i, i + 1) for i in range(count - 1)]
    if periodic:
        forward.append((count - 1, 0))
    backward = [(target, source) for source, target in forward]
    return forward, backward


FB = 32

def sweep_kernel(q_ref, hn_ref, hs_ref, he_ref, hw_ref, u_ref, v_ref, k_ref, o_ref):
    rows, cols = q_ref.shape[1], q_ref.shape[2]
    row = lax.broadcasted_iota(jnp.int32, (rows, cols), 0)
    lane = lax.broadcasted_iota(jnp.int32, (rows, cols), 1)
    he = he_ref[0]
    hw = hw_ref[0]
    for f in range(FB):
        q = q_ref[f]
        north = jnp.where(row == rows - 1, jnp.broadcast_to(hn_ref[f], (rows, cols)), pltpu.roll(q, rows - 1, 0))
        south = jnp.where(row == 0, jnp.broadcast_to(hs_ref[f], (rows, cols)), pltpu.roll(q, 1, 0))
        east = jnp.where(lane == cols - 1, jnp.broadcast_to(he[:, f:f + 1], (rows, cols)), pltpu.roll(q, cols - 1, 1))
        west = jnp.where(lane == 0, jnp.broadcast_to(hw[:, f:f + 1], (rows, cols)), pltpu.roll(q, 1, 1))
        u = u_ref[f]
        v = v_ref[f]
        k = k_ref[f]
        o_ref[f] = (q - 0.5 * u * (east - west) - 0.5 * v * (north - south)
                    + k * (east + west + north + south - 4.0 * q))


def sweep(q, hn, hs, he, hw, u, v, k):
    feats, rows, cols = q.shape
    levels = u.shape[0]
    nb = feats // FB
    per = levels // FB
    big = pl.BlockSpec((FB, rows, cols), lambda i: (i, 0, 0))
    field = pl.BlockSpec((FB, rows, cols), lambda i: (i % per, 0, 0))
    edge_row = pl.BlockSpec((FB, 1, cols), lambda i: (i, 0, 0))
    edge_col = pl.BlockSpec((1, rows, FB), lambda i: (i, 0, 0))
    return pl.pallas_call(
        sweep_kernel,
        grid=(nb,),
        in_specs=[big, edge_row, edge_row, edge_col, edge_col, field, field, field],
        out_specs=big,
        out_shape=jax.ShapeDtypeStruct(q.shape, q.dtype),
        cost_estimate=pl.CostEstimate(flops=20 * q.size, bytes_accessed=8 * q.size + 12 * u.size, transcendentals=0),
    )(q, hn, hs, he, hw, u, v, k)


def columns_of(edge):
    feats, rows = edge.shape
    return jnp.swapaxes(edge.reshape(feats // FB, FB, rows), 1, 2)


def step(x, u, v, k):
    feats, rows, cols = x.shape
    lat_forward, lat_backward = neighbours("lat", False)
    lon_forward, lon_backward = neighbours("lon", True)
    hn = lax.ppermute(x[:, :1, :], "lat", lat_backward)
    hs = lax.ppermute(x[:, rows - 1:, :], "lat", lat_forward)
    he = lax.ppermute(columns_of(x[:, :, 0]), "lon", lon_backward)
    hw = lax.ppermute(columns_of(x[:, :, cols - 1]), "lon", lon_forward)
    return sweep(x, hn, hs, he, hw, u, v, k)


def positions(targets_all, experts):
    count = targets_all.shape[0]
    block = 128
    onehot = (targets_all[:, None] == jnp.arange(experts, dtype=jnp.int32)[None, :]).astype(
        jnp.bfloat16
    )
    blocks = onehot.reshape(count // block, block, experts)
    rows = jnp.arange(block, dtype=jnp.int32)
    before = (rows[:, None] > rows[None, :]).astype(jnp.bfloat16)
    within = jnp.einsum("ij,bje->bie", before, blocks, preferred_element_type=jnp.float32)
    totals = jnp.sum(blocks.astype(jnp.float32), axis=1)
    offsets = jnp.cumsum(totals, axis=0) - totals
    ranks = within + offsets[:, None, :]
    position = jnp.sum(ranks * blocks.astype(jnp.float32), axis=2)
    return position.reshape(count).astype(jnp.int32)


ROWS = 256
HALF = ROWS // 2


def silu(t):
    return t * (0.5 * jnp.tanh(0.5 * t) + 0.5)


def layers(x, w_first, w_middle, w_last):
    hidden = silu(jnp.dot(x, w_first, preferred_element_type=jnp.float32)).astype(jnp.bfloat16)
    for layer_index in range(w_middle.shape[0]):
        hidden = silu(
            jnp.dot(hidden, w_middle[layer_index], preferred_element_type=jnp.float32)
        ).astype(jnp.bfloat16)
    return jnp.dot(hidden, w_last, preferred_element_type=jnp.float32).astype(jnp.bfloat16)


def network_kernel(filled_ref, x_ref, first_ref, middle_ref, last_ref, o_ref):
    filled = filled_ref[pl.program_id(0)]

    @pl.when(filled == 2)
    def _():
        o_ref[...] = layers(x_ref[...], first_ref[...], middle_ref[...], last_ref[...])

    @pl.when(filled == 1)
    def _():
        o_ref[:HALF, :] = layers(x_ref[:HALF, :], first_ref[...], middle_ref[...], last_ref[...])
        o_ref[HALF:, :] = jnp.zeros((ROWS - HALF, o_ref.shape[1]), o_ref.dtype)

    @pl.when(filled == 0)
    def _():
        o_ref[...] = jnp.zeros(o_ref.shape, o_ref.dtype)


def network(rows_in, input_weight, middle_weight, output_weight):
    count, feats = rows_in.shape
    blocks = count // ROWS
    hid = input_weight.shape[1]
    first = input_weight[0].T
    middle = jnp.swapaxes(middle_weight[0], 1, 2)
    last = output_weight[0].T
    nonzero = jnp.any(rows_in.reshape(blocks, 2, HALF * feats) != 0, axis=2)
    filled = jnp.where(nonzero[:, 1], 2, jnp.where(nonzero[:, 0], 1, 0)).astype(jnp.int32)
    mats = 2 * (hid * feats * 2 + middle_weight.shape[1] * hid * hid)
    return pl.pallas_call(
        network_kernel,
        grid_spec=pltpu.PrefetchScalarGridSpec(
            num_scalar_prefetch=1,
            grid=(blocks,),
            in_specs=[
                pl.BlockSpec((ROWS, feats), lambda i, f: (i, 0)),
                pl.BlockSpec(first.shape, lambda i, f: (0, 0)),
                pl.BlockSpec(middle.shape, lambda i, f: (0, 0, 0)),
                pl.BlockSpec(last.shape, lambda i, f: (0, 0)),
            ],
            out_specs=pl.BlockSpec((ROWS, feats), lambda i, f: (i, 0)),
        ),
        out_shape=jax.ShapeDtypeStruct((count, feats), jnp.bfloat16),
        cost_estimate=pl.CostEstimate(
            flops=mats * count,
            bytes_accessed=4 * count * feats + 2 * (mats // 2),
            transcendentals=(1 + middle_weight.shape[1]) * hid * count,
        ),
    )(filled, rows_in, first, middle, last)


def local(
    column_state, wind_speed, diffusivity, batch_index, input_weight, middle_weight, output_weight
):
    num_vars, levels, lat_cells, lon_cells = column_state.shape
    features = num_vars * levels
    current = column_state.reshape(features, lat_cells, lon_cells)
    for sweep_index in range(2):
        current = step(current, wind_speed[0], wind_speed[1], diffusivity)
    column_count = lat_cells * lon_cells
    columns = current.reshape(features, column_count).astype(jnp.bfloat16)
    experts = lax.axis_size("lon")
    capacity = 2 * column_count // experts
    targets_all = batch_index.reshape(column_count)
    position = positions(targets_all, experts)
    targets = targets_all * capacity + position
    packed = jnp.zeros((features, experts * capacity), jnp.bfloat16).at[:, targets].set(columns)
    packed = packed.reshape(features, experts, capacity)
    chunks = 1
    width = capacity // chunks
    answers = []
    for chunk in range(chunks):
        part = packed[:, :, chunk * width:(chunk + 1) * width]
        received = lax.all_to_all(part, "lon", split_axis=1, concat_axis=1, tiled=True)
        rows_in = received.reshape(features, experts * width).T
        result = network(rows_in, input_weight, middle_weight, output_weight).T
        answers.append(
            lax.all_to_all(result.reshape(features, experts, width), "lon", split_axis=1, concat_axis=1, tiled=True)
        )
    returned = jnp.concatenate(answers, axis=2)
    tendency = returned.reshape(features, -1)[:, targets]
    return (current + tendency.astype(jnp.float32).reshape(current.shape)).reshape(column_state.shape)


def solution(mesh):
    in_specs = (
        P(None, None, "lat", "lon"),
        P(None, None, "lat", "lon"),
        P(None, "lat", "lon"),
        P("lat", "lon", None),
        P("lon", None, None),
        P("lon", None, None, None),
        P("lon", None, None),
    )
    out_specs = P(None, None, "lat", "lon")
    return jax.shard_map(local, mesh=mesh, in_specs=in_specs, out_specs=out_specs, check_vma=False)
```

```python
import jax
import jax.numpy as jnp
from jax import lax
from jax.experimental import pallas as pl
from jax.experimental.pallas import tpu as pltpu
from jax.sharding import PartitionSpec as P


def neighbours(axis, periodic):
    count = lax.axis_size(axis)
    forward = [(i, i + 1) for i in range(count - 1)]
    if periodic:
        forward.append((count - 1, 0))
    backward = [(target, source) for source, target in forward]
    return forward, backward


FB = 32

def sweep_kernel(q_ref, hn_ref, hs_ref, he_ref, hw_ref, u_ref, v_ref, k_ref, o_ref):
    rows, cols = q_ref.shape[1], q_ref.shape[2]
    row = lax.broadcasted_iota(jnp.int32, (rows, cols), 0)
    lane = lax.broadcasted_iota(jnp.int32, (rows, cols), 1)
    he = he_ref[0]
    hw = hw_ref[0]
    for f in range(FB):
        q = q_ref[f]
        north = jnp.where(row == rows - 1, jnp.broadcast_to(hn_ref[f], (rows, cols)), pltpu.roll(q, rows - 1, 0))
        south = jnp.where(row == 0, jnp.broadcast_to(hs_ref[f], (rows, cols)), pltpu.roll(q, 1, 0))
        east = jnp.where(lane == cols - 1, jnp.broadcast_to(he[:, f:f + 1], (rows, cols)), pltpu.roll(q, cols - 1, 1))
        west = jnp.where(lane == 0, jnp.broadcast_to(hw[:, f:f + 1], (rows, cols)), pltpu.roll(q, 1, 1))
        u = u_ref[f]
        v = v_ref[f]
        k = k_ref[f]
        o_ref[f] = (q - 0.5 * u * (east - west) - 0.5 * v * (north - south)
                    + k * (east + west + north + south - 4.0 * q))


def sweep(q, hn, hs, he, hw, u, v, k):
    feats, rows, cols = q.shape
    levels = u.shape[0]
    nb = feats // FB
    per = levels // FB
    big = pl.BlockSpec((FB, rows, cols), lambda i: (i, 0, 0))
    field = pl.BlockSpec((FB, rows, cols), lambda i: (i % per, 0, 0))
    edge_row = pl.BlockSpec((FB, 1, cols), lambda i: (i, 0, 0))
    edge_col = pl.BlockSpec((1, rows, FB), lambda i: (i, 0, 0))
    return pl.pallas_call(
        sweep_kernel,
        grid=(nb,),
        in_specs=[big, edge_row, edge_row, edge_col, edge_col, field, field, field],
        out_specs=big,
        out_shape=jax.ShapeDtypeStruct(q.shape, q.dtype),
        cost_estimate=pl.CostEstimate(flops=20 * q.size, bytes_accessed=8 * q.size + 12 * u.size, transcendentals=0),
    )(q, hn, hs, he, hw, u, v, k)


def columns_of(edge):
    feats, rows = edge.shape
    return jnp.swapaxes(edge.reshape(feats // FB, FB, rows), 1, 2)


def step(x, u, v, k):
    feats, rows, cols = x.shape
    lat_forward, lat_backward = neighbours("lat", False)
    lon_forward, lon_backward = neighbours("lon", True)
    hn = lax.ppermute(x[:, :1, :], "lat", lat_backward)
    hs = lax.ppermute(x[:, rows - 1:, :], "lat", lat_forward)
    he = lax.ppermute(columns_of(x[:, :, 0]), "lon", lon_backward)
    hw = lax.ppermute(columns_of(x[:, :, cols - 1]), "lon", lon_forward)
    return sweep(x, hn, hs, he, hw, u, v, k)


def positions(targets_all, experts):
    count = targets_all.shape[0]
    block = 128
    onehot = (targets_all[:, None] == jnp.arange(experts, dtype=jnp.int32)[None, :]).astype(
        jnp.bfloat16
    )
    blocks = onehot.reshape(count // block, block, experts)
    rows = jnp.arange(block, dtype=jnp.int32)
    before = (rows[:, None] > rows[None, :]).astype(jnp.bfloat16)
    within = jnp.einsum("ij,bje->bie", before, blocks, preferred_element_type=jnp.float32)
    totals = jnp.sum(blocks.astype(jnp.float32), axis=1)
    offsets = jnp.cumsum(totals, axis=0) - totals
    ranks = within + offsets[:, None, :]
    position = jnp.sum(ranks * blocks.astype(jnp.float32), axis=2)
    return position.reshape(count).astype(jnp.int32)


ROWS = 1024
HALF = 128


def silu(t):
    return t * (0.5 * jnp.tanh(0.5 * t) + 0.5)


def layers(x, w_first, w_middle, w_last):
    hidden = silu(jnp.dot(x, w_first, preferred_element_type=jnp.float32)).astype(jnp.bfloat16)
    for layer_index in range(w_middle.shape[0]):
        hidden = silu(
            jnp.dot(hidden, w_middle[layer_index], preferred_element_type=jnp.float32)
        ).astype(jnp.bfloat16)
    return jnp.dot(hidden, w_last, preferred_element_type=jnp.float32).astype(jnp.bfloat16)


def network_kernel(active_ref, x_ref, first_ref, middle_ref, last_ref, o_ref):
    @pl.when(pl.program_id(0) < active_ref[0])
    def _():
        o_ref[...] = layers(x_ref[...], first_ref[...], middle_ref[...], last_ref[...])

    @pl.when(pl.program_id(0) >= active_ref[0])
    def _():
        o_ref[...] = jnp.zeros(o_ref.shape, o_ref.dtype)


def network(rows_in, input_weight, middle_weight, output_weight):
    count, feats = rows_in.shape
    groups = count // HALF
    hid = input_weight.shape[1]
    first = input_weight[0].T
    middle = jnp.swapaxes(middle_weight[0], 1, 2)
    last = output_weight[0].T
    grouped = rows_in.reshape(groups, HALF * feats)
    nonzero = jnp.any(grouped != 0, axis=1).astype(jnp.int32)
    used = jnp.sum(nonzero)
    ahead = jnp.cumsum(nonzero) - nonzero
    place = jnp.where(nonzero > 0, ahead, used + jnp.arange(groups, dtype=jnp.int32) - ahead)
    source = jnp.zeros((groups,), jnp.int32).at[place].set(jnp.arange(groups, dtype=jnp.int32))
    packed_rows = grouped[source].reshape(count, feats)
    active = ((used * HALF + ROWS - 1) // ROWS).reshape(1)
    mats = 2 * (hid * feats * 2 + middle_weight.shape[1] * hid * hid)
    out = pl.pallas_call(
        network_kernel,
        grid_spec=pltpu.PrefetchScalarGridSpec(
            num_scalar_prefetch=1,
            grid=(count // ROWS,),
            in_specs=[
                pl.BlockSpec((ROWS, feats), lambda i, a: (i, 0)),
                pl.BlockSpec(first.shape, lambda i, a: (0, 0)),
                pl.BlockSpec(middle.shape, lambda i, a: (0, 0, 0)),
                pl.BlockSpec(last.shape, lambda i, a: (0, 0)),
            ],
            out_specs=pl.BlockSpec((ROWS, feats), lambda i, a: (i, 0)),
        ),
        out_shape=jax.ShapeDtypeStruct((count, feats), jnp.bfloat16),
        cost_estimate=pl.CostEstimate(
            flops=mats * count,
            bytes_accessed=4 * count * feats + 2 * (mats // 2),
            transcendentals=(1 + middle_weight.shape[1]) * hid * count,
        ),
    )(active, packed_rows, first, middle, last)
    return out.reshape(groups, HALF * feats)[place].reshape(count, feats)


def local(
    column_state, wind_speed, diffusivity, batch_index, input_weight, middle_weight, output_weight
):
    num_vars, levels, lat_cells, lon_cells = column_state.shape
    features = num_vars * levels
    current = column_state.reshape(features, lat_cells, lon_cells)
    for sweep_index in range(2):
        current = step(current, wind_speed[0], wind_speed[1], diffusivity)
    column_count = lat_cells * lon_cells
    columns = current.reshape(features, column_count).astype(jnp.bfloat16)
    experts = lax.axis_size("lon")
    capacity = 2 * column_count // experts
    targets_all = batch_index.reshape(column_count)
    position = positions(targets_all, experts)
    targets = targets_all * capacity + position
    packed = jnp.zeros((features, experts * capacity), jnp.bfloat16).at[:, targets].set(columns)
    packed = packed.reshape(features, experts, capacity)
    chunks = 1
    width = capacity // chunks
    answers = []
    for chunk in range(chunks):
        part = packed[:, :, chunk * width:(chunk + 1) * width]
        received = lax.all_to_all(part, "lon", split_axis=1, concat_axis=1, tiled=True)
        rows_in = received.reshape(features, experts * width).T
        result = network(rows_in, input_weight, middle_weight, output_weight).T
        answers.append(
            lax.all_to_all(result.reshape(features, experts, width), "lon", split_axis=1, concat_axis=1, tiled=True)
        )
    returned = jnp.concatenate(answers, axis=2)
    tendency = returned.reshape(features, -1)[:, targets]
    return (current + tendency.astype(jnp.float32).reshape(current.shape)).reshape(column_state.shape)


def solution(mesh):
    in_specs = (
        P(None, None, "lat", "lon"),
        P(None, None, "lat", "lon"),
        P(None, "lat", "lon"),
        P("lat", "lon", None),
        P("lon", None, None),
        P("lon", None, None, None),
        P("lon", None, None),
    )
    out_specs = P(None, None, "lat", "lon")
    return jax.shard_map(local, mesh=mesh, in_specs=in_specs, out_specs=out_specs, check_vma=False)
```

```python
import jax
import jax.numpy as jnp
from jax import lax
from jax.experimental import pallas as pl
from jax.experimental.pallas import tpu as pltpu
from jax.sharding import PartitionSpec as P


def neighbours(axis, periodic):
    count = lax.axis_size(axis)
    forward = [(i, i + 1) for i in range(count - 1)]
    if periodic:
        forward.append((count - 1, 0))
    backward = [(target, source) for source, target in forward]
    return forward, backward


FB = 32

def sweep_kernel(q_ref, hn_ref, hs_ref, he_ref, hw_ref, u_ref, v_ref, k_ref, o_ref):
    rows, cols = q_ref.shape[1], q_ref.shape[2]
    row = lax.broadcasted_iota(jnp.int32, (rows, cols), 0)
    lane = lax.broadcasted_iota(jnp.int32, (rows, cols), 1)
    he = he_ref[0]
    hw = hw_ref[0]
    for f in range(FB):
        q = q_ref[f]
        north = jnp.where(row == rows - 1, jnp.broadcast_to(hn_ref[f], (rows, cols)), pltpu.roll(q, rows - 1, 0))
        south = jnp.where(row == 0, jnp.broadcast_to(hs_ref[f], (rows, cols)), pltpu.roll(q, 1, 0))
        east = jnp.where(lane == cols - 1, jnp.broadcast_to(he[:, f:f + 1], (rows, cols)), pltpu.roll(q, cols - 1, 1))
        west = jnp.where(lane == 0, jnp.broadcast_to(hw[:, f:f + 1], (rows, cols)), pltpu.roll(q, 1, 1))
        u = u_ref[f]
        v = v_ref[f]
        k = k_ref[f]
        o_ref[f] = (q - 0.5 * u * (east - west) - 0.5 * v * (north - south)
                    + k * (east + west + north + south - 4.0 * q))


def sweep(q, hn, hs, he, hw, u, v, k):
    feats, rows, cols = q.shape
    levels = u.shape[0]
    nb = feats // FB
    per = levels // FB
    big = pl.BlockSpec((FB, rows, cols), lambda i: (i, 0, 0))
    field = pl.BlockSpec((FB, rows, cols), lambda i: (i % per, 0, 0))
    edge_row = pl.BlockSpec((FB, 1, cols), lambda i: (i, 0, 0))
    edge_col = pl.BlockSpec((1, rows, FB), lambda i: (i, 0, 0))
    return pl.pallas_call(
        sweep_kernel,
        grid=(nb,),
        in_specs=[big, edge_row, edge_row, edge_col, edge_col, field, field, field],
        out_specs=big,
        out_shape=jax.ShapeDtypeStruct(q.shape, q.dtype),
        cost_estimate=pl.CostEstimate(flops=20 * q.size, bytes_accessed=8 * q.size + 12 * u.size, transcendentals=0),
    )(q, hn, hs, he, hw, u, v, k)


def columns_of(edge):
    feats, rows = edge.shape
    return jnp.swapaxes(edge.reshape(feats // FB, FB, rows), 1, 2)


def step(x, u, v, k):
    feats, rows, cols = x.shape
    lat_forward, lat_backward = neighbours("lat", False)
    lon_forward, lon_backward = neighbours("lon", True)
    hn = lax.ppermute(x[:, :1, :], "lat", lat_backward)
    hs = lax.ppermute(x[:, rows - 1:, :], "lat", lat_forward)
    he = lax.ppermute(columns_of(x[:, :, 0]), "lon", lon_backward)
    hw = lax.ppermute(columns_of(x[:, :, cols - 1]), "lon", lon_forward)
    return sweep(x, hn, hs, he, hw, u, v, k)


def positions(targets_all, experts):
    count = targets_all.shape[0]
    block = 128
    onehot = (targets_all[:, None] == jnp.arange(experts, dtype=jnp.int32)[None, :]).astype(
        jnp.bfloat16
    )
    blocks = onehot.reshape(count // block, block, experts)
    rows = jnp.arange(block, dtype=jnp.int32)
    before = (rows[:, None] > rows[None, :]).astype(jnp.bfloat16)
    within = jnp.einsum("ij,bje->bie", before, blocks, preferred_element_type=jnp.float32)
    totals = jnp.sum(blocks.astype(jnp.float32), axis=1)
    offsets = jnp.cumsum(totals, axis=0) - totals
    ranks = within + offsets[:, None, :]
    position = jnp.sum(ranks * blocks.astype(jnp.float32), axis=2)
    return position.reshape(count).astype(jnp.int32)


ROWS = 1024
HALF = 128


def silu(t):
    return t * (0.5 * jnp.tanh(0.5 * t) + 0.5)


def layers(x, w_first, w_middle, w_last):
    hidden = silu(jnp.dot(x, w_first, preferred_element_type=jnp.float32)).astype(jnp.bfloat16)
    for layer_index in range(w_middle.shape[0]):
        hidden = silu(
            jnp.dot(hidden, w_middle[layer_index], preferred_element_type=jnp.float32)
        ).astype(jnp.bfloat16)
    return jnp.dot(hidden, w_last, preferred_element_type=jnp.float32).astype(jnp.bfloat16)


def network_kernel(active_ref, source_ref, x_hbm, first_ref, middle_ref, last_ref, o_hbm, buf, res, sems):
    block = pl.program_id(0)
    per = ROWS // HALF

    @pl.when(block < active_ref[0])
    def _():
        loads = []
        for j in range(per):
            group = source_ref[block * per + j]
            copy = pltpu.make_async_copy(
                x_hbm.at[pl.ds(group * HALF, HALF)], buf.at[pl.ds(j * HALF, HALF)], sems.at[j]
            )
            copy.start()
            loads.append(copy)
        for copy in loads:
            copy.wait()
        res[...] = layers(buf[...], first_ref[...], middle_ref[...], last_ref[...])

    @pl.when(block >= active_ref[0])
    def _():
        res[...] = jnp.zeros(res.shape, res.dtype)

    stores = []
    for j in range(per):
        group = source_ref[block * per + j]
        copy = pltpu.make_async_copy(
            res.at[pl.ds(j * HALF, HALF)], o_hbm.at[pl.ds(group * HALF, HALF)], sems.at[per + j]
        )
        copy.start()
        stores.append(copy)
    for copy in stores:
        copy.wait()


def network(rows_in, input_weight, middle_weight, output_weight):
    count, feats = rows_in.shape
    groups = count // HALF
    hid = input_weight.shape[1]
    first = input_weight[0].T
    middle = jnp.swapaxes(middle_weight[0], 1, 2)
    last = output_weight[0].T
    grouped = rows_in.reshape(groups, HALF, feats)
    nonzero = jnp.any(grouped != 0, axis=(1, 2)).astype(jnp.int32)
    used = jnp.sum(nonzero)
    ahead = jnp.cumsum(nonzero) - nonzero
    place = jnp.where(nonzero > 0, ahead, used + jnp.arange(groups, dtype=jnp.int32) - ahead)
    source = jnp.zeros((groups,), jnp.int32).at[place].set(jnp.arange(groups, dtype=jnp.int32))
    active = ((used * HALF + ROWS - 1) // ROWS).reshape(1)
    mats = 2 * (hid * feats * 2 + middle_weight.shape[1] * hid * hid)
    per = ROWS // HALF
    return pl.pallas_call(
        network_kernel,
        grid_spec=pltpu.PrefetchScalarGridSpec(
            num_scalar_prefetch=2,
            grid=(count // ROWS,),
            in_specs=[
                pl.BlockSpec(memory_space=pl.ANY),
                pl.BlockSpec(first.shape, lambda i, a, s: (0, 0)),
                pl.BlockSpec(middle.shape, lambda i, a, s: (0, 0, 0)),
                pl.BlockSpec(last.shape, lambda i, a, s: (0, 0)),
            ],
            out_specs=pl.BlockSpec(memory_space=pl.ANY),
            scratch_shapes=[
                pltpu.VMEM((ROWS, feats), jnp.bfloat16),
                pltpu.VMEM((ROWS, feats), jnp.bfloat16),
                pltpu.SemaphoreType.DMA((2 * per,)),
            ],
        ),
        out_shape=jax.ShapeDtypeStruct((count, feats), jnp.bfloat16),
        cost_estimate=pl.CostEstimate(
            flops=mats * count,
            bytes_accessed=4 * count * feats + 2 * (mats // 2),
            transcendentals=(1 + middle_weight.shape[1]) * hid * count,
        ),
    )(active, source, rows_in, first, middle, last)


def local(
    column_state, wind_speed, diffusivity, batch_index, input_weight, middle_weight, output_weight
):
    num_vars, levels, lat_cells, lon_cells = column_state.shape
    features = num_vars * levels
    current = column_state.reshape(features, lat_cells, lon_cells)
    for sweep_index in range(2):
        current = step(current, wind_speed[0], wind_speed[1], diffusivity)
    column_count = lat_cells * lon_cells
    columns = current.reshape(features, column_count).astype(jnp.bfloat16)
    experts = lax.axis_size("lon")
    capacity = 2 * column_count // experts
    targets_all = batch_index.reshape(column_count)
    position = positions(targets_all, experts)
    targets = targets_all * capacity + position
    packed = jnp.zeros((features, experts * capacity), jnp.bfloat16).at[:, targets].set(columns)
    packed = packed.reshape(features, experts, capacity)
    chunks = 1
    width = capacity // chunks
    answers = []
    for chunk in range(chunks):
        part = packed[:, :, chunk * width:(chunk + 1) * width]
        received = lax.all_to_all(part, "lon", split_axis=1, concat_axis=1, tiled=True)
        rows_in = received.reshape(features, experts * width).T
        result = network(rows_in, input_weight, middle_weight, output_weight).T
        answers.append(
            lax.all_to_all(result.reshape(features, experts, width), "lon", split_axis=1, concat_axis=1, tiled=True)
        )
    returned = jnp.concatenate(answers, axis=2)
    tendency = returned.reshape(features, -1)[:, targets]
    return (current + tendency.astype(jnp.float32).reshape(current.shape)).reshape(column_state.shape)


def solution(mesh):
    in_specs = (
        P(None, None, "lat", "lon"),
        P(None, None, "lat", "lon"),
        P(None, "lat", "lon"),
        P("lat", "lon", None),
        P("lon", None, None),
        P("lon", None, None, None),
        P("lon", None, None),
    )
    out_specs = P(None, None, "lat", "lon")
    return jax.shard_map(local, mesh=mesh, in_specs=in_specs, out_specs=out_specs, check_vma=False)
```

```python
import jax
import jax.numpy as jnp
from jax import lax
from jax.experimental import pallas as pl
from jax.experimental.pallas import tpu as pltpu
from jax.sharding import PartitionSpec as P


def neighbours(axis, periodic):
    count = lax.axis_size(axis)
    forward = [(i, i + 1) for i in range(count - 1)]
    if periodic:
        forward.append((count - 1, 0))
    backward = [(target, source) for source, target in forward]
    return forward, backward


FB = 32

def sweep_kernel(q_ref, hn_ref, hs_ref, he_ref, hw_ref, u_ref, v_ref, k_ref, o_ref):
    rows, cols = q_ref.shape[1], q_ref.shape[2]
    row = lax.broadcasted_iota(jnp.int32, (rows, cols), 0)
    lane = lax.broadcasted_iota(jnp.int32, (rows, cols), 1)
    he = he_ref[0]
    hw = hw_ref[0]
    for f in range(FB):
        q = q_ref[f]
        north = jnp.where(row == rows - 1, jnp.broadcast_to(hn_ref[f], (rows, cols)), pltpu.roll(q, rows - 1, 0))
        south = jnp.where(row == 0, jnp.broadcast_to(hs_ref[f], (rows, cols)), pltpu.roll(q, 1, 0))
        east = jnp.where(lane == cols - 1, jnp.broadcast_to(he[:, f:f + 1], (rows, cols)), pltpu.roll(q, cols - 1, 1))
        west = jnp.where(lane == 0, jnp.broadcast_to(hw[:, f:f + 1], (rows, cols)), pltpu.roll(q, 1, 1))
        u = u_ref[f]
        v = v_ref[f]
        k = k_ref[f]
        o_ref[f] = (q - 0.5 * u * (east - west) - 0.5 * v * (north - south)
                    + k * (east + west + north + south - 4.0 * q))


def sweep(q, hn, hs, he, hw, u, v, k):
    feats, rows, cols = q.shape
    levels = u.shape[0]
    nb = feats // FB
    per = levels // FB
    big = pl.BlockSpec((FB, rows, cols), lambda i: (i, 0, 0))
    field = pl.BlockSpec((FB, rows, cols), lambda i: (i % per, 0, 0))
    edge_row = pl.BlockSpec((FB, 1, cols), lambda i: (i, 0, 0))
    edge_col = pl.BlockSpec((1, rows, FB), lambda i: (i, 0, 0))
    return pl.pallas_call(
        sweep_kernel,
        grid=(nb,),
        in_specs=[big, edge_row, edge_row, edge_col, edge_col, field, field, field],
        out_specs=big,
        out_shape=jax.ShapeDtypeStruct(q.shape, q.dtype),
        cost_estimate=pl.CostEstimate(flops=20 * q.size, bytes_accessed=8 * q.size + 12 * u.size, transcendentals=0),
    )(q, hn, hs, he, hw, u, v, k)


def columns_of(edge):
    feats, rows = edge.shape
    return jnp.swapaxes(edge.reshape(feats // FB, FB, rows), 1, 2)


def step(x, u, v, k):
    feats, rows, cols = x.shape
    lat_forward, lat_backward = neighbours("lat", False)
    lon_forward, lon_backward = neighbours("lon", True)
    hn = lax.ppermute(x[:, :1, :], "lat", lat_backward)
    hs = lax.ppermute(x[:, rows - 1:, :], "lat", lat_forward)
    he = lax.ppermute(columns_of(x[:, :, 0]), "lon", lon_backward)
    hw = lax.ppermute(columns_of(x[:, :, cols - 1]), "lon", lon_forward)
    return sweep(x, hn, hs, he, hw, u, v, k)


def positions(targets_all, experts):
    count = targets_all.shape[0]
    block = 128
    onehot = (targets_all[:, None] == jnp.arange(experts, dtype=jnp.int32)[None, :]).astype(
        jnp.bfloat16
    )
    blocks = onehot.reshape(count // block, block, experts)
    rows = jnp.arange(block, dtype=jnp.int32)
    before = (rows[:, None] > rows[None, :]).astype(jnp.bfloat16)
    within = jnp.einsum("ij,bje->bie", before, blocks, preferred_element_type=jnp.float32)
    totals = jnp.sum(blocks.astype(jnp.float32), axis=1)
    offsets = jnp.cumsum(totals, axis=0) - totals
    ranks = within + offsets[:, None, :]
    position = jnp.sum(ranks * blocks.astype(jnp.float32), axis=2)
    return position.reshape(count).astype(jnp.int32)


ROWS = 1024
HALF = 128


def silu(t):
    return t * (0.5 * jnp.tanh(0.5 * t) + 0.5)


def layers(x, w_first, w_middle, w_last):
    hidden = silu(jnp.dot(x, w_first, preferred_element_type=jnp.float32)).astype(jnp.bfloat16)
    for layer_index in range(w_middle.shape[0]):
        hidden = silu(
            jnp.dot(hidden, w_middle[layer_index], preferred_element_type=jnp.float32)
        ).astype(jnp.bfloat16)
    return jnp.dot(hidden, w_last, preferred_element_type=jnp.float32).astype(jnp.bfloat16)


def network_kernel(active_ref, source_ref, x_hbm, first_ref, middle_ref, last_ref, o_hbm, buf, res, lsem, ssem):
    block = pl.program_id(0)
    blocks = pl.num_programs(0)
    active = active_ref[0]
    slot = block % 2
    per = ROWS // HALF

    def loads(index, into):
        return [
            pltpu.make_async_copy(
                x_hbm.at[pl.ds(source_ref[index * per + j] * HALF, HALF)],
                buf.at[into, pl.ds(j * HALF, HALF)],
                lsem.at[into, j],
            )
            for j in range(per)
        ]

    def stores(index, outof):
        return [
            pltpu.make_async_copy(
                res.at[outof, pl.ds(j * HALF, HALF)],
                o_hbm.at[pl.ds(source_ref[index * per + j] * HALF, HALF)],
                ssem.at[outof, j],
            )
            for j in range(per)
        ]

    @pl.when((block == 0) & (active > 0))
    def _():
        for copy in loads(0, 0):
            copy.start()

    @pl.when(block + 1 < active)
    def _():
        for copy in loads(block + 1, 1 - slot):
            copy.start()

    @pl.when(block >= 2)
    def _():
        for copy in stores(block - 2, slot):
            copy.wait()

    @pl.when(block < active)
    def _():
        for copy in loads(block, slot):
            copy.wait()
        res[slot] = layers(buf[slot], first_ref[...], middle_ref[...], last_ref[...])

    @pl.when(block >= active)
    def _():
        res[slot] = jnp.zeros(res.shape[1:], res.dtype)

    for copy in stores(block, slot):
        copy.start()

    @pl.when(block == blocks - 1)
    def _():
        for copy in stores(block - 1, 1 - slot):
            copy.wait()
        for copy in stores(block, slot):
            copy.wait()


def network(rows_in, input_weight, middle_weight, output_weight):
    count, feats = rows_in.shape
    groups = count // HALF
    hid = input_weight.shape[1]
    first = input_weight[0].T
    middle = jnp.swapaxes(middle_weight[0], 1, 2)
    last = output_weight[0].T
    grouped = rows_in.reshape(groups, HALF, feats)
    nonzero = jnp.any(grouped != 0, axis=(1, 2)).astype(jnp.int32)
    used = jnp.sum(nonzero)
    ahead = jnp.cumsum(nonzero) - nonzero
    place = jnp.where(nonzero > 0, ahead, used + jnp.arange(groups, dtype=jnp.int32) - ahead)
    source = jnp.zeros((groups,), jnp.int32).at[place].set(jnp.arange(groups, dtype=jnp.int32))
    active = ((used * HALF + ROWS - 1) // ROWS).reshape(1)
    mats = 2 * (hid * feats * 2 + middle_weight.shape[1] * hid * hid)
    per = ROWS // HALF
    return pl.pallas_call(
        network_kernel,
        grid_spec=pltpu.PrefetchScalarGridSpec(
            num_scalar_prefetch=2,
            grid=(count // ROWS,),
            in_specs=[
                pl.BlockSpec(memory_space=pl.ANY),
                pl.BlockSpec(first.shape, lambda i, a, s: (0, 0)),
                pl.BlockSpec(middle.shape, lambda i, a, s: (0, 0, 0)),
                pl.BlockSpec(last.shape, lambda i, a, s: (0, 0)),
            ],
            out_specs=pl.BlockSpec(memory_space=pl.ANY),
            scratch_shapes=[
                pltpu.VMEM((2, ROWS, feats), jnp.bfloat16),
                pltpu.VMEM((2, ROWS, feats), jnp.bfloat16),
                pltpu.SemaphoreType.DMA((2, per)),
                pltpu.SemaphoreType.DMA((2, per)),
            ],
        ),
        out_shape=jax.ShapeDtypeStruct((count, feats), jnp.bfloat16),
        cost_estimate=pl.CostEstimate(
            flops=mats * count,
            bytes_accessed=4 * count * feats + 2 * (mats // 2),
            transcendentals=(1 + middle_weight.shape[1]) * hid * count,
        ),
    )(active, source, rows_in, first, middle, last)


def local(
    column_state, wind_speed, diffusivity, batch_index, input_weight, middle_weight, output_weight
):
    num_vars, levels, lat_cells, lon_cells = column_state.shape
    features = num_vars * levels
    current = column_state.reshape(features, lat_cells, lon_cells)
    for sweep_index in range(2):
        current = step(current, wind_speed[0], wind_speed[1], diffusivity)
    column_count = lat_cells * lon_cells
    columns = current.reshape(features, column_count).astype(jnp.bfloat16)
    experts = lax.axis_size("lon")
    capacity = 2 * column_count // experts
    targets_all = batch_index.reshape(column_count)
    position = positions(targets_all, experts)
    targets = targets_all * capacity + position
    packed = jnp.zeros((features, experts * capacity), jnp.bfloat16).at[:, targets].set(columns)
    packed = packed.reshape(features, experts, capacity)
    chunks = 1
    width = capacity // chunks
    answers = []
    for chunk in range(chunks):
        part = packed[:, :, chunk * width:(chunk + 1) * width]
        received = lax.all_to_all(part, "lon", split_axis=1, concat_axis=1, tiled=True)
        rows_in = received.reshape(features, experts * width).T
        result = network(rows_in, input_weight, middle_weight, output_weight).T
        answers.append(
            lax.all_to_all(result.reshape(features, experts, width), "lon", split_axis=1, concat_axis=1, tiled=True)
        )
    returned = jnp.concatenate(answers, axis=2)
    tendency = returned.reshape(features, -1)[:, targets]
    return (current + tendency.astype(jnp.float32).reshape(current.shape)).reshape(column_state.shape)


def solution(mesh):
    in_specs = (
        P(None, None, "lat", "lon"),
        P(None, None, "lat", "lon"),
        P(None, "lat", "lon"),
        P("lat", "lon", None),
        P("lon", None, None),
        P("lon", None, None, None),
        P("lon", None, None),
    )
    out_specs = P(None, None, "lat", "lon")
    return jax.shard_map(local, mesh=mesh, in_specs=in_specs, out_specs=out_specs, check_vma=False)
```

```python
import jax
import jax.numpy as jnp
from jax import lax
from jax.experimental import pallas as pl
from jax.experimental.pallas import tpu as pltpu
from jax.sharding import PartitionSpec as P


def neighbours(axis, periodic):
    count = lax.axis_size(axis)
    forward = [(i, i + 1) for i in range(count - 1)]
    if periodic:
        forward.append((count - 1, 0))
    backward = [(target, source) for source, target in forward]
    return forward, backward


FB = 32

def sweep_kernel(q_ref, hn_ref, hs_ref, he_ref, hw_ref, u_ref, v_ref, k_ref, o_ref):
    rows, cols = q_ref.shape[1], q_ref.shape[2]
    row = lax.broadcasted_iota(jnp.int32, (rows, cols), 0)
    lane = lax.broadcasted_iota(jnp.int32, (rows, cols), 1)
    he = he_ref[0]
    hw = hw_ref[0]
    for f in range(FB):
        q = q_ref[f]
        north = jnp.where(row == rows - 1, jnp.broadcast_to(hn_ref[f], (rows, cols)), pltpu.roll(q, rows - 1, 0))
        south = jnp.where(row == 0, jnp.broadcast_to(hs_ref[f], (rows, cols)), pltpu.roll(q, 1, 0))
        east = jnp.where(lane == cols - 1, jnp.broadcast_to(he[:, f:f + 1], (rows, cols)), pltpu.roll(q, cols - 1, 1))
        west = jnp.where(lane == 0, jnp.broadcast_to(hw[:, f:f + 1], (rows, cols)), pltpu.roll(q, 1, 1))
        u = u_ref[f]
        v = v_ref[f]
        k = k_ref[f]
        o_ref[f] = (q - 0.5 * u * (east - west) - 0.5 * v * (north - south)
                    + k * (east + west + north + south - 4.0 * q))


def sweep(q, hn, hs, he, hw, u, v, k):
    feats, rows, cols = q.shape
    levels = u.shape[0]
    nb = feats // FB
    per = levels // FB
    big = pl.BlockSpec((FB, rows, cols), lambda i: (i, 0, 0))
    field = pl.BlockSpec((FB, rows, cols), lambda i: (i % per, 0, 0))
    edge_row = pl.BlockSpec((FB, 1, cols), lambda i: (i, 0, 0))
    edge_col = pl.BlockSpec((1, rows, FB), lambda i: (i, 0, 0))
    return pl.pallas_call(
        sweep_kernel,
        grid=(nb,),
        in_specs=[big, edge_row, edge_row, edge_col, edge_col, field, field, field],
        out_specs=big,
        out_shape=jax.ShapeDtypeStruct(q.shape, q.dtype),
        cost_estimate=pl.CostEstimate(flops=20 * q.size, bytes_accessed=8 * q.size + 12 * u.size, transcendentals=0),
    )(q, hn, hs, he, hw, u, v, k)


def columns_of(edge):
    feats, rows = edge.shape
    return jnp.swapaxes(edge.reshape(feats // FB, FB, rows), 1, 2)


def step(x, u, v, k):
    feats, rows, cols = x.shape
    lat_forward, lat_backward = neighbours("lat", False)
    lon_forward, lon_backward = neighbours("lon", True)
    hn = lax.ppermute(x[:, :1, :], "lat", lat_backward)
    hs = lax.ppermute(x[:, rows - 1:, :], "lat", lat_forward)
    he = lax.ppermute(columns_of(x[:, :, 0]), "lon", lon_backward)
    hw = lax.ppermute(columns_of(x[:, :, cols - 1]), "lon", lon_forward)
    return sweep(x, hn, hs, he, hw, u, v, k)


def positions(targets_all, experts):
    count = targets_all.shape[0]
    block = 128
    onehot = (targets_all[:, None] == jnp.arange(experts, dtype=jnp.int32)[None, :]).astype(
        jnp.bfloat16
    )
    blocks = onehot.reshape(count // block, block, experts)
    rows = jnp.arange(block, dtype=jnp.int32)
    before = (rows[:, None] > rows[None, :]).astype(jnp.bfloat16)
    within = jnp.einsum("ij,bje->bie", before, blocks, preferred_element_type=jnp.float32)
    totals = jnp.sum(blocks.astype(jnp.float32), axis=1)
    offsets = jnp.cumsum(totals, axis=0) - totals
    ranks = within + offsets[:, None, :]
    position = jnp.sum(ranks * blocks.astype(jnp.float32), axis=2)
    return position.reshape(count).astype(jnp.int32)


ROWS = 1024
HALF = 128


def silu(t):
    return t * (0.5 * jnp.tanh(0.5 * t) + 0.5)


def layers(x, w_first, w_middle, w_last):
    hidden = silu(jnp.dot(x, w_first, preferred_element_type=jnp.float32)).astype(jnp.bfloat16)
    for layer_index in range(w_middle.shape[0]):
        hidden = silu(
            jnp.dot(hidden, w_middle[layer_index], preferred_element_type=jnp.float32)
        ).astype(jnp.bfloat16)
    return jnp.dot(hidden, w_last, preferred_element_type=jnp.float32).astype(jnp.bfloat16)


def network_kernel(active_ref, source_ref, x_hbm, first_ref, middle_ref, last_ref, o_hbm, buf, res, lsem, ssem):
    block = pl.program_id(0)
    blocks = pl.num_programs(0)
    active = active_ref[0]
    slot = block % 2
    per = ROWS // HALF

    def loads(index, into):
        return [
            pltpu.make_async_copy(
                x_hbm.at[pl.ds(source_ref[index * per + j] * HALF, HALF)],
                buf.at[into, pl.ds(j * HALF, HALF)],
                lsem.at[into, j],
            )
            for j in range(per)
        ]

    def stores(index, outof):
        return [
            pltpu.make_async_copy(
                res.at[outof, pl.ds(j * HALF, HALF)],
                o_hbm.at[pl.ds(source_ref[index * per + j] * HALF, HALF)],
                ssem.at[outof, j],
            )
            for j in range(per)
        ]

    @pl.when((block == 0) & (active > 0))
    def _():
        for copy in loads(0, 0):
            copy.start()

    @pl.when(block + 1 < active)
    def _():
        for copy in loads(block + 1, 1 - slot):
            copy.start()

    @pl.when(block >= 2)
    def _():
        for copy in stores(block - 2, slot):
            copy.wait()

    @pl.when(block < active)
    def _():
        for copy in loads(block, slot):
            copy.wait()
        res[slot] = layers(buf[slot], first_ref[...], middle_ref[...], last_ref[...])

    @pl.when(block >= active)
    def _():
        res[slot] = jnp.zeros(res.shape[1:], res.dtype)

    for copy in stores(block, slot):
        copy.start()

    @pl.when(block == blocks - 1)
    def _():
        for copy in stores(block - 1, 1 - slot):
            copy.wait()
        for copy in stores(block, slot):
            copy.wait()


def network(rows_in, input_weight, middle_weight, output_weight):
    count, feats = rows_in.shape
    groups = count // HALF
    hid = input_weight.shape[1]
    first = input_weight[0].T
    middle = jnp.swapaxes(middle_weight[0], 1, 2)
    last = output_weight[0].T
    grouped = rows_in.reshape(groups, HALF, feats)
    nonzero = jnp.any(grouped != 0, axis=(1, 2)).astype(jnp.int32)
    used = jnp.sum(nonzero)
    ahead = jnp.cumsum(nonzero) - nonzero
    place = jnp.where(nonzero > 0, ahead, used + jnp.arange(groups, dtype=jnp.int32) - ahead)
    source = jnp.zeros((groups,), jnp.int32).at[place].set(jnp.arange(groups, dtype=jnp.int32))
    active = ((used * HALF + ROWS - 1) // ROWS).reshape(1)
    mats = 2 * (hid * feats * 2 + middle_weight.shape[1] * hid * hid)
    per = ROWS // HALF
    return pl.pallas_call(
        network_kernel,
        grid_spec=pltpu.PrefetchScalarGridSpec(
            num_scalar_prefetch=2,
            grid=(count // ROWS,),
            in_specs=[
                pl.BlockSpec(memory_space=pl.ANY),
                pl.BlockSpec(first.shape, lambda i, a, s: (0, 0)),
                pl.BlockSpec(middle.shape, lambda i, a, s: (0, 0, 0)),
                pl.BlockSpec(last.shape, lambda i, a, s: (0, 0)),
            ],
            out_specs=pl.BlockSpec(memory_space=pl.ANY),
            scratch_shapes=[
                pltpu.VMEM((2, ROWS, feats), jnp.bfloat16),
                pltpu.VMEM((2, ROWS, feats), jnp.bfloat16),
                pltpu.SemaphoreType.DMA((2, per)),
                pltpu.SemaphoreType.DMA((2, per)),
            ],
        ),
        out_shape=jax.ShapeDtypeStruct((count, feats), jnp.bfloat16),
        cost_estimate=pl.CostEstimate(
            flops=mats * count,
            bytes_accessed=4 * count * feats + 2 * (mats // 2),
            transcendentals=(1 + middle_weight.shape[1]) * hid * count,
        ),
    )(active, source, rows_in, first, middle, last)


def pack_kernel(t_ref, cur_ref, o_ref, rows, full):
    feats, lat_cells, lon_cells = cur_ref.shape
    for r in range(lat_cells):
        rows[r * lon_cells:(r + 1) * lon_cells, :] = cur_ref[:, r, :].T
    full[...] = jnp.zeros(full.shape, full.dtype)

    def body(i, carry):
        for u in range(8):
            c = i * 8 + u
            full[pl.ds(t_ref[c], 1), :] = rows[pl.ds(c, 1), :]
        return carry

    lax.fori_loop(0, rows.shape[0] // 8, body, 0)
    o_ref[...] = full[...].astype(o_ref.dtype)


def pack(targets, current, slots):
    feats, lat_cells, lon_cells = current.shape
    count = lat_cells * lon_cells
    return pl.pallas_call(
        pack_kernel,
        grid_spec=pltpu.PrefetchScalarGridSpec(
            num_scalar_prefetch=1,
            grid=(1,),
            in_specs=[pl.BlockSpec(current.shape, lambda i, t: (0, 0, 0))],
            out_specs=pl.BlockSpec((slots, feats), lambda i, t: (0, 0)),
            scratch_shapes=[pltpu.VMEM((count, feats), jnp.float32), pltpu.VMEM((slots, feats), jnp.float32)],
        ),
        out_shape=jax.ShapeDtypeStruct((slots, feats), jnp.bfloat16),
    )(targets, current)


def combine_kernel(t_ref, ret_ref, cur_ref, o_ref, full, tend):
    feats, lat_cells, lon_cells = cur_ref.shape
    full[...] = ret_ref[...].astype(jnp.float32)

    def body(i, carry):
        for u in range(8):
            c = i * 8 + u
            tend[pl.ds(c, 1), :] = full[pl.ds(t_ref[c], 1), :]
        return carry

    lax.fori_loop(0, tend.shape[0] // 8, body, 0)
    for r in range(lat_cells):
        o_ref[:, r, :] = cur_ref[:, r, :] + tend[r * lon_cells:(r + 1) * lon_cells, :].T


def combine(targets, returned_rows, current):
    feats, lat_cells, lon_cells = current.shape
    slots = returned_rows.shape[0]
    return pl.pallas_call(
        combine_kernel,
        grid_spec=pltpu.PrefetchScalarGridSpec(
            num_scalar_prefetch=1,
            grid=(1,),
            in_specs=[
                pl.BlockSpec((slots, feats), lambda i, t: (0, 0)),
                pl.BlockSpec(current.shape, lambda i, t: (0, 0, 0)),
            ],
            out_specs=pl.BlockSpec(current.shape, lambda i, t: (0, 0, 0)),
            scratch_shapes=[
                pltpu.VMEM((slots, feats), jnp.float32),
                pltpu.VMEM((lat_cells * lon_cells, feats), jnp.float32),
            ],
        ),
        out_shape=jax.ShapeDtypeStruct(current.shape, jnp.float32),
    )(targets, returned_rows, current)


def local(
    column_state, wind_speed, diffusivity, batch_index, input_weight, middle_weight, output_weight
):
    num_vars, levels, lat_cells, lon_cells = column_state.shape
    features = num_vars * levels
    current = column_state.reshape(features, lat_cells, lon_cells)
    for sweep_index in range(2):
        current = step(current, wind_speed[0], wind_speed[1], diffusivity)
    column_count = lat_cells * lon_cells
    experts = lax.axis_size("lon")
    capacity = 2 * column_count // experts
    targets_all = batch_index.reshape(column_count)
    position = positions(targets_all, experts)
    targets = targets_all * capacity + position
    packed = pack(targets, current, experts * capacity).T.reshape(features, experts, capacity)
    chunks = 1
    width = capacity // chunks
    answers = []
    for chunk in range(chunks):
        part = packed[:, :, chunk * width:(chunk + 1) * width]
        received = lax.all_to_all(part, "lon", split_axis=1, concat_axis=1, tiled=True)
        rows_in = received.reshape(features, experts * width).T
        result = network(rows_in, input_weight, middle_weight, output_weight).T
        answers.append(
            lax.all_to_all(result.reshape(features, experts, width), "lon", split_axis=1, concat_axis=1, tiled=True)
        )
    returned = jnp.concatenate(answers, axis=2)
    return combine(targets, returned.reshape(features, -1).T, current).reshape(column_state.shape)


def solution(mesh):
    in_specs = (
        P(None, None, "lat", "lon"),
        P(None, None, "lat", "lon"),
        P(None, "lat", "lon"),
        P("lat", "lon", None),
        P("lon", None, None),
        P("lon", None, None, None),
        P("lon", None, None),
    )
    out_specs = P(None, None, "lat", "lon")
    return jax.shard_map(local, mesh=mesh, in_specs=in_specs, out_specs=out_specs, check_vma=False)
```

```python
import jax
import jax.numpy as jnp
from jax import lax
from jax.experimental import pallas as pl
from jax.experimental.pallas import tpu as pltpu
from jax.sharding import PartitionSpec as P


def neighbours(axis, periodic):
    count = lax.axis_size(axis)
    forward = [(i, i + 1) for i in range(count - 1)]
    if periodic:
        forward.append((count - 1, 0))
    backward = [(target, source) for source, target in forward]
    return forward, backward


FB = 8


def keep_edges(f, s, top_ref, bottom_ref, lanes, first, last):
    rows, cols = s.shape
    top_ref[f] = s[0:1, :]
    bottom_ref[f] = s[rows - 1:rows, :]
    first = jnp.where(lanes == f, jnp.broadcast_to(s[:, 0:1], first.shape), first)
    last = jnp.where(lanes == f, jnp.broadcast_to(s[:, cols - 1:cols], last.shape), last)
    return first, last


def edges_kernel(q_ref, top_ref, bottom_ref, first_ref, last_ref):
    rows = q_ref.shape[1]
    lanes = lax.broadcasted_iota(jnp.int32, (rows, FB), 1)
    first = jnp.zeros((rows, FB), jnp.float32)
    last = jnp.zeros((rows, FB), jnp.float32)
    for f in range(FB):
        first, last = keep_edges(f, q_ref[f], top_ref, bottom_ref, lanes, first, last)
    first_ref[0] = first
    last_ref[0] = last


def sweep_kernel(q_ref, hn_ref, hs_ref, he_ref, hw_ref, u_ref, v_ref, k_ref,
                 o_ref, top_ref, bottom_ref, first_ref, last_ref):
    rows, cols = q_ref.shape[1], q_ref.shape[2]
    row = lax.broadcasted_iota(jnp.int32, (rows, cols), 0)
    lane = lax.broadcasted_iota(jnp.int32, (rows, cols), 1)
    lanes = lax.broadcasted_iota(jnp.int32, (rows, FB), 1)
    he = he_ref[0]
    hw = hw_ref[0]
    first = jnp.zeros((rows, FB), jnp.float32)
    last = jnp.zeros((rows, FB), jnp.float32)
    for f in range(FB):
        q = q_ref[f]
        north = jnp.where(row == rows - 1, jnp.broadcast_to(hn_ref[f], (rows, cols)), pltpu.roll(q, rows - 1, 0))
        south = jnp.where(row == 0, jnp.broadcast_to(hs_ref[f], (rows, cols)), pltpu.roll(q, 1, 0))
        east = jnp.where(lane == cols - 1, jnp.broadcast_to(he[:, f:f + 1], (rows, cols)), pltpu.roll(q, cols - 1, 1))
        west = jnp.where(lane == 0, jnp.broadcast_to(hw[:, f:f + 1], (rows, cols)), pltpu.roll(q, 1, 1))
        u = u_ref[f]
        v = v_ref[f]
        k = k_ref[f]
        s = (q - 0.5 * u * (east - west) - 0.5 * v * (north - south)
             + k * (east + west + north + south - 4.0 * q))
        o_ref[f] = s
        first, last = keep_edges(f, s, top_ref, bottom_ref, lanes, first, last)
    first_ref[0] = first
    last_ref[0] = last


def edge_specs(feats, rows, cols):
    nb = feats // FB
    edge_row = pl.BlockSpec((FB, 1, cols), lambda i: (i, 0, 0))
    edge_col = pl.BlockSpec((1, rows, FB), lambda i: (i, 0, 0))
    shapes = [
        jax.ShapeDtypeStruct((feats, 1, cols), jnp.float32),
        jax.ShapeDtypeStruct((feats, 1, cols), jnp.float32),
        jax.ShapeDtypeStruct((nb, rows, FB), jnp.float32),
        jax.ShapeDtypeStruct((nb, rows, FB), jnp.float32),
    ]
    return [edge_row, edge_row, edge_col, edge_col], shapes


def edges(q):
    feats, rows, cols = q.shape
    specs, shapes = edge_specs(feats, rows, cols)
    return pl.pallas_call(
        edges_kernel,
        grid=(feats // FB,),
        in_specs=[pl.BlockSpec((FB, rows, cols), lambda i: (i, 0, 0))],
        out_specs=specs,
        out_shape=shapes,
    )(q)


def sweep(q, halos, u, v, k):
    feats, rows, cols = q.shape
    levels = u.shape[0]
    nb = feats // FB
    per = levels // FB
    big = pl.BlockSpec((FB, rows, cols), lambda i: (i, 0, 0))
    field = pl.BlockSpec((FB, rows, cols), lambda i: (i % per, 0, 0))
    specs, shapes = edge_specs(feats, rows, cols)
    return pl.pallas_call(
        sweep_kernel,
        grid=(nb,),
        in_specs=[big] + specs + [field, field, field],
        out_specs=[big] + specs,
        out_shape=[jax.ShapeDtypeStruct(q.shape, q.dtype)] + shapes,
        cost_estimate=pl.CostEstimate(flops=20 * q.size, bytes_accessed=8 * q.size + 12 * u.size, transcendentals=0),
    )(q, *halos, u, v, k)


def exchange(top, bottom, first, last):
    lat_forward, lat_backward = neighbours("lat", False)
    lon_forward, lon_backward = neighbours("lon", True)
    hn = lax.ppermute(top, "lat", lat_backward)
    hs = lax.ppermute(bottom, "lat", lat_forward)
    he = lax.ppermute(first, "lon", lon_backward)
    hw = lax.ppermute(last, "lon", lon_forward)
    return hn, hs, he, hw


def positions(targets_all, experts):
    count = targets_all.shape[0]
    block = 128
    onehot = (targets_all[:, None] == jnp.arange(experts, dtype=jnp.int32)[None, :]).astype(
        jnp.bfloat16
    )
    blocks = onehot.reshape(count // block, block, experts)
    rows = jnp.arange(block, dtype=jnp.int32)
    before = (rows[:, None] > rows[None, :]).astype(jnp.bfloat16)
    within = jnp.einsum("ij,bje->bie", before, blocks, preferred_element_type=jnp.float32)
    totals = jnp.sum(blocks.astype(jnp.float32), axis=1)
    offsets = jnp.cumsum(totals, axis=0) - totals
    ranks = within + offsets[:, None, :]
    position = jnp.sum(ranks * blocks.astype(jnp.float32), axis=2)
    return position.reshape(count).astype(jnp.int32)


ROWS = 1024
HALF = 128


def silu(t):
    return t * (0.5 * jnp.tanh(0.5 * t) + 0.5)


def layers(x, w_first, w_middle, w_last):
    hidden = silu(jnp.dot(x, w_first, preferred_element_type=jnp.float32)).astype(jnp.bfloat16)
    for layer_index in range(w_middle.shape[0]):
        hidden = silu(
            jnp.dot(hidden, w_middle[layer_index], preferred_element_type=jnp.float32)
        ).astype(jnp.bfloat16)
    return jnp.dot(hidden, w_last, preferred_element_type=jnp.float32).astype(jnp.bfloat16)


def network_kernel(active_ref, source_ref, x_hbm, first_ref, middle_ref, last_ref, o_hbm, buf, res, lsem, ssem):
    block = pl.program_id(0)
    blocks = pl.num_programs(0)
    active = active_ref[0]
    slot = block % 2
    per = ROWS // HALF

    def loads(index, into):
        return [
            pltpu.make_async_copy(
                x_hbm.at[pl.ds(source_ref[index * per + j] * HALF, HALF)],
                buf.at[into, pl.ds(j * HALF, HALF)],
                lsem.at[into, j],
            )
            for j in range(per)
        ]

    def stores(index, outof):
        return [
            pltpu.make_async_copy(
                res.at[outof, pl.ds(j * HALF, HALF)],
                o_hbm.at[pl.ds(source_ref[index * per + j] * HALF, HALF)],
                ssem.at[outof, j],
            )
            for j in range(per)
        ]

    @pl.when((block == 0) & (active > 0))
    def _():
        for copy in loads(0, 0):
            copy.start()

    @pl.when(block + 1 < active)
    def _():
        for copy in loads(block + 1, 1 - slot):
            copy.start()

    @pl.when(block >= 2)
    def _():
        for copy in stores(block - 2, slot):
            copy.wait()

    @pl.when(block < active)
    def _():
        for copy in loads(block, slot):
            copy.wait()
        res[slot] = layers(buf[slot], first_ref[...], middle_ref[...], last_ref[...])

    @pl.when(block >= active)
    def _():
        res[slot] = jnp.zeros(res.shape[1:], res.dtype)

    for copy in stores(block, slot):
        copy.start()

    @pl.when(block == blocks - 1)
    def _():
        for copy in stores(block - 1, 1 - slot):
            copy.wait()
        for copy in stores(block, slot):
            copy.wait()


def network(rows_in, input_weight, middle_weight, output_weight):
    count, feats = rows_in.shape
    groups = count // HALF
    hid = input_weight.shape[1]
    first = input_weight[0].T
    middle = jnp.swapaxes(middle_weight[0], 1, 2)
    last = output_weight[0].T
    grouped = rows_in.reshape(groups, HALF, feats)
    nonzero = jnp.any(grouped != 0, axis=(1, 2)).astype(jnp.int32)
    used = jnp.sum(nonzero)
    ahead = jnp.cumsum(nonzero) - nonzero
    place = jnp.where(nonzero > 0, ahead, used + jnp.arange(groups, dtype=jnp.int32) - ahead)
    source = jnp.zeros((groups,), jnp.int32).at[place].set(jnp.arange(groups, dtype=jnp.int32))
    active = ((used * HALF + ROWS - 1) // ROWS).reshape(1)
    mats = 2 * (hid * feats * 2 + middle_weight.shape[1] * hid * hid)
    per = ROWS // HALF
    return pl.pallas_call(
        network_kernel,
        grid_spec=pltpu.PrefetchScalarGridSpec(
            num_scalar_prefetch=2,
            grid=(count // ROWS,),
            in_specs=[
                pl.BlockSpec(memory_space=pl.ANY),
                pl.BlockSpec(first.shape, lambda i, a, s: (0, 0)),
                pl.BlockSpec(middle.shape, lambda i, a, s: (0, 0, 0)),
                pl.BlockSpec(last.shape, lambda i, a, s: (0, 0)),
            ],
            out_specs=pl.BlockSpec(memory_space=pl.ANY),
            scratch_shapes=[
                pltpu.VMEM((2, ROWS, feats), jnp.bfloat16),
                pltpu.VMEM((2, ROWS, feats), jnp.bfloat16),
                pltpu.SemaphoreType.DMA((2, per)),
                pltpu.SemaphoreType.DMA((2, per)),
            ],
        ),
        out_shape=jax.ShapeDtypeStruct((count, feats), jnp.bfloat16),
        cost_estimate=pl.CostEstimate(
            flops=mats * count,
            bytes_accessed=4 * count * feats + 2 * (mats // 2),
            transcendentals=(1 + middle_weight.shape[1]) * hid * count,
        ),
    )(active, source, rows_in, first, middle, last)


def pack_kernel(t_ref, cur_ref, o_ref, rows, full):
    feats, lat_cells, lon_cells = cur_ref.shape
    for r in range(lat_cells):
        rows[r * lon_cells:(r + 1) * lon_cells, :] = cur_ref[:, r, :].T
    full[...] = jnp.zeros(full.shape, full.dtype)

    def body(i, carry):
        for u in range(8):
            c = i * 8 + u
            full[pl.ds(t_ref[c], 1), :] = rows[pl.ds(c, 1), :]
        return carry

    lax.fori_loop(0, rows.shape[0] // 8, body, 0)
    o_ref[...] = full[...].astype(o_ref.dtype)


def pack(targets, current, slots):
    feats, lat_cells, lon_cells = current.shape
    count = lat_cells * lon_cells
    return pl.pallas_call(
        pack_kernel,
        grid_spec=pltpu.PrefetchScalarGridSpec(
            num_scalar_prefetch=1,
            grid=(1,),
            in_specs=[pl.BlockSpec(current.shape, lambda i, t: (0, 0, 0))],
            out_specs=pl.BlockSpec((slots, feats), lambda i, t: (0, 0)),
            scratch_shapes=[pltpu.VMEM((count, feats), jnp.float32), pltpu.VMEM((slots, feats), jnp.float32)],
        ),
        out_shape=jax.ShapeDtypeStruct((slots, feats), jnp.bfloat16),
    )(targets, current)


def combine_kernel(t_ref, ret_ref, cur_ref, o_ref, full, tend):
    feats, lat_cells, lon_cells = cur_ref.shape
    full[...] = ret_ref[...].astype(jnp.float32)

    def body(i, carry):
        for u in range(8):
            c = i * 8 + u
            tend[pl.ds(c, 1), :] = full[pl.ds(t_ref[c], 1), :]
        return carry

    lax.fori_loop(0, tend.shape[0] // 8, body, 0)
    for r in range(lat_cells):
        o_ref[:, r, :] = cur_ref[:, r, :] + tend[r * lon_cells:(r + 1) * lon_cells, :].T


def combine(targets, returned_rows, current):
    feats, lat_cells, lon_cells = current.shape
    slots = returned_rows.shape[0]
    return pl.pallas_call(
        combine_kernel,
        grid_spec=pltpu.PrefetchScalarGridSpec(
            num_scalar_prefetch=1,
            grid=(1,),
            in_specs=[
                pl.BlockSpec((slots, feats), lambda i, t: (0, 0)),
                pl.BlockSpec(current.shape, lambda i, t: (0, 0, 0)),
            ],
            out_specs=pl.BlockSpec(current.shape, lambda i, t: (0, 0, 0)),
            scratch_shapes=[
                pltpu.VMEM((slots, feats), jnp.float32),
                pltpu.VMEM((lat_cells * lon_cells, feats), jnp.float32),
            ],
        ),
        out_shape=jax.ShapeDtypeStruct(current.shape, jnp.float32),
    )(targets, returned_rows, current)


def local(
    column_state, wind_speed, diffusivity, batch_index, input_weight, middle_weight, output_weight
):
    num_vars, levels, lat_cells, lon_cells = column_state.shape
    features = num_vars * levels
    current = column_state.reshape(features, lat_cells, lon_cells)
    sides = edges(current)
    for sweep_index in range(2):
        current, *sides = sweep(current, exchange(*sides), wind_speed[0], wind_speed[1], diffusivity)
    column_count = lat_cells * lon_cells
    experts = lax.axis_size("lon")
    capacity = 2 * column_count // experts
    targets_all = batch_index.reshape(column_count)
    position = positions(targets_all, experts)
    targets = targets_all * capacity + position
    packed = pack(targets, current, experts * capacity).T.reshape(features, experts, capacity)
    chunks = 1
    width = capacity // chunks
    answers = []
    for chunk in range(chunks):
        part = packed[:, :, chunk * width:(chunk + 1) * width]
        received = lax.all_to_all(part, "lon", split_axis=1, concat_axis=1, tiled=True)
        rows_in = received.reshape(features, experts * width).T
        result = network(rows_in, input_weight, middle_weight, output_weight).T
        answers.append(
            lax.all_to_all(result.reshape(features, experts, width), "lon", split_axis=1, concat_axis=1, tiled=True)
        )
    returned = jnp.concatenate(answers, axis=2)
    return combine(targets, returned.reshape(features, -1).T, current).reshape(column_state.shape)


def solution(mesh):
    in_specs = (
        P(None, None, "lat", "lon"),
        P(None, None, "lat", "lon"),
        P(None, "lat", "lon"),
        P("lat", "lon", None),
        P("lon", None, None),
        P("lon", None, None, None),
        P("lon", None, None),
    )
    out_specs = P(None, None, "lat", "lon")
    return jax.shard_map(local, mesh=mesh, in_specs=in_specs, out_specs=out_specs, check_vma=False)
```

```python
import jax
import jax.numpy as jnp
from jax import lax
from jax.experimental import pallas as pl
from jax.experimental.pallas import tpu as pltpu
from jax.sharding import PartitionSpec as P


def neighbours(axis, periodic):
    count = lax.axis_size(axis)
    forward = [(i, i + 1) for i in range(count - 1)]
    if periodic:
        forward.append((count - 1, 0))
    backward = [(target, source) for source, target in forward]
    return forward, backward


FB = 32

def sweep_kernel(q_ref, hn_ref, hs_ref, he_ref, hw_ref, u_ref, v_ref, k_ref, o_ref):
    rows, cols = q_ref.shape[1], q_ref.shape[2]
    row = lax.broadcasted_iota(jnp.int32, (rows, cols), 0)
    lane = lax.broadcasted_iota(jnp.int32, (rows, cols), 1)
    he = he_ref[0]
    hw = hw_ref[0]
    for f in range(FB):
        q = q_ref[f]
        north = jnp.where(row == rows - 1, jnp.broadcast_to(hn_ref[f], (rows, cols)), pltpu.roll(q, rows - 1, 0))
        south = jnp.where(row == 0, jnp.broadcast_to(hs_ref[f], (rows, cols)), pltpu.roll(q, 1, 0))
        east = jnp.where(lane == cols - 1, jnp.broadcast_to(he[:, f:f + 1], (rows, cols)), pltpu.roll(q, cols - 1, 1))
        west = jnp.where(lane == 0, jnp.broadcast_to(hw[:, f:f + 1], (rows, cols)), pltpu.roll(q, 1, 1))
        u = u_ref[f]
        v = v_ref[f]
        k = k_ref[f]
        o_ref[f] = (q - 0.5 * u * (east - west) - 0.5 * v * (north - south)
                    + k * (east + west + north + south - 4.0 * q))


def sweep(q, hn, hs, he, hw, u, v, k):
    feats, rows, cols = q.shape
    levels = u.shape[0]
    nb = feats // FB
    per = levels // FB
    big = pl.BlockSpec((FB, rows, cols), lambda i: (i, 0, 0))
    field = pl.BlockSpec((FB, rows, cols), lambda i: (i % per, 0, 0))
    edge_row = pl.BlockSpec((FB, 1, cols), lambda i: (i, 0, 0))
    edge_col = pl.BlockSpec((1, rows, FB), lambda i: (i, 0, 0))
    return pl.pallas_call(
        sweep_kernel,
        grid=(nb,),
        in_specs=[big, edge_row, edge_row, edge_col, edge_col, field, field, field],
        out_specs=big,
        out_shape=jax.ShapeDtypeStruct(q.shape, q.dtype),
        cost_estimate=pl.CostEstimate(flops=20 * q.size, bytes_accessed=8 * q.size + 12 * u.size, transcendentals=0),
    )(q, hn, hs, he, hw, u, v, k)


def columns_of(edge):
    feats, rows = edge.shape
    return jnp.swapaxes(edge.reshape(feats // FB, FB, rows), 1, 2)


def step(x, u, v, k):
    feats, rows, cols = x.shape
    lat_forward, lat_backward = neighbours("lat", False)
    lon_forward, lon_backward = neighbours("lon", True)
    hn = lax.ppermute(x[:, :1, :], "lat", lat_backward)
    hs = lax.ppermute(x[:, rows - 1:, :], "lat", lat_forward)
    lane = lax.broadcasted_iota(jnp.int32, (cols, 2), 0)
    which = lax.broadcasted_iota(jnp.int32, (cols, 2), 1)
    pick = (lane == which * (cols - 1)).astype(jnp.float32)
    ends = jnp.dot(x.reshape(feats * rows, cols), pick, precision=lax.Precision.HIGHEST)
    he = lax.ppermute(columns_of(ends[:, 0].reshape(feats, rows)), "lon", lon_backward)
    hw = lax.ppermute(columns_of(ends[:, 1].reshape(feats, rows)), "lon", lon_forward)
    return sweep(x, hn, hs, he, hw, u, v, k)


def positions(targets_all, experts):
    count = targets_all.shape[0]
    block = 128
    onehot = (targets_all[:, None] == jnp.arange(experts, dtype=jnp.int32)[None, :]).astype(
        jnp.bfloat16
    )
    blocks = onehot.reshape(count // block, block, experts)
    rows = jnp.arange(block, dtype=jnp.int32)
    before = (rows[:, None] > rows[None, :]).astype(jnp.bfloat16)
    within = jnp.einsum("ij,bje->bie", before, blocks, preferred_element_type=jnp.float32)
    totals = jnp.sum(blocks.astype(jnp.float32), axis=1)
    offsets = jnp.cumsum(totals, axis=0) - totals
    ranks = within + offsets[:, None, :]
    position = jnp.sum(ranks * blocks.astype(jnp.float32), axis=2)
    return position.reshape(count).astype(jnp.int32)


ROWS = 1024
HALF = 128


def silu(t):
    return t * (0.5 * jnp.tanh(0.5 * t) + 0.5)


def layers(x, w_first, w_middle, w_last):
    hidden = silu(jnp.dot(x, w_first, preferred_element_type=jnp.float32)).astype(jnp.bfloat16)
    for layer_index in range(w_middle.shape[0]):
        hidden = silu(
            jnp.dot(hidden, w_middle[layer_index], preferred_element_type=jnp.float32)
        ).astype(jnp.bfloat16)
    return jnp.dot(hidden, w_last, preferred_element_type=jnp.float32).astype(jnp.bfloat16)


def network_kernel(active_ref, source_ref, x_hbm, first_ref, middle_ref, last_ref, o_hbm, buf, res, lsem, ssem):
    block = pl.program_id(0)
    blocks = pl.num_programs(0)
    active = active_ref[0]
    slot = block % 2
    per = ROWS // HALF

    def loads(index, into):
        return [
            pltpu.make_async_copy(
                x_hbm.at[pl.ds(source_ref[index * per + j] * HALF, HALF)],
                buf.at[into, pl.ds(j * HALF, HALF)],
                lsem.at[into, j],
            )
            for j in range(per)
        ]

    def stores(index, outof):
        return [
            pltpu.make_async_copy(
                res.at[outof, pl.ds(j * HALF, HALF)],
                o_hbm.at[pl.ds(source_ref[index * per + j] * HALF, HALF)],
                ssem.at[outof, j],
            )
            for j in range(per)
        ]

    @pl.when((block == 0) & (active > 0))
    def _():
        for copy in loads(0, 0):
            copy.start()

    @pl.when(block + 1 < active)
    def _():
        for copy in loads(block + 1, 1 - slot):
            copy.start()

    @pl.when(block >= 2)
    def _():
        for copy in stores(block - 2, slot):
            copy.wait()

    @pl.when(block < active)
    def _():
        for copy in loads(block, slot):
            copy.wait()
        res[slot] = layers(buf[slot], first_ref[...], middle_ref[...], last_ref[...])

    @pl.when(block >= active)
    def _():
        res[slot] = jnp.zeros(res.shape[1:], res.dtype)

    for copy in stores(block, slot):
        copy.start()

    @pl.when(block == blocks - 1)
    def _():
        for copy in stores(block - 1, 1 - slot):
            copy.wait()
        for copy in stores(block, slot):
            copy.wait()


def network(rows_in, input_weight, middle_weight, output_weight):
    count, feats = rows_in.shape
    groups = count // HALF
    hid = input_weight.shape[1]
    first = input_weight[0].T
    middle = jnp.swapaxes(middle_weight[0], 1, 2)
    last = output_weight[0].T
    grouped = rows_in.reshape(groups, HALF, feats)
    nonzero = jnp.any(grouped != 0, axis=(1, 2)).astype(jnp.int32)
    used = jnp.sum(nonzero)
    ahead = jnp.cumsum(nonzero) - nonzero
    place = jnp.where(nonzero > 0, ahead, used + jnp.arange(groups, dtype=jnp.int32) - ahead)
    source = jnp.zeros((groups,), jnp.int32).at[place].set(jnp.arange(groups, dtype=jnp.int32))
    active = ((used * HALF + ROWS - 1) // ROWS).reshape(1)
    mats = 2 * (hid * feats * 2 + middle_weight.shape[1] * hid * hid)
    per = ROWS // HALF
    return pl.pallas_call(
        network_kernel,
        grid_spec=pltpu.PrefetchScalarGridSpec(
            num_scalar_prefetch=2,
            grid=(count // ROWS,),
            in_specs=[
                pl.BlockSpec(memory_space=pl.ANY),
                pl.BlockSpec(first.shape, lambda i, a, s: (0, 0)),
                pl.BlockSpec(middle.shape, lambda i, a, s: (0, 0, 0)),
                pl.BlockSpec(last.shape, lambda i, a, s: (0, 0)),
            ],
            out_specs=pl.BlockSpec(memory_space=pl.ANY),
            scratch_shapes=[
                pltpu.VMEM((2, ROWS, feats), jnp.bfloat16),
                pltpu.VMEM((2, ROWS, feats), jnp.bfloat16),
                pltpu.SemaphoreType.DMA((2, per)),
                pltpu.SemaphoreType.DMA((2, per)),
            ],
        ),
        out_shape=jax.ShapeDtypeStruct((count, feats), jnp.bfloat16),
        cost_estimate=pl.CostEstimate(
            flops=mats * count,
            bytes_accessed=4 * count * feats + 2 * (mats // 2),
            transcendentals=(1 + middle_weight.shape[1]) * hid * count,
        ),
    )(active, source, rows_in, first, middle, last)


def pack_kernel(t_ref, cur_ref, o_ref, rows, full):
    feats, lat_cells, lon_cells = cur_ref.shape
    for r in range(lat_cells):
        rows[r * lon_cells:(r + 1) * lon_cells, :] = cur_ref[:, r, :].T
    full[...] = jnp.zeros(full.shape, full.dtype)

    def body(i, carry):
        for u in range(8):
            c = i * 8 + u
            full[pl.ds(t_ref[c], 1), :] = rows[pl.ds(c, 1), :]
        return carry

    lax.fori_loop(0, rows.shape[0] // 8, body, 0)
    o_ref[...] = full[...].astype(o_ref.dtype)


def pack(targets, current, slots):
    feats, lat_cells, lon_cells = current.shape
    count = lat_cells * lon_cells
    return pl.pallas_call(
        pack_kernel,
        grid_spec=pltpu.PrefetchScalarGridSpec(
            num_scalar_prefetch=1,
            grid=(1,),
            in_specs=[pl.BlockSpec(current.shape, lambda i, t: (0, 0, 0))],
            out_specs=pl.BlockSpec((slots, feats), lambda i, t: (0, 0)),
            scratch_shapes=[pltpu.VMEM((count, feats), jnp.float32), pltpu.VMEM((slots, feats), jnp.float32)],
        ),
        out_shape=jax.ShapeDtypeStruct((slots, feats), jnp.bfloat16),
    )(targets, current)


def combine_kernel(t_ref, ret_ref, cur_ref, o_ref, full, tend):
    feats, lat_cells, lon_cells = cur_ref.shape
    full[...] = ret_ref[...].astype(jnp.float32)

    def body(i, carry):
        for u in range(8):
            c = i * 8 + u
            tend[pl.ds(c, 1), :] = full[pl.ds(t_ref[c], 1), :]
        return carry

    lax.fori_loop(0, tend.shape[0] // 8, body, 0)
    for r in range(lat_cells):
        o_ref[:, r, :] = cur_ref[:, r, :] + tend[r * lon_cells:(r + 1) * lon_cells, :].T


def combine(targets, returned_rows, current):
    feats, lat_cells, lon_cells = current.shape
    slots = returned_rows.shape[0]
    return pl.pallas_call(
        combine_kernel,
        grid_spec=pltpu.PrefetchScalarGridSpec(
            num_scalar_prefetch=1,
            grid=(1,),
            in_specs=[
                pl.BlockSpec((slots, feats), lambda i, t: (0, 0)),
                pl.BlockSpec(current.shape, lambda i, t: (0, 0, 0)),
            ],
            out_specs=pl.BlockSpec(current.shape, lambda i, t: (0, 0, 0)),
            scratch_shapes=[
                pltpu.VMEM((slots, feats), jnp.float32),
                pltpu.VMEM((lat_cells * lon_cells, feats), jnp.float32),
            ],
        ),
        out_shape=jax.ShapeDtypeStruct(current.shape, jnp.float32),
    )(targets, returned_rows, current)


def local(
    column_state, wind_speed, diffusivity, batch_index, input_weight, middle_weight, output_weight
):
    num_vars, levels, lat_cells, lon_cells = column_state.shape
    features = num_vars * levels
    current = column_state.reshape(features, lat_cells, lon_cells)
    for sweep_index in range(2):
        current = step(current, wind_speed[0], wind_speed[1], diffusivity)
    column_count = lat_cells * lon_cells
    experts = lax.axis_size("lon")
    capacity = 2 * column_count // experts
    targets_all = batch_index.reshape(column_count)
    position = positions(targets_all, experts)
    targets = targets_all * capacity + position
    packed = pack(targets, current, experts * capacity).T.reshape(features, experts, capacity)
    chunks = 1
    width = capacity // chunks
    answers = []
    for chunk in range(chunks):
        part = packed[:, :, chunk * width:(chunk + 1) * width]
        received = lax.all_to_all(part, "lon", split_axis=1, concat_axis=1, tiled=True)
        rows_in = received.reshape(features, experts * width).T
        result = network(rows_in, input_weight, middle_weight, output_weight).T
        answers.append(
            lax.all_to_all(result.reshape(features, experts, width), "lon", split_axis=1, concat_axis=1, tiled=True)
        )
    returned = jnp.concatenate(answers, axis=2)
    return combine(targets, returned.reshape(features, -1).T, current).reshape(column_state.shape)


def solution(mesh):
    in_specs = (
        P(None, None, "lat", "lon"),
        P(None, None, "lat", "lon"),
        P(None, "lat", "lon"),
        P("lat", "lon", None),
        P("lon", None, None),
        P("lon", None, None, None),
        P("lon", None, None),
    )
    out_specs = P(None, None, "lat", "lon")
    return jax.shard_map(local, mesh=mesh, in_specs=in_specs, out_specs=out_specs, check_vma=False)
```

```python
import jax
import jax.numpy as jnp
from jax import lax
from jax.experimental import pallas as pl
from jax.experimental.pallas import tpu as pltpu
from jax.sharding import PartitionSpec as P


def neighbours(axis, periodic):
    count = lax.axis_size(axis)
    forward = [(i, i + 1) for i in range(count - 1)]
    if periodic:
        forward.append((count - 1, 0))
    backward = [(target, source) for source, target in forward]
    return forward, backward


FB = 32

def sweep_kernel(q_ref, hn_ref, hs_ref, he_ref, hw_ref, u_ref, v_ref, k_ref, o_ref):
    rows, cols = q_ref.shape[1], q_ref.shape[2]
    row = lax.broadcasted_iota(jnp.int32, (rows, cols), 0)
    lane = lax.broadcasted_iota(jnp.int32, (rows, cols), 1)
    he = he_ref[0]
    hw = hw_ref[0]
    for f in range(FB):
        q = q_ref[f]
        north = jnp.where(row == rows - 1, jnp.broadcast_to(hn_ref[f], (rows, cols)), pltpu.roll(q, rows - 1, 0))
        south = jnp.where(row == 0, jnp.broadcast_to(hs_ref[f], (rows, cols)), pltpu.roll(q, 1, 0))
        east = jnp.where(lane == cols - 1, jnp.broadcast_to(he[:, f:f + 1], (rows, cols)), pltpu.roll(q, cols - 1, 1))
        west = jnp.where(lane == 0, jnp.broadcast_to(hw[:, f:f + 1], (rows, cols)), pltpu.roll(q, 1, 1))
        u = u_ref[f]
        v = v_ref[f]
        k = k_ref[f]
        o_ref[f] = (q - 0.5 * u * (east - west) - 0.5 * v * (north - south)
                    + k * (east + west + north + south - 4.0 * q))


def sweep(q, hn, hs, he, hw, u, v, k):
    feats, rows, cols = q.shape
    levels = u.shape[0]
    nb = feats // FB
    per = levels // FB
    big = pl.BlockSpec((FB, rows, cols), lambda i: (i, 0, 0))
    field = pl.BlockSpec((FB, rows, cols), lambda i: (i % per, 0, 0))
    edge_row = pl.BlockSpec((FB, 1, cols), lambda i: (i, 0, 0))
    edge_col = pl.BlockSpec((1, rows, FB), lambda i: (i, 0, 0))
    return pl.pallas_call(
        sweep_kernel,
        grid=(nb,),
        in_specs=[big, edge_row, edge_row, edge_col, edge_col, field, field, field],
        out_specs=big,
        out_shape=jax.ShapeDtypeStruct(q.shape, q.dtype),
        cost_estimate=pl.CostEstimate(flops=20 * q.size, bytes_accessed=8 * q.size + 12 * u.size, transcendentals=0),
    )(q, hn, hs, he, hw, u, v, k)


def columns_of(edge):
    feats, rows = edge.shape
    return jnp.swapaxes(edge.reshape(feats // FB, FB, rows), 1, 2)


def step(x, u, v, k):
    feats, rows, cols = x.shape
    lat_forward, lat_backward = neighbours("lat", False)
    lon_forward, lon_backward = neighbours("lon", True)
    hn = lax.ppermute(x[:, :1, :], "lat", lat_backward)
    hs = lax.ppermute(x[:, rows - 1:, :], "lat", lat_forward)
    lane = lax.broadcasted_iota(jnp.int32, (cols, 2), 0)
    which = lax.broadcasted_iota(jnp.int32, (cols, 2), 1)
    pick = (lane == which * (cols - 1)).astype(jnp.float32)
    ends = jnp.dot(x.reshape(feats * rows, cols), pick, precision=lax.Precision.HIGHEST)
    he = lax.ppermute(columns_of(ends[:, 0].reshape(feats, rows)), "lon", lon_backward)
    hw = lax.ppermute(columns_of(ends[:, 1].reshape(feats, rows)), "lon", lon_forward)
    return sweep(x, hn, hs, he, hw, u, v, k)


def positions(targets_all, experts):
    count = targets_all.shape[0]
    block = 128
    onehot = (targets_all[:, None] == jnp.arange(experts, dtype=jnp.int32)[None, :]).astype(
        jnp.bfloat16
    )
    blocks = onehot.reshape(count // block, block, experts)
    rows = jnp.arange(block, dtype=jnp.int32)
    before = (rows[:, None] > rows[None, :]).astype(jnp.bfloat16)
    within = jnp.einsum("ij,bje->bie", before, blocks, preferred_element_type=jnp.float32)
    totals = jnp.sum(blocks.astype(jnp.float32), axis=1)
    offsets = jnp.cumsum(totals, axis=0) - totals
    ranks = within + offsets[:, None, :]
    position = jnp.sum(ranks * blocks.astype(jnp.float32), axis=2)
    return position.reshape(count).astype(jnp.int32)


ROWS = 1024
HALF = 128


def silu(t):
    return t * (0.5 * jnp.tanh(0.5 * t) + 0.5)


def layers(x, w_first, w_middle, w_last):
    hidden = silu(jnp.dot(x, w_first, preferred_element_type=jnp.float32)).astype(jnp.bfloat16)
    for layer_index in range(w_middle.shape[0]):
        hidden = silu(
            jnp.dot(hidden, w_middle[layer_index], preferred_element_type=jnp.float32)
        ).astype(jnp.bfloat16)
    return jnp.dot(hidden, w_last, preferred_element_type=jnp.float32).astype(jnp.bfloat16)


def network_kernel(active_ref, source_ref, x_hbm, first_ref, middle_ref, last_ref, o_hbm, buf, res, lsem, ssem):
    block = pl.program_id(0)
    blocks = pl.num_programs(0)
    active = active_ref[0]
    slot = block % 2
    per = ROWS // HALF

    def loads(index, into):
        return [
            pltpu.make_async_copy(
                x_hbm.at[pl.ds(source_ref[index * per + j] * HALF, HALF)],
                buf.at[into, pl.ds(j * HALF, HALF)],
                lsem.at[into, j],
            )
            for j in range(per)
        ]

    def stores(index, outof):
        return [
            pltpu.make_async_copy(
                res.at[outof, pl.ds(j * HALF, HALF)],
                o_hbm.at[pl.ds(source_ref[index * per + j] * HALF, HALF)],
                ssem.at[outof, j],
            )
            for j in range(per)
        ]

    @pl.when((block == 0) & (active > 0))
    def _():
        for copy in loads(0, 0):
            copy.start()

    @pl.when(block + 1 < active)
    def _():
        for copy in loads(block + 1, 1 - slot):
            copy.start()

    @pl.when(block >= 2)
    def _():
        for copy in stores(block - 2, slot):
            copy.wait()

    @pl.when(block < active)
    def _():
        for copy in loads(block, slot):
            copy.wait()
        res[slot] = layers(buf[slot], first_ref[...], middle_ref[...], last_ref[...])

    @pl.when(block >= active)
    def _():
        res[slot] = jnp.zeros(res.shape[1:], res.dtype)

    for copy in stores(block, slot):
        copy.start()

    @pl.when(block == blocks - 1)
    def _():
        for copy in stores(block - 1, 1 - slot):
            copy.wait()
        for copy in stores(block, slot):
            copy.wait()


def network(rows_in, input_weight, middle_weight, output_weight):
    count, feats = rows_in.shape
    groups = count // HALF
    hid = input_weight.shape[1]
    first = input_weight[0].T
    middle = jnp.swapaxes(middle_weight[0], 1, 2)
    last = output_weight[0].T
    grouped = rows_in.reshape(groups, HALF, feats)
    nonzero = jnp.any(grouped != 0, axis=(1, 2)).astype(jnp.int32)
    used = jnp.sum(nonzero)
    ahead = jnp.cumsum(nonzero) - nonzero
    place = jnp.where(nonzero > 0, ahead, used + jnp.arange(groups, dtype=jnp.int32) - ahead)
    source = jnp.zeros((groups,), jnp.int32).at[place].set(jnp.arange(groups, dtype=jnp.int32))
    active = ((used * HALF + ROWS - 1) // ROWS).reshape(1)
    mats = 2 * (hid * feats * 2 + middle_weight.shape[1] * hid * hid)
    per = ROWS // HALF
    return pl.pallas_call(
        network_kernel,
        grid_spec=pltpu.PrefetchScalarGridSpec(
            num_scalar_prefetch=2,
            grid=(count // ROWS,),
            in_specs=[
                pl.BlockSpec(memory_space=pl.ANY),
                pl.BlockSpec(first.shape, lambda i, a, s: (0, 0)),
                pl.BlockSpec(middle.shape, lambda i, a, s: (0, 0, 0)),
                pl.BlockSpec(last.shape, lambda i, a, s: (0, 0)),
            ],
            out_specs=pl.BlockSpec(memory_space=pl.ANY),
            scratch_shapes=[
                pltpu.VMEM((2, ROWS, feats), jnp.bfloat16),
                pltpu.VMEM((2, ROWS, feats), jnp.bfloat16),
                pltpu.SemaphoreType.DMA((2, per)),
                pltpu.SemaphoreType.DMA((2, per)),
            ],
        ),
        out_shape=jax.ShapeDtypeStruct((count, feats), jnp.bfloat16),
        cost_estimate=pl.CostEstimate(
            flops=mats * count,
            bytes_accessed=4 * count * feats + 2 * (mats // 2),
            transcendentals=(1 + middle_weight.shape[1]) * hid * count,
        ),
    )(active, source, rows_in, first, middle, last)


UNROLL = 32


def pack_kernel(t_ref, cur_ref, o_ref, rows, full):
    feats, lat_cells, lon_cells = cur_ref.shape
    for r in range(lat_cells):
        rows[r * lon_cells:(r + 1) * lon_cells, :] = cur_ref[:, r, :].T
    full[...] = jnp.zeros(full.shape, full.dtype)

    def body(i, carry):
        for u in range(UNROLL):
            c = i * UNROLL + u
            full[pl.ds(t_ref[c], 1), :] = rows[pl.ds(c, 1), :]
        return carry

    lax.fori_loop(0, rows.shape[0] // UNROLL, body, 0)
    o_ref[...] = full[...].astype(o_ref.dtype)


def pack(targets, current, slots):
    feats, lat_cells, lon_cells = current.shape
    count = lat_cells * lon_cells
    return pl.pallas_call(
        pack_kernel,
        grid_spec=pltpu.PrefetchScalarGridSpec(
            num_scalar_prefetch=1,
            grid=(1,),
            in_specs=[pl.BlockSpec(current.shape, lambda i, t: (0, 0, 0))],
            out_specs=pl.BlockSpec((slots, feats), lambda i, t: (0, 0)),
            scratch_shapes=[pltpu.VMEM((count, feats), jnp.float32), pltpu.VMEM((slots, feats), jnp.float32)],
        ),
        out_shape=jax.ShapeDtypeStruct((slots, feats), jnp.bfloat16),
    )(targets, current)


def combine_kernel(t_ref, ret_ref, cur_ref, o_ref, full, tend):
    feats, lat_cells, lon_cells = cur_ref.shape
    full[...] = ret_ref[...].astype(jnp.float32)

    def body(i, carry):
        for u in range(UNROLL):
            c = i * UNROLL + u
            tend[pl.ds(c, 1), :] = full[pl.ds(t_ref[c], 1), :]
        return carry

    lax.fori_loop(0, tend.shape[0] // UNROLL, body, 0)
    for r in range(lat_cells):
        o_ref[:, r, :] = cur_ref[:, r, :] + tend[r * lon_cells:(r + 1) * lon_cells, :].T


def combine(targets, returned_rows, current):
    feats, lat_cells, lon_cells = current.shape
    slots = returned_rows.shape[0]
    return pl.pallas_call(
        combine_kernel,
        grid_spec=pltpu.PrefetchScalarGridSpec(
            num_scalar_prefetch=1,
            grid=(1,),
            in_specs=[
                pl.BlockSpec((slots, feats), lambda i, t: (0, 0)),
                pl.BlockSpec(current.shape, lambda i, t: (0, 0, 0)),
            ],
            out_specs=pl.BlockSpec(current.shape, lambda i, t: (0, 0, 0)),
            scratch_shapes=[
                pltpu.VMEM((slots, feats), jnp.float32),
                pltpu.VMEM((lat_cells * lon_cells, feats), jnp.float32),
            ],
        ),
        out_shape=jax.ShapeDtypeStruct(current.shape, jnp.float32),
    )(targets, returned_rows, current)


def local(
    column_state, wind_speed, diffusivity, batch_index, input_weight, middle_weight, output_weight
):
    num_vars, levels, lat_cells, lon_cells = column_state.shape
    features = num_vars * levels
    current = column_state.reshape(features, lat_cells, lon_cells)
    for sweep_index in range(2):
        current = step(current, wind_speed[0], wind_speed[1], diffusivity)
    column_count = lat_cells * lon_cells
    experts = lax.axis_size("lon")
    capacity = 2 * column_count // experts
    targets_all = batch_index.reshape(column_count)
    position = positions(targets_all, experts)
    targets = targets_all * capacity + position
    packed = pack(targets, current, experts * capacity).T.reshape(features, experts, capacity)
    chunks = 1
    width = capacity // chunks
    answers = []
    for chunk in range(chunks):
        part = packed[:, :, chunk * width:(chunk + 1) * width]
        received = lax.all_to_all(part, "lon", split_axis=1, concat_axis=1, tiled=True)
        rows_in = received.reshape(features, experts * width).T
        result = network(rows_in, input_weight, middle_weight, output_weight).T
        answers.append(
            lax.all_to_all(result.reshape(features, experts, width), "lon", split_axis=1, concat_axis=1, tiled=True)
        )
    returned = jnp.concatenate(answers, axis=2)
    return combine(targets, returned.reshape(features, -1).T, current).reshape(column_state.shape)


def solution(mesh):
    in_specs = (
        P(None, None, "lat", "lon"),
        P(None, None, "lat", "lon"),
        P(None, "lat", "lon"),
        P("lat", "lon", None),
        P("lon", None, None),
        P("lon", None, None, None),
        P("lon", None, None),
    )
    out_specs = P(None, None, "lat", "lon")
    return jax.shard_map(local, mesh=mesh, in_specs=in_specs, out_specs=out_specs, check_vma=False)
```

```python
import jax
import jax.numpy as jnp
from jax import lax
from jax.experimental import pallas as pl
from jax.experimental.pallas import tpu as pltpu
from jax.sharding import PartitionSpec as P


def neighbours(axis, periodic):
    count = lax.axis_size(axis)
    forward = [(i, i + 1) for i in range(count - 1)]
    if periodic:
        forward.append((count - 1, 0))
    backward = [(target, source) for source, target in forward]
    return forward, backward


FB = 32


def keep_edges(block_ref, top_ref, bottom_ref, ends_ref):
    feats, rows, cols = block_ref.shape
    for f in range(feats):
        top_ref[f] = block_ref[f, 0:1, :]
        bottom_ref[f] = block_ref[f, rows - 1:rows, :]
    lane = lax.broadcasted_iota(jnp.int32, (2, cols), 1)
    which = lax.broadcasted_iota(jnp.int32, (2, cols), 0)
    pick = (lane == which * (cols - 1)).astype(jnp.float32)
    ends_ref[...] = lax.dot_general(
        pick, block_ref[...].reshape(feats * rows, cols), (((1,), (1,)), ((), ())),
        precision=lax.Precision.HIGHEST, preferred_element_type=jnp.float32,
    )


def edges_kernel(q_ref, top_ref, bottom_ref, ends_ref):
    keep_edges(q_ref, top_ref, bottom_ref, ends_ref)


def sweep_kernel(q_ref, hn_ref, hs_ref, he_ref, hw_ref, u_ref, v_ref, k_ref, o_ref, top_ref, bottom_ref, ends_ref):
    rows, cols = q_ref.shape[1], q_ref.shape[2]
    row = lax.broadcasted_iota(jnp.int32, (rows, cols), 0)
    lane = lax.broadcasted_iota(jnp.int32, (rows, cols), 1)
    he = he_ref[0]
    hw = hw_ref[0]
    for f in range(FB):
        q = q_ref[f]
        north = jnp.where(row == rows - 1, jnp.broadcast_to(hn_ref[f], (rows, cols)), pltpu.roll(q, rows - 1, 0))
        south = jnp.where(row == 0, jnp.broadcast_to(hs_ref[f], (rows, cols)), pltpu.roll(q, 1, 0))
        east = jnp.where(lane == cols - 1, jnp.broadcast_to(he[:, f:f + 1], (rows, cols)), pltpu.roll(q, cols - 1, 1))
        west = jnp.where(lane == 0, jnp.broadcast_to(hw[:, f:f + 1], (rows, cols)), pltpu.roll(q, 1, 1))
        u = u_ref[f]
        v = v_ref[f]
        k = k_ref[f]
        o_ref[f] = (q - 0.5 * u * (east - west) - 0.5 * v * (north - south)
                    + k * (east + west + north + south - 4.0 * q))
    keep_edges(o_ref, top_ref, bottom_ref, ends_ref)


def edge_specs(feats, rows, cols):
    edge_row = pl.BlockSpec((FB, 1, cols), lambda i: (i, 0, 0))
    ends = pl.BlockSpec((2, FB * rows), lambda i: (0, i))
    shapes = [
        jax.ShapeDtypeStruct((feats, 1, cols), jnp.float32),
        jax.ShapeDtypeStruct((feats, 1, cols), jnp.float32),
        jax.ShapeDtypeStruct((2, feats * rows), jnp.float32),
    ]
    return [edge_row, edge_row, ends], shapes


def edges(q):
    feats, rows, cols = q.shape
    specs, shapes = edge_specs(feats, rows, cols)
    return pl.pallas_call(
        edges_kernel,
        grid=(feats // FB,),
        in_specs=[pl.BlockSpec((FB, rows, cols), lambda i: (i, 0, 0))],
        out_specs=specs,
        out_shape=shapes,
    )(q)


def sweep(q, halos, u, v, k):
    feats, rows, cols = q.shape
    levels = u.shape[0]
    nb = feats // FB
    per = levels // FB
    big = pl.BlockSpec((FB, rows, cols), lambda i: (i, 0, 0))
    field = pl.BlockSpec((FB, rows, cols), lambda i: (i % per, 0, 0))
    edge_row = pl.BlockSpec((FB, 1, cols), lambda i: (i, 0, 0))
    edge_col = pl.BlockSpec((1, rows, FB), lambda i: (i, 0, 0))
    specs, shapes = edge_specs(feats, rows, cols)
    return pl.pallas_call(
        sweep_kernel,
        grid=(nb,),
        in_specs=[big, edge_row, edge_row, edge_col, edge_col, field, field, field],
        out_specs=[big] + specs,
        out_shape=[jax.ShapeDtypeStruct(q.shape, q.dtype)] + shapes,
        cost_estimate=pl.CostEstimate(flops=20 * q.size, bytes_accessed=8 * q.size + 12 * u.size, transcendentals=0),
    )(q, *halos, u, v, k)


def columns_of(edge):
    feats, rows = edge.shape
    return jnp.swapaxes(edge.reshape(feats // FB, FB, rows), 1, 2)


def exchange(top, bottom, ends, feats, rows):
    lat_forward, lat_backward = neighbours("lat", False)
    lon_forward, lon_backward = neighbours("lon", True)
    hn = lax.ppermute(top, "lat", lat_backward)
    hs = lax.ppermute(bottom, "lat", lat_forward)
    he = lax.ppermute(columns_of(ends[0].reshape(feats, rows)), "lon", lon_backward)
    hw = lax.ppermute(columns_of(ends[1].reshape(feats, rows)), "lon", lon_forward)
    return hn, hs, he, hw


def positions(targets_all, experts):
    count = targets_all.shape[0]
    block = 128
    onehot = (targets_all[:, None] == jnp.arange(experts, dtype=jnp.int32)[None, :]).astype(
        jnp.bfloat16
    )
    blocks = onehot.reshape(count // block, block, experts)
    rows = jnp.arange(block, dtype=jnp.int32)
    before = (rows[:, None] > rows[None, :]).astype(jnp.bfloat16)
    within = jnp.einsum("ij,bje->bie", before, blocks, preferred_element_type=jnp.float32)
    totals = jnp.sum(blocks.astype(jnp.float32), axis=1)
    offsets = jnp.cumsum(totals, axis=0) - totals
    ranks = within + offsets[:, None, :]
    position = jnp.sum(ranks * blocks.astype(jnp.float32), axis=2)
    return position.reshape(count).astype(jnp.int32)


ROWS = 1024
HALF = 128


def silu(t):
    return t * (0.5 * jnp.tanh(0.5 * t) + 0.5)


def layers(x, w_first, w_middle, w_last):
    hidden = silu(jnp.dot(x, w_first, preferred_element_type=jnp.float32)).astype(jnp.bfloat16)
    for layer_index in range(w_middle.shape[0]):
        hidden = silu(
            jnp.dot(hidden, w_middle[layer_index], preferred_element_type=jnp.float32)
        ).astype(jnp.bfloat16)
    return jnp.dot(hidden, w_last, preferred_element_type=jnp.float32).astype(jnp.bfloat16)


def network_kernel(active_ref, source_ref, x_hbm, first_ref, middle_ref, last_ref, o_hbm, buf, res, lsem, ssem):
    block = pl.program_id(0)
    blocks = pl.num_programs(0)
    active = active_ref[0]
    slot = block % 2
    per = ROWS // HALF

    def loads(index, into):
        return [
            pltpu.make_async_copy(
                x_hbm.at[pl.ds(source_ref[index * per + j] * HALF, HALF)],
                buf.at[into, pl.ds(j * HALF, HALF)],
                lsem.at[into, j],
            )
            for j in range(per)
        ]

    def stores(index, outof):
        return [
            pltpu.make_async_copy(
                res.at[outof, pl.ds(j * HALF, HALF)],
                o_hbm.at[pl.ds(source_ref[index * per + j] * HALF, HALF)],
                ssem.at[outof, j],
            )
            for j in range(per)
        ]

    @pl.when((block == 0) & (active > 0))
    def _():
        for copy in loads(0, 0):
            copy.start()

    @pl.when(block + 1 < active)
    def _():
        for copy in loads(block + 1, 1 - slot):
            copy.start()

    @pl.when(block >= 2)
    def _():
        for copy in stores(block - 2, slot):
            copy.wait()

    @pl.when(block < active)
    def _():
        for copy in loads(block, slot):
            copy.wait()
        res[slot] = layers(buf[slot], first_ref[...], middle_ref[...], last_ref[...])

    @pl.when(block >= active)
    def _():
        res[slot] = jnp.zeros(res.shape[1:], res.dtype)

    for copy in stores(block, slot):
        copy.start()

    @pl.when(block == blocks - 1)
    def _():
        for copy in stores(block - 1, 1 - slot):
            copy.wait()
        for copy in stores(block, slot):
            copy.wait()


def network(rows_in, input_weight, middle_weight, output_weight):
    count, feats = rows_in.shape
    groups = count // HALF
    hid = input_weight.shape[1]
    first = input_weight[0].T
    middle = jnp.swapaxes(middle_weight[0], 1, 2)
    last = output_weight[0].T
    grouped = rows_in.reshape(groups, HALF, feats)
    nonzero = jnp.any(grouped != 0, axis=(1, 2)).astype(jnp.int32)
    used = jnp.sum(nonzero)
    ahead = jnp.cumsum(nonzero) - nonzero
    place = jnp.where(nonzero > 0, ahead, used + jnp.arange(groups, dtype=jnp.int32) - ahead)
    source = jnp.zeros((groups,), jnp.int32).at[place].set(jnp.arange(groups, dtype=jnp.int32))
    active = ((used * HALF + ROWS - 1) // ROWS).reshape(1)
    mats = 2 * (hid * feats * 2 + middle_weight.shape[1] * hid * hid)
    per = ROWS // HALF
    return pl.pallas_call(
        network_kernel,
        grid_spec=pltpu.PrefetchScalarGridSpec(
            num_scalar_prefetch=2,
            grid=(count // ROWS,),
            in_specs=[
                pl.BlockSpec(memory_space=pl.ANY),
                pl.BlockSpec(first.shape, lambda i, a, s: (0, 0)),
                pl.BlockSpec(middle.shape, lambda i, a, s: (0, 0, 0)),
                pl.BlockSpec(last.shape, lambda i, a, s: (0, 0)),
            ],
            out_specs=pl.BlockSpec(memory_space=pl.ANY),
            scratch_shapes=[
                pltpu.VMEM((2, ROWS, feats), jnp.bfloat16),
                pltpu.VMEM((2, ROWS, feats), jnp.bfloat16),
                pltpu.SemaphoreType.DMA((2, per)),
                pltpu.SemaphoreType.DMA((2, per)),
            ],
        ),
        out_shape=jax.ShapeDtypeStruct((count, feats), jnp.bfloat16),
        cost_estimate=pl.CostEstimate(
            flops=mats * count,
            bytes_accessed=4 * count * feats + 2 * (mats // 2),
            transcendentals=(1 + middle_weight.shape[1]) * hid * count,
        ),
    )(active, source, rows_in, first, middle, last)


UNROLL = 32


def pack_kernel(t_ref, cur_ref, o_ref, rows, full):
    feats, lat_cells, lon_cells = cur_ref.shape
    for r in range(lat_cells):
        rows[r * lon_cells:(r + 1) * lon_cells, :] = cur_ref[:, r, :].T
    full[...] = jnp.zeros(full.shape, full.dtype)

    def body(i, carry):
        for u in range(UNROLL):
            c = i * UNROLL + u
            full[pl.ds(t_ref[c], 1), :] = rows[pl.ds(c, 1), :]
        return carry

    lax.fori_loop(0, rows.shape[0] // UNROLL, body, 0)
    o_ref[...] = full[...].astype(o_ref.dtype)


def pack(targets, current, slots):
    feats, lat_cells, lon_cells = current.shape
    count = lat_cells * lon_cells
    return pl.pallas_call(
        pack_kernel,
        grid_spec=pltpu.PrefetchScalarGridSpec(
            num_scalar_prefetch=1,
            grid=(1,),
            in_specs=[pl.BlockSpec(current.shape, lambda i, t: (0, 0, 0))],
            out_specs=pl.BlockSpec((slots, feats), lambda i, t: (0, 0)),
            scratch_shapes=[pltpu.VMEM((count, feats), jnp.float32), pltpu.VMEM((slots, feats), jnp.float32)],
        ),
        out_shape=jax.ShapeDtypeStruct((slots, feats), jnp.bfloat16),
    )(targets, current)


def combine_kernel(t_ref, ret_ref, cur_ref, o_ref, full, tend):
    feats, lat_cells, lon_cells = cur_ref.shape
    full[...] = ret_ref[...].astype(jnp.float32)

    def body(i, carry):
        for u in range(UNROLL):
            c = i * UNROLL + u
            tend[pl.ds(c, 1), :] = full[pl.ds(t_ref[c], 1), :]
        return carry

    lax.fori_loop(0, tend.shape[0] // UNROLL, body, 0)
    for r in range(lat_cells):
        o_ref[:, r, :] = cur_ref[:, r, :] + tend[r * lon_cells:(r + 1) * lon_cells, :].T


def combine(targets, returned_rows, current):
    feats, lat_cells, lon_cells = current.shape
    slots = returned_rows.shape[0]
    return pl.pallas_call(
        combine_kernel,
        grid_spec=pltpu.PrefetchScalarGridSpec(
            num_scalar_prefetch=1,
            grid=(1,),
            in_specs=[
                pl.BlockSpec((slots, feats), lambda i, t: (0, 0)),
                pl.BlockSpec(current.shape, lambda i, t: (0, 0, 0)),
            ],
            out_specs=pl.BlockSpec(current.shape, lambda i, t: (0, 0, 0)),
            scratch_shapes=[
                pltpu.VMEM((slots, feats), jnp.float32),
                pltpu.VMEM((lat_cells * lon_cells, feats), jnp.float32),
            ],
        ),
        out_shape=jax.ShapeDtypeStruct(current.shape, jnp.float32),
    )(targets, returned_rows, current)


def local(
    column_state, wind_speed, diffusivity, batch_index, input_weight, middle_weight, output_weight
):
    num_vars, levels, lat_cells, lon_cells = column_state.shape
    features = num_vars * levels
    current = column_state.reshape(features, lat_cells, lon_cells)
    sides = edges(current)
    for sweep_index in range(2):
        halos = exchange(*sides, features, lat_cells)
        current, *sides = sweep(current, halos, wind_speed[0], wind_speed[1], diffusivity)
    column_count = lat_cells * lon_cells
    experts = lax.axis_size("lon")
    capacity = 2 * column_count // experts
    targets_all = batch_index.reshape(column_count)
    position = positions(targets_all, experts)
    targets = targets_all * capacity + position
    packed = pack(targets, current, experts * capacity).T.reshape(features, experts, capacity)
    chunks = 1
    width = capacity // chunks
    answers = []
    for chunk in range(chunks):
        part = packed[:, :, chunk * width:(chunk + 1) * width]
        received = lax.all_to_all(part, "lon", split_axis=1, concat_axis=1, tiled=True)
        rows_in = received.reshape(features, experts * width).T
        result = network(rows_in, input_weight, middle_weight, output_weight).T
        answers.append(
            lax.all_to_all(result.reshape(features, experts, width), "lon", split_axis=1, concat_axis=1, tiled=True)
        )
    returned = jnp.concatenate(answers, axis=2)
    return combine(targets, returned.reshape(features, -1).T, current).reshape(column_state.shape)


def solution(mesh):
    in_specs = (
        P(None, None, "lat", "lon"),
        P(None, None, "lat", "lon"),
        P(None, "lat", "lon"),
        P("lat", "lon", None),
        P("lon", None, None),
        P("lon", None, None, None),
        P("lon", None, None),
    )
    out_specs = P(None, None, "lat", "lon")
    return jax.shard_map(local, mesh=mesh, in_specs=in_specs, out_specs=out_specs, check_vma=False)
```

```python
import jax
import jax.numpy as jnp
from jax import lax
from jax.experimental import pallas as pl
from jax.experimental.pallas import tpu as pltpu
from jax.sharding import PartitionSpec as P


def neighbours(axis, periodic):
    count = lax.axis_size(axis)
    forward = [(i, i + 1) for i in range(count - 1)]
    if periodic:
        forward.append((count - 1, 0))
    backward = [(target, source) for source, target in forward]
    return forward, backward


FB = 32

def sweep_kernel(q_ref, hn_ref, hs_ref, he_ref, hw_ref, u_ref, v_ref, k_ref, o_ref):
    rows, cols = q_ref.shape[1], q_ref.shape[2]
    row = lax.broadcasted_iota(jnp.int32, (rows, cols), 0)
    lane = lax.broadcasted_iota(jnp.int32, (rows, cols), 1)
    he = he_ref[0]
    hw = hw_ref[0]
    for f in range(FB):
        q = q_ref[f]
        north = jnp.where(row == rows - 1, jnp.broadcast_to(hn_ref[f], (rows, cols)), pltpu.roll(q, rows - 1, 0))
        south = jnp.where(row == 0, jnp.broadcast_to(hs_ref[f], (rows, cols)), pltpu.roll(q, 1, 0))
        east = jnp.where(lane == cols - 1, jnp.broadcast_to(he[:, f:f + 1], (rows, cols)), pltpu.roll(q, cols - 1, 1))
        west = jnp.where(lane == 0, jnp.broadcast_to(hw[:, f:f + 1], (rows, cols)), pltpu.roll(q, 1, 1))
        u = u_ref[f]
        v = v_ref[f]
        k = k_ref[f]
        o_ref[f] = (q - 0.5 * u * (east - west) - 0.5 * v * (north - south)
                    + k * (east + west + north + south - 4.0 * q))


def sweep(q, hn, hs, he, hw, u, v, k):
    feats, rows, cols = q.shape
    levels = u.shape[0]
    nb = feats // FB
    per = levels // FB
    big = pl.BlockSpec((FB, rows, cols), lambda i: (i, 0, 0))
    field = pl.BlockSpec((FB, rows, cols), lambda i: (i % per, 0, 0))
    edge_row = pl.BlockSpec((FB, 1, cols), lambda i: (i, 0, 0))
    edge_col = pl.BlockSpec((1, rows, FB), lambda i: (i, 0, 0))
    return pl.pallas_call(
        sweep_kernel,
        grid=(nb,),
        in_specs=[big, edge_row, edge_row, edge_col, edge_col, field, field, field],
        out_specs=big,
        out_shape=jax.ShapeDtypeStruct(q.shape, q.dtype),
        cost_estimate=pl.CostEstimate(flops=20 * q.size, bytes_accessed=8 * q.size + 12 * u.size, transcendentals=0),
    )(q, hn, hs, he, hw, u, v, k)


def columns_of(edge):
    feats, rows = edge.shape
    return jnp.swapaxes(edge.reshape(feats // FB, FB, rows), 1, 2)


def step(x, u, v, k):
    feats, rows, cols = x.shape
    lat_forward, lat_backward = neighbours("lat", False)
    lon_forward, lon_backward = neighbours("lon", True)
    hn = lax.ppermute(x[:, :1, :], "lat", lat_backward)
    hs = lax.ppermute(x[:, rows - 1:, :], "lat", lat_forward)
    lane = lax.broadcasted_iota(jnp.int32, (cols, 2), 0)
    which = lax.broadcasted_iota(jnp.int32, (cols, 2), 1)
    pick = (lane == which * (cols - 1)).astype(jnp.float32)
    ends = jnp.dot(x.reshape(feats * rows, cols), pick, precision=lax.Precision.HIGHEST)
    he = lax.ppermute(columns_of(ends[:, 0].reshape(feats, rows)), "lon", lon_backward)
    hw = lax.ppermute(columns_of(ends[:, 1].reshape(feats, rows)), "lon", lon_forward)
    return sweep(x, hn, hs, he, hw, u, v, k)


def positions(targets_all, experts):
    count = targets_all.shape[0]
    block = 128
    onehot = (targets_all[:, None] == jnp.arange(experts, dtype=jnp.int32)[None, :]).astype(
        jnp.bfloat16
    )
    blocks = onehot.reshape(count // block, block, experts)
    rows = jnp.arange(block, dtype=jnp.int32)
    before = (rows[:, None] > rows[None, :]).astype(jnp.bfloat16)
    within = jnp.einsum("ij,bje->bie", before, blocks, preferred_element_type=jnp.float32)
    totals = jnp.sum(blocks.astype(jnp.float32), axis=1)
    offsets = jnp.cumsum(totals, axis=0) - totals
    ranks = within + offsets[:, None, :]
    position = jnp.sum(ranks * blocks.astype(jnp.float32), axis=2)
    return position.reshape(count).astype(jnp.int32)


ROWS = 1024
HALF = 128


def silu(t):
    return t * (0.5 * jnp.tanh(0.5 * t) + 0.5)


def layers(x, w_first, w_middle, w_last):
    hidden = silu(jnp.dot(x, w_first, preferred_element_type=jnp.float32)).astype(jnp.bfloat16)
    for layer_index in range(w_middle.shape[0]):
        hidden = silu(
            jnp.dot(hidden, w_middle[layer_index], preferred_element_type=jnp.float32)
        ).astype(jnp.bfloat16)
    return jnp.dot(hidden, w_last, preferred_element_type=jnp.float32).astype(jnp.bfloat16)


def network_kernel(nonzero_ref, x_hbm, first_ref, middle_ref, last_ref, o_hbm, buf, res, lsem, ssem, source_ref, used_ref):
    block = pl.program_id(0)
    blocks = pl.num_programs(0)
    per = ROWS // HALF
    groups = source_ref.shape[0]

    @pl.when(block == 0)
    def _():
        def nonempty(g, used):
            @pl.when(nonzero_ref[g] > 0)
            def _():
                source_ref[used] = g

            return used + nonzero_ref[g]

        used = lax.fori_loop(0, groups, nonempty, 0)
        used_ref[0] = used

        def empty(g, at):
            @pl.when(nonzero_ref[g] == 0)
            def _():
                source_ref[at] = g

            return at + 1 - nonzero_ref[g]

        lax.fori_loop(0, groups, empty, used)

    active = (used_ref[0] * HALF + ROWS - 1) // ROWS
    slot = block % 2

    def loads(index, into):
        return [
            pltpu.make_async_copy(
                x_hbm.at[pl.ds(source_ref[index * per + j] * HALF, HALF)],
                buf.at[into, pl.ds(j * HALF, HALF)],
                lsem.at[into, j],
            )
            for j in range(per)
        ]

    def stores(index, outof):
        return [
            pltpu.make_async_copy(
                res.at[outof, pl.ds(j * HALF, HALF)],
                o_hbm.at[pl.ds(source_ref[index * per + j] * HALF, HALF)],
                ssem.at[outof, j],
            )
            for j in range(per)
        ]

    @pl.when((block == 0) & (active > 0))
    def _():
        for copy in loads(0, 0):
            copy.start()

    @pl.when(block + 1 < active)
    def _():
        for copy in loads(block + 1, 1 - slot):
            copy.start()

    @pl.when(block >= 2)
    def _():
        for copy in stores(block - 2, slot):
            copy.wait()

    @pl.when(block < active)
    def _():
        for copy in loads(block, slot):
            copy.wait()
        res[slot] = layers(buf[slot], first_ref[...], middle_ref[...], last_ref[...])

    @pl.when(block >= active)
    def _():
        res[slot] = jnp.zeros(res.shape[1:], res.dtype)

    for copy in stores(block, slot):
        copy.start()

    @pl.when(block == blocks - 1)
    def _():
        for copy in stores(block - 1, 1 - slot):
            copy.wait()
        for copy in stores(block, slot):
            copy.wait()


def network(rows_in, input_weight, middle_weight, output_weight):
    count, feats = rows_in.shape
    groups = count // HALF
    hid = input_weight.shape[1]
    first = input_weight[0].T
    middle = jnp.swapaxes(middle_weight[0], 1, 2)
    last = output_weight[0].T
    grouped = rows_in.reshape(groups, HALF, feats)
    nonzero = jnp.any(grouped != 0, axis=(1, 2)).astype(jnp.int32)
    mats = 2 * (hid * feats * 2 + middle_weight.shape[1] * hid * hid)
    per = ROWS // HALF
    return pl.pallas_call(
        network_kernel,
        grid_spec=pltpu.PrefetchScalarGridSpec(
            num_scalar_prefetch=1,
            grid=(count // ROWS,),
            in_specs=[
                pl.BlockSpec(memory_space=pl.ANY),
                pl.BlockSpec(first.shape, lambda i, n: (0, 0)),
                pl.BlockSpec(middle.shape, lambda i, n: (0, 0, 0)),
                pl.BlockSpec(last.shape, lambda i, n: (0, 0)),
            ],
            out_specs=pl.BlockSpec(memory_space=pl.ANY),
            scratch_shapes=[
                pltpu.VMEM((2, ROWS, feats), jnp.bfloat16),
                pltpu.VMEM((2, ROWS, feats), jnp.bfloat16),
                pltpu.SemaphoreType.DMA((2, per)),
                pltpu.SemaphoreType.DMA((2, per)),
                pltpu.SMEM((groups,), jnp.int32),
                pltpu.SMEM((1,), jnp.int32),
            ],
        ),
        out_shape=jax.ShapeDtypeStruct((count, feats), jnp.bfloat16),
        cost_estimate=pl.CostEstimate(
            flops=mats * count,
            bytes_accessed=4 * count * feats + 2 * (mats // 2),
            transcendentals=(1 + middle_weight.shape[1]) * hid * count,
        ),
    )(nonzero, rows_in, first, middle, last)


UNROLL = 32


def pack_kernel(t_ref, cur_ref, o_ref, rows, full):
    feats, lat_cells, lon_cells = cur_ref.shape
    for r in range(lat_cells):
        rows[r * lon_cells:(r + 1) * lon_cells, :] = cur_ref[:, r, :].T
    full[...] = jnp.zeros(full.shape, full.dtype)

    def body(i, carry):
        for u in range(UNROLL):
            c = i * UNROLL + u
            full[pl.ds(t_ref[c], 1), :] = rows[pl.ds(c, 1), :]
        return carry

    lax.fori_loop(0, rows.shape[0] // UNROLL, body, 0)
    o_ref[...] = full[...].astype(o_ref.dtype)


def pack(targets, current, slots):
    feats, lat_cells, lon_cells = current.shape
    count = lat_cells * lon_cells
    return pl.pallas_call(
        pack_kernel,
        grid_spec=pltpu.PrefetchScalarGridSpec(
            num_scalar_prefetch=1,
            grid=(1,),
            in_specs=[pl.BlockSpec(current.shape, lambda i, t: (0, 0, 0))],
            out_specs=pl.BlockSpec((slots, feats), lambda i, t: (0, 0)),
            scratch_shapes=[pltpu.VMEM((count, feats), jnp.float32), pltpu.VMEM((slots, feats), jnp.float32)],
        ),
        out_shape=jax.ShapeDtypeStruct((slots, feats), jnp.bfloat16),
    )(targets, current)


def combine_kernel(t_ref, ret_ref, cur_ref, o_ref, full, tend):
    feats, lat_cells, lon_cells = cur_ref.shape
    full[...] = ret_ref[...].astype(jnp.float32)

    def body(i, carry):
        for u in range(UNROLL):
            c = i * UNROLL + u
            tend[pl.ds(c, 1), :] = full[pl.ds(t_ref[c], 1), :]
        return carry

    lax.fori_loop(0, tend.shape[0] // UNROLL, body, 0)
    for r in range(lat_cells):
        o_ref[:, r, :] = cur_ref[:, r, :] + tend[r * lon_cells:(r + 1) * lon_cells, :].T


def combine(targets, returned_rows, current):
    feats, lat_cells, lon_cells = current.shape
    slots = returned_rows.shape[0]
    return pl.pallas_call(
        combine_kernel,
        grid_spec=pltpu.PrefetchScalarGridSpec(
            num_scalar_prefetch=1,
            grid=(1,),
            in_specs=[
                pl.BlockSpec((slots, feats), lambda i, t: (0, 0)),
                pl.BlockSpec(current.shape, lambda i, t: (0, 0, 0)),
            ],
            out_specs=pl.BlockSpec(current.shape, lambda i, t: (0, 0, 0)),
            scratch_shapes=[
                pltpu.VMEM((slots, feats), jnp.float32),
                pltpu.VMEM((lat_cells * lon_cells, feats), jnp.float32),
            ],
        ),
        out_shape=jax.ShapeDtypeStruct(current.shape, jnp.float32),
    )(targets, returned_rows, current)


def local(
    column_state, wind_speed, diffusivity, batch_index, input_weight, middle_weight, output_weight
):
    num_vars, levels, lat_cells, lon_cells = column_state.shape
    features = num_vars * levels
    current = column_state.reshape(features, lat_cells, lon_cells)
    for sweep_index in range(2):
        current = step(current, wind_speed[0], wind_speed[1], diffusivity)
    column_count = lat_cells * lon_cells
    experts = lax.axis_size("lon")
    capacity = 2 * column_count // experts
    targets_all = batch_index.reshape(column_count)
    position = positions(targets_all, experts)
    targets = targets_all * capacity + position
    packed = pack(targets, current, experts * capacity).T.reshape(features, experts, capacity)
    chunks = 1
    width = capacity // chunks
    answers = []
    for chunk in range(chunks):
        part = packed[:, :, chunk * width:(chunk + 1) * width]
        received = lax.all_to_all(part, "lon", split_axis=1, concat_axis=1, tiled=True)
        rows_in = received.reshape(features, experts * width).T
        result = network(rows_in, input_weight, middle_weight, output_weight).T
        answers.append(
            lax.all_to_all(result.reshape(features, experts, width), "lon", split_axis=1, concat_axis=1, tiled=True)
        )
    returned = jnp.concatenate(answers, axis=2)
    return combine(targets, returned.reshape(features, -1).T, current).reshape(column_state.shape)


def solution(mesh):
    in_specs = (
        P(None, None, "lat", "lon"),
        P(None, None, "lat", "lon"),
        P(None, "lat", "lon"),
        P("lat", "lon", None),
        P("lon", None, None),
        P("lon", None, None, None),
        P("lon", None, None),
    )
    out_specs = P(None, None, "lat", "lon")
    return jax.shard_map(local, mesh=mesh, in_specs=in_specs, out_specs=out_specs, check_vma=False)
```

```python
import jax
import jax.numpy as jnp
from jax import lax
from jax.experimental import pallas as pl
from jax.experimental.pallas import tpu as pltpu
from jax.sharding import PartitionSpec as P


def neighbours(axis, periodic):
    count = lax.axis_size(axis)
    forward = [(i, i + 1) for i in range(count - 1)]
    if periodic:
        forward.append((count - 1, 0))
    backward = [(target, source) for source, target in forward]
    return forward, backward


FB = 32

def keep_edges(block_ref, top_ref, bottom_ref, ends_ref):
    feats, rows, cols = block_ref.shape
    for f in range(feats):
        top_ref[f] = block_ref[f, 0:1, :]
        bottom_ref[f] = block_ref[f, rows - 1:rows, :]
    lane = lax.broadcasted_iota(jnp.int32, (2, cols), 1)
    which = lax.broadcasted_iota(jnp.int32, (2, cols), 0)
    pick = (lane == which * (cols - 1)).astype(jnp.float32)
    ends_ref[...] = lax.dot_general(
        pick, block_ref[...].reshape(feats * rows, cols), (((1,), (1,)), ((), ())),
        precision=lax.Precision.HIGHEST, preferred_element_type=jnp.float32,
    )


def sweep_kernel(q_ref, hn_ref, hs_ref, he_ref, hw_ref, u_ref, v_ref, k_ref, o_ref, *edge_refs):
    rows, cols = q_ref.shape[1], q_ref.shape[2]
    row = lax.broadcasted_iota(jnp.int32, (rows, cols), 0)
    lane = lax.broadcasted_iota(jnp.int32, (rows, cols), 1)
    he = he_ref[0]
    hw = hw_ref[0]
    for f in range(FB):
        q = q_ref[f]
        north = jnp.where(row == rows - 1, jnp.broadcast_to(hn_ref[f], (rows, cols)), pltpu.roll(q, rows - 1, 0))
        south = jnp.where(row == 0, jnp.broadcast_to(hs_ref[f], (rows, cols)), pltpu.roll(q, 1, 0))
        east = jnp.where(lane == cols - 1, jnp.broadcast_to(he[:, f:f + 1], (rows, cols)), pltpu.roll(q, cols - 1, 1))
        west = jnp.where(lane == 0, jnp.broadcast_to(hw[:, f:f + 1], (rows, cols)), pltpu.roll(q, 1, 1))
        u = u_ref[f]
        v = v_ref[f]
        k = k_ref[f]
        o_ref[f] = (q - 0.5 * u * (east - west) - 0.5 * v * (north - south)
                    + k * (east + west + north + south - 4.0 * q))
    if edge_refs:
        keep_edges(o_ref, *edge_refs)


def sweep(q, halos, u, v, k, emit_edges):
    feats, rows, cols = q.shape
    levels = u.shape[0]
    nb = feats // FB
    per = levels // FB
    big = pl.BlockSpec((FB, rows, cols), lambda i: (i, 0, 0))
    field = pl.BlockSpec((FB, rows, cols), lambda i: (i % per, 0, 0))
    edge_row = pl.BlockSpec((FB, 1, cols), lambda i: (i, 0, 0))
    edge_col = pl.BlockSpec((1, rows, FB), lambda i: (i, 0, 0))
    out_specs, out_shape = [big], [jax.ShapeDtypeStruct(q.shape, q.dtype)]
    if emit_edges:
        out_specs += [edge_row, edge_row, pl.BlockSpec((2, FB * rows), lambda i: (0, i))]
        out_shape += [
            jax.ShapeDtypeStruct((feats, 1, cols), jnp.float32),
            jax.ShapeDtypeStruct((feats, 1, cols), jnp.float32),
            jax.ShapeDtypeStruct((2, feats * rows), jnp.float32),
        ]
    return pl.pallas_call(
        sweep_kernel,
        grid=(nb,),
        in_specs=[big, edge_row, edge_row, edge_col, edge_col, field, field, field],
        out_specs=out_specs,
        out_shape=out_shape,
        cost_estimate=pl.CostEstimate(flops=20 * q.size, bytes_accessed=8 * q.size + 12 * u.size, transcendentals=0),
    )(q, *halos, u, v, k)


def columns_of(edge):
    feats, rows = edge.shape
    return jnp.swapaxes(edge.reshape(feats // FB, FB, rows), 1, 2)


def exchange(top, bottom, ends, feats, rows):
    lat_forward, lat_backward = neighbours("lat", False)
    lon_forward, lon_backward = neighbours("lon", True)
    hn = lax.ppermute(top, "lat", lat_backward)
    hs = lax.ppermute(bottom, "lat", lat_forward)
    he = lax.ppermute(columns_of(ends[0].reshape(feats, rows)), "lon", lon_backward)
    hw = lax.ppermute(columns_of(ends[1].reshape(feats, rows)), "lon", lon_forward)
    return hn, hs, he, hw


def edges(x):
    feats, rows, cols = x.shape
    lane = lax.broadcasted_iota(jnp.int32, (cols, 2), 0)
    which = lax.broadcasted_iota(jnp.int32, (cols, 2), 1)
    pick = (lane == which * (cols - 1)).astype(jnp.float32)
    ends = jnp.dot(x.reshape(feats * rows, cols), pick, precision=lax.Precision.HIGHEST)
    return x[:, :1, :], x[:, rows - 1:, :], ends.T


def positions(targets_all, experts):
    count = targets_all.shape[0]
    block = 128
    onehot = (targets_all[:, None] == jnp.arange(experts, dtype=jnp.int32)[None, :]).astype(
        jnp.bfloat16
    )
    blocks = onehot.reshape(count // block, block, experts)
    rows = jnp.arange(block, dtype=jnp.int32)
    before = (rows[:, None] > rows[None, :]).astype(jnp.bfloat16)
    within = jnp.einsum("ij,bje->bie", before, blocks, preferred_element_type=jnp.float32)
    totals = jnp.sum(blocks.astype(jnp.float32), axis=1)
    offsets = jnp.cumsum(totals, axis=0) - totals
    ranks = within + offsets[:, None, :]
    position = jnp.sum(ranks * blocks.astype(jnp.float32), axis=2)
    return position.reshape(count).astype(jnp.int32)


ROWS = 1024
HALF = 128


def silu(t):
    return t * (0.5 * jnp.tanh(0.5 * t) + 0.5)


def layers(x, w_first, w_middle, w_last):
    hidden = silu(jnp.dot(x, w_first, preferred_element_type=jnp.float32)).astype(jnp.bfloat16)
    for layer_index in range(w_middle.shape[0]):
        hidden = silu(
            jnp.dot(hidden, w_middle[layer_index], preferred_element_type=jnp.float32)
        ).astype(jnp.bfloat16)
    return jnp.dot(hidden, w_last, preferred_element_type=jnp.float32).astype(jnp.bfloat16)


def network_kernel(nonzero_ref, x_hbm, first_ref, middle_ref, last_ref, o_hbm, buf, res, lsem, ssem, source_ref, used_ref):
    block = pl.program_id(0)
    blocks = pl.num_programs(0)
    per = ROWS // HALF
    groups = source_ref.shape[0]

    @pl.when(block == 0)
    def _():
        def nonempty(g, used):
            @pl.when(nonzero_ref[g] > 0)
            def _():
                source_ref[used] = g

            return used + nonzero_ref[g]

        used = lax.fori_loop(0, groups, nonempty, 0)
        used_ref[0] = used

        def empty(g, at):
            @pl.when(nonzero_ref[g] == 0)
            def _():
                source_ref[at] = g

            return at + 1 - nonzero_ref[g]

        lax.fori_loop(0, groups, empty, used)

    active = (used_ref[0] * HALF + ROWS - 1) // ROWS
    slot = block % 2

    def loads(index, into):
        return [
            pltpu.make_async_copy(
                x_hbm.at[pl.ds(source_ref[index * per + j] * HALF, HALF)],
                buf.at[into, pl.ds(j * HALF, HALF)],
                lsem.at[into, j],
            )
            for j in range(per)
        ]

    def stores(index, outof):
        return [
            pltpu.make_async_copy(
                res.at[outof, pl.ds(j * HALF, HALF)],
                o_hbm.at[pl.ds(source_ref[index * per + j] * HALF, HALF)],
                ssem.at[outof, j],
            )
            for j in range(per)
        ]

    @pl.when((block == 0) & (active > 0))
    def _():
        for copy in loads(0, 0):
            copy.start()

    @pl.when(block + 1 < active)
    def _():
        for copy in loads(block + 1, 1 - slot):
            copy.start()

    @pl.when(block >= 2)
    def _():
        for copy in stores(block - 2, slot):
            copy.wait()

    @pl.when(block < active)
    def _():
        for copy in loads(block, slot):
            copy.wait()
        res[slot] = layers(buf[slot], first_ref[...], middle_ref[...], last_ref[...])

    @pl.when(block >= active)
    def _():
        res[slot] = jnp.zeros(res.shape[1:], res.dtype)

    for copy in stores(block, slot):
        copy.start()

    @pl.when(block == blocks - 1)
    def _():
        for copy in stores(block - 1, 1 - slot):
            copy.wait()
        for copy in stores(block, slot):
            copy.wait()


def network(rows_in, input_weight, middle_weight, output_weight):
    count, feats = rows_in.shape
    groups = count // HALF
    hid = input_weight.shape[1]
    first = input_weight[0].T
    middle = jnp.swapaxes(middle_weight[0], 1, 2)
    last = output_weight[0].T
    grouped = rows_in.reshape(groups, HALF, feats)
    nonzero = jnp.any(grouped != 0, axis=(1, 2)).astype(jnp.int32)
    mats = 2 * (hid * feats * 2 + middle_weight.shape[1] * hid * hid)
    per = ROWS // HALF
    return pl.pallas_call(
        network_kernel,
        grid_spec=pltpu.PrefetchScalarGridSpec(
            num_scalar_prefetch=1,
            grid=(count // ROWS,),
            in_specs=[
                pl.BlockSpec(memory_space=pl.ANY),
                pl.BlockSpec(first.shape, lambda i, n: (0, 0)),
                pl.BlockSpec(middle.shape, lambda i, n: (0, 0, 0)),
                pl.BlockSpec(last.shape, lambda i, n: (0, 0)),
            ],
            out_specs=pl.BlockSpec(memory_space=pl.ANY),
            scratch_shapes=[
                pltpu.VMEM((2, ROWS, feats), jnp.bfloat16),
                pltpu.VMEM((2, ROWS, feats), jnp.bfloat16),
                pltpu.SemaphoreType.DMA((2, per)),
                pltpu.SemaphoreType.DMA((2, per)),
                pltpu.SMEM((groups,), jnp.int32),
                pltpu.SMEM((1,), jnp.int32),
            ],
        ),
        out_shape=jax.ShapeDtypeStruct((count, feats), jnp.bfloat16),
        cost_estimate=pl.CostEstimate(
            flops=mats * count,
            bytes_accessed=4 * count * feats + 2 * (mats // 2),
            transcendentals=(1 + middle_weight.shape[1]) * hid * count,
        ),
    )(nonzero, rows_in, first, middle, last)


UNROLL = 32


def pack_kernel(t_ref, cur_ref, o_ref, rows, full):
    feats, lat_cells, lon_cells = cur_ref.shape
    for r in range(lat_cells):
        rows[r * lon_cells:(r + 1) * lon_cells, :] = cur_ref[:, r, :].T
    full[...] = jnp.zeros(full.shape, full.dtype)

    def body(i, carry):
        for u in range(UNROLL):
            c = i * UNROLL + u
            full[pl.ds(t_ref[c], 1), :] = rows[pl.ds(c, 1), :]
        return carry

    lax.fori_loop(0, rows.shape[0] // UNROLL, body, 0)
    o_ref[...] = full[...].astype(o_ref.dtype)


def pack(targets, current, slots):
    feats, lat_cells, lon_cells = current.shape
    count = lat_cells * lon_cells
    return pl.pallas_call(
        pack_kernel,
        grid_spec=pltpu.PrefetchScalarGridSpec(
            num_scalar_prefetch=1,
            grid=(1,),
            in_specs=[pl.BlockSpec(current.shape, lambda i, t: (0, 0, 0))],
            out_specs=pl.BlockSpec((slots, feats), lambda i, t: (0, 0)),
            scratch_shapes=[pltpu.VMEM((count, feats), jnp.float32), pltpu.VMEM((slots, feats), jnp.float32)],
        ),
        out_shape=jax.ShapeDtypeStruct((slots, feats), jnp.bfloat16),
    )(targets, current)


def combine_kernel(t_ref, ret_ref, cur_ref, o_ref, full, tend):
    feats, lat_cells, lon_cells = cur_ref.shape
    full[...] = ret_ref[...].astype(jnp.float32)

    def body(i, carry):
        for u in range(UNROLL):
            c = i * UNROLL + u
            tend[pl.ds(c, 1), :] = full[pl.ds(t_ref[c], 1), :]
        return carry

    lax.fori_loop(0, tend.shape[0] // UNROLL, body, 0)
    for r in range(lat_cells):
        o_ref[:, r, :] = cur_ref[:, r, :] + tend[r * lon_cells:(r + 1) * lon_cells, :].T


def combine(targets, returned_rows, current):
    feats, lat_cells, lon_cells = current.shape
    slots = returned_rows.shape[0]
    return pl.pallas_call(
        combine_kernel,
        grid_spec=pltpu.PrefetchScalarGridSpec(
            num_scalar_prefetch=1,
            grid=(1,),
            in_specs=[
                pl.BlockSpec((slots, feats), lambda i, t: (0, 0)),
                pl.BlockSpec(current.shape, lambda i, t: (0, 0, 0)),
            ],
            out_specs=pl.BlockSpec(current.shape, lambda i, t: (0, 0, 0)),
            scratch_shapes=[
                pltpu.VMEM((slots, feats), jnp.float32),
                pltpu.VMEM((lat_cells * lon_cells, feats), jnp.float32),
            ],
        ),
        out_shape=jax.ShapeDtypeStruct(current.shape, jnp.float32),
    )(targets, returned_rows, current)


def local(
    column_state, wind_speed, diffusivity, batch_index, input_weight, middle_weight, output_weight
):
    num_vars, levels, lat_cells, lon_cells = column_state.shape
    features = num_vars * levels
    current = column_state.reshape(features, lat_cells, lon_cells)
    sides = edges(current)
    for sweep_index in range(2):
        halos = exchange(*sides, features, lat_cells)
        current, *sides = sweep(current, halos, wind_speed[0], wind_speed[1], diffusivity, sweep_index == 0)
    column_count = lat_cells * lon_cells
    experts = lax.axis_size("lon")
    capacity = 2 * column_count // experts
    targets_all = batch_index.reshape(column_count)
    position = positions(targets_all, experts)
    targets = targets_all * capacity + position
    packed = pack(targets, current, experts * capacity).T.reshape(features, experts, capacity)
    chunks = 1
    width = capacity // chunks
    answers = []
    for chunk in range(chunks):
        part = packed[:, :, chunk * width:(chunk + 1) * width]
        received = lax.all_to_all(part, "lon", split_axis=1, concat_axis=1, tiled=True)
        rows_in = received.reshape(features, experts * width).T
        result = network(rows_in, input_weight, middle_weight, output_weight).T
        answers.append(
            lax.all_to_all(result.reshape(features, experts, width), "lon", split_axis=1, concat_axis=1, tiled=True)
        )
    returned = jnp.concatenate(answers, axis=2)
    return combine(targets, returned.reshape(features, -1).T, current).reshape(column_state.shape)


def solution(mesh):
    in_specs = (
        P(None, None, "lat", "lon"),
        P(None, None, "lat", "lon"),
        P(None, "lat", "lon"),
        P("lat", "lon", None),
        P("lon", None, None),
        P("lon", None, None, None),
        P("lon", None, None),
    )
    out_specs = P(None, None, "lat", "lon")
    return jax.shard_map(local, mesh=mesh, in_specs=in_specs, out_specs=out_specs, check_vma=False)
```

```python
import jax
import jax.numpy as jnp
from jax import lax
from jax.experimental import pallas as pl
from jax.experimental.pallas import tpu as pltpu
from jax.sharding import PartitionSpec as P


def neighbours(axis, periodic):
    count = lax.axis_size(axis)
    forward = [(i, i + 1) for i in range(count - 1)]
    if periodic:
        forward.append((count - 1, 0))
    backward = [(target, source) for source, target in forward]
    return forward, backward


FB = 16

def keep_edges(block_ref, top_ref, bottom_ref, ends_ref):
    feats, rows, cols = block_ref.shape
    for f in range(feats):
        top_ref[f] = block_ref[f, 0:1, :]
        bottom_ref[f] = block_ref[f, rows - 1:rows, :]
    lane = lax.broadcasted_iota(jnp.int32, (2, cols), 1)
    which = lax.broadcasted_iota(jnp.int32, (2, cols), 0)
    pick = (lane == which * (cols - 1)).astype(jnp.float32)
    ends_ref[...] = lax.dot_general(
        pick, block_ref[...].reshape(feats * rows, cols), (((1,), (1,)), ((), ())),
        precision=lax.Precision.HIGHEST, preferred_element_type=jnp.float32,
    )


def sweep_kernel(q_ref, hn_ref, hs_ref, he_ref, hw_ref, u_ref, v_ref, k_ref, o_ref, *edge_refs):
    rows, cols = q_ref.shape[1], q_ref.shape[2]
    row = lax.broadcasted_iota(jnp.int32, (rows, cols), 0)
    lane = lax.broadcasted_iota(jnp.int32, (rows, cols), 1)
    he = he_ref[0]
    hw = hw_ref[0]
    for f in range(FB):
        q = q_ref[f]
        north = jnp.where(row == rows - 1, jnp.broadcast_to(hn_ref[f], (rows, cols)), pltpu.roll(q, rows - 1, 0))
        south = jnp.where(row == 0, jnp.broadcast_to(hs_ref[f], (rows, cols)), pltpu.roll(q, 1, 0))
        east = jnp.where(lane == cols - 1, jnp.broadcast_to(he[:, f:f + 1], (rows, cols)), pltpu.roll(q, cols - 1, 1))
        west = jnp.where(lane == 0, jnp.broadcast_to(hw[:, f:f + 1], (rows, cols)), pltpu.roll(q, 1, 1))
        u = u_ref[f]
        v = v_ref[f]
        k = k_ref[f]
        o_ref[f] = (q - 0.5 * u * (east - west) - 0.5 * v * (north - south)
                    + k * (east + west + north + south - 4.0 * q))
    if edge_refs:
        keep_edges(o_ref, *edge_refs)


def sweep(q, halos, u, v, k, emit_edges):
    feats, rows, cols = q.shape
    levels = u.shape[0]
    nb = feats // FB
    per = levels // FB
    big = pl.BlockSpec((FB, rows, cols), lambda i: (i, 0, 0))
    field = pl.BlockSpec((FB, rows, cols), lambda i: (i % per, 0, 0))
    edge_row = pl.BlockSpec((FB, 1, cols), lambda i: (i, 0, 0))
    edge_col = pl.BlockSpec((1, rows, FB), lambda i: (i, 0, 0))
    out_specs, out_shape = [big], [jax.ShapeDtypeStruct(q.shape, q.dtype)]
    if emit_edges:
        out_specs += [edge_row, edge_row, pl.BlockSpec((2, FB * rows), lambda i: (0, i))]
        out_shape += [
            jax.ShapeDtypeStruct((feats, 1, cols), jnp.float32),
            jax.ShapeDtypeStruct((feats, 1, cols), jnp.float32),
            jax.ShapeDtypeStruct((2, feats * rows), jnp.float32),
        ]
    return pl.pallas_call(
        sweep_kernel,
        grid=(nb,),
        in_specs=[big, edge_row, edge_row, edge_col, edge_col, field, field, field],
        out_specs=out_specs,
        out_shape=out_shape,
        cost_estimate=pl.CostEstimate(flops=20 * q.size, bytes_accessed=8 * q.size + 12 * u.size, transcendentals=0),
    )(q, *halos, u, v, k)


def columns_of(edge):
    feats, rows = edge.shape
    return jnp.swapaxes(edge.reshape(feats // FB, FB, rows), 1, 2)


def exchange(top, bottom, ends, feats, rows):
    lat_forward, lat_backward = neighbours("lat", False)
    lon_forward, lon_backward = neighbours("lon", True)
    hn = lax.ppermute(top, "lat", lat_backward)
    hs = lax.ppermute(bottom, "lat", lat_forward)
    he = lax.ppermute(columns_of(ends[0].reshape(feats, rows)), "lon", lon_backward)
    hw = lax.ppermute(columns_of(ends[1].reshape(feats, rows)), "lon", lon_forward)
    return hn, hs, he, hw


def edges(x):
    feats, rows, cols = x.shape
    lane = lax.broadcasted_iota(jnp.int32, (cols, 2), 0)
    which = lax.broadcasted_iota(jnp.int32, (cols, 2), 1)
    pick = (lane == which * (cols - 1)).astype(jnp.float32)
    ends = jnp.dot(x.reshape(feats * rows, cols), pick, precision=lax.Precision.HIGHEST)
    return x[:, :1, :], x[:, rows - 1:, :], ends.T


def positions(targets_all, experts):
    count = targets_all.shape[0]
    block = 128
    onehot = (targets_all[:, None] == jnp.arange(experts, dtype=jnp.int32)[None, :]).astype(
        jnp.bfloat16
    )
    blocks = onehot.reshape(count // block, block, experts)
    rows = jnp.arange(block, dtype=jnp.int32)
    before = (rows[:, None] > rows[None, :]).astype(jnp.bfloat16)
    within = jnp.einsum("ij,bje->bie", before, blocks, preferred_element_type=jnp.float32)
    totals = jnp.sum(blocks.astype(jnp.float32), axis=1)
    offsets = jnp.cumsum(totals, axis=0) - totals
    ranks = within + offsets[:, None, :]
    position = jnp.sum(ranks * blocks.astype(jnp.float32), axis=2)
    return position.reshape(count).astype(jnp.int32)


ROWS = 1024
HALF = 128


def silu(t):
    return t * (0.5 * jnp.tanh(0.5 * t) + 0.5)


def layers(x, w_first, w_middle, w_last):
    hidden = silu(jnp.dot(x, w_first, preferred_element_type=jnp.float32)).astype(jnp.bfloat16)
    for layer_index in range(w_middle.shape[0]):
        hidden = silu(
            jnp.dot(hidden, w_middle[layer_index], preferred_element_type=jnp.float32)
        ).astype(jnp.bfloat16)
    return jnp.dot(hidden, w_last, preferred_element_type=jnp.float32).astype(jnp.bfloat16)


def network_kernel(nonzero_ref, x_hbm, first_ref, middle_ref, last_ref, o_hbm, buf, res, lsem, ssem, source_ref, used_ref):
    block = pl.program_id(0)
    blocks = pl.num_programs(0)
    per = ROWS // HALF
    groups = source_ref.shape[0]

    @pl.when(block == 0)
    def _():
        def nonempty(g, used):
            @pl.when(nonzero_ref[g] > 0)
            def _():
                source_ref[used] = g

            return used + nonzero_ref[g]

        used = lax.fori_loop(0, groups, nonempty, 0)
        used_ref[0] = used

        def empty(g, at):
            @pl.when(nonzero_ref[g] == 0)
            def _():
                source_ref[at] = g

            return at + 1 - nonzero_ref[g]

        lax.fori_loop(0, groups, empty, used)

    active = (used_ref[0] * HALF + ROWS - 1) // ROWS
    slot = block % 2

    def loads(index, into):
        return [
            pltpu.make_async_copy(
                x_hbm.at[pl.ds(source_ref[index * per + j] * HALF, HALF)],
                buf.at[into, pl.ds(j * HALF, HALF)],
                lsem.at[into, j],
            )
            for j in range(per)
        ]

    def stores(index, outof):
        return [
            pltpu.make_async_copy(
                res.at[outof, pl.ds(j * HALF, HALF)],
                o_hbm.at[pl.ds(source_ref[index * per + j] * HALF, HALF)],
                ssem.at[outof, j],
            )
            for j in range(per)
        ]

    @pl.when((block == 0) & (active > 0))
    def _():
        for copy in loads(0, 0):
            copy.start()

    @pl.when(block + 1 < active)
    def _():
        for copy in loads(block + 1, 1 - slot):
            copy.start()

    @pl.when(block >= 2)
    def _():
        for copy in stores(block - 2, slot):
            copy.wait()

    @pl.when(block < active)
    def _():
        for copy in loads(block, slot):
            copy.wait()
        res[slot] = layers(buf[slot], first_ref[...], middle_ref[...], last_ref[...])

    @pl.when(block >= active)
    def _():
        res[slot] = jnp.zeros(res.shape[1:], res.dtype)

    for copy in stores(block, slot):
        copy.start()

    @pl.when(block == blocks - 1)
    def _():
        for copy in stores(block - 1, 1 - slot):
            copy.wait()
        for copy in stores(block, slot):
            copy.wait()


def network(rows_in, input_weight, middle_weight, output_weight):
    count, feats = rows_in.shape
    groups = count // HALF
    hid = input_weight.shape[1]
    first = input_weight[0].T
    middle = jnp.swapaxes(middle_weight[0], 1, 2)
    last = output_weight[0].T
    grouped = rows_in.reshape(groups, HALF, feats)
    nonzero = jnp.any(grouped != 0, axis=(1, 2)).astype(jnp.int32)
    mats = 2 * (hid * feats * 2 + middle_weight.shape[1] * hid * hid)
    per = ROWS // HALF
    return pl.pallas_call(
        network_kernel,
        grid_spec=pltpu.PrefetchScalarGridSpec(
            num_scalar_prefetch=1,
            grid=(count // ROWS,),
            in_specs=[
                pl.BlockSpec(memory_space=pl.ANY),
                pl.BlockSpec(first.shape, lambda i, n: (0, 0)),
                pl.BlockSpec(middle.shape, lambda i, n: (0, 0, 0)),
                pl.BlockSpec(last.shape, lambda i, n: (0, 0)),
            ],
            out_specs=pl.BlockSpec(memory_space=pl.ANY),
            scratch_shapes=[
                pltpu.VMEM((2, ROWS, feats), jnp.bfloat16),
                pltpu.VMEM((2, ROWS, feats), jnp.bfloat16),
                pltpu.SemaphoreType.DMA((2, per)),
                pltpu.SemaphoreType.DMA((2, per)),
                pltpu.SMEM((groups,), jnp.int32),
                pltpu.SMEM((1,), jnp.int32),
            ],
        ),
        out_shape=jax.ShapeDtypeStruct((count, feats), jnp.bfloat16),
        cost_estimate=pl.CostEstimate(
            flops=mats * count,
            bytes_accessed=4 * count * feats + 2 * (mats // 2),
            transcendentals=(1 + middle_weight.shape[1]) * hid * count,
        ),
    )(nonzero, rows_in, first, middle, last)


UNROLL = 32


def pack_kernel(t_ref, cur_ref, o_ref, rows, full):
    feats, lat_cells, lon_cells = cur_ref.shape
    for r in range(lat_cells):
        rows[r * lon_cells:(r + 1) * lon_cells, :] = cur_ref[:, r, :].T
    full[...] = jnp.zeros(full.shape, full.dtype)

    def body(i, carry):
        for u in range(UNROLL):
            c = i * UNROLL + u
            full[pl.ds(t_ref[c], 1), :] = rows[pl.ds(c, 1), :]
        return carry

    lax.fori_loop(0, rows.shape[0] // UNROLL, body, 0)
    o_ref[...] = full[...].astype(o_ref.dtype)


def pack(targets, current, slots):
    feats, lat_cells, lon_cells = current.shape
    count = lat_cells * lon_cells
    return pl.pallas_call(
        pack_kernel,
        grid_spec=pltpu.PrefetchScalarGridSpec(
            num_scalar_prefetch=1,
            grid=(1,),
            in_specs=[pl.BlockSpec(current.shape, lambda i, t: (0, 0, 0))],
            out_specs=pl.BlockSpec((slots, feats), lambda i, t: (0, 0)),
            scratch_shapes=[pltpu.VMEM((count, feats), jnp.float32), pltpu.VMEM((slots, feats), jnp.float32)],
        ),
        out_shape=jax.ShapeDtypeStruct((slots, feats), jnp.bfloat16),
    )(targets, current)


def combine_kernel(t_ref, ret_ref, cur_ref, o_ref, full, tend):
    feats, lat_cells, lon_cells = cur_ref.shape
    full[...] = ret_ref[...].astype(jnp.float32)

    def body(i, carry):
        for u in range(UNROLL):
            c = i * UNROLL + u
            tend[pl.ds(c, 1), :] = full[pl.ds(t_ref[c], 1), :]
        return carry

    lax.fori_loop(0, tend.shape[0] // UNROLL, body, 0)
    for r in range(lat_cells):
        o_ref[:, r, :] = cur_ref[:, r, :] + tend[r * lon_cells:(r + 1) * lon_cells, :].T


def combine(targets, returned_rows, current):
    feats, lat_cells, lon_cells = current.shape
    slots = returned_rows.shape[0]
    return pl.pallas_call(
        combine_kernel,
        grid_spec=pltpu.PrefetchScalarGridSpec(
            num_scalar_prefetch=1,
            grid=(1,),
            in_specs=[
                pl.BlockSpec((slots, feats), lambda i, t: (0, 0)),
                pl.BlockSpec(current.shape, lambda i, t: (0, 0, 0)),
            ],
            out_specs=pl.BlockSpec(current.shape, lambda i, t: (0, 0, 0)),
            scratch_shapes=[
                pltpu.VMEM((slots, feats), jnp.float32),
                pltpu.VMEM((lat_cells * lon_cells, feats), jnp.float32),
            ],
        ),
        out_shape=jax.ShapeDtypeStruct(current.shape, jnp.float32),
    )(targets, returned_rows, current)


def local(
    column_state, wind_speed, diffusivity, batch_index, input_weight, middle_weight, output_weight
):
    num_vars, levels, lat_cells, lon_cells = column_state.shape
    features = num_vars * levels
    current = column_state.reshape(features, lat_cells, lon_cells)
    sides = edges(current)
    for sweep_index in range(2):
        halos = exchange(*sides, features, lat_cells)
        current, *sides = sweep(current, halos, wind_speed[0], wind_speed[1], diffusivity, sweep_index == 0)
    column_count = lat_cells * lon_cells
    experts = lax.axis_size("lon")
    capacity = 2 * column_count // experts
    targets_all = batch_index.reshape(column_count)
    position = positions(targets_all, experts)
    targets = targets_all * capacity + position
    packed = pack(targets, current, experts * capacity).T.reshape(features, experts, capacity)
    chunks = 1
    width = capacity // chunks
    answers = []
    for chunk in range(chunks):
        part = packed[:, :, chunk * width:(chunk + 1) * width]
        received = lax.all_to_all(part, "lon", split_axis=1, concat_axis=1, tiled=True)
        rows_in = received.reshape(features, experts * width).T
        result = network(rows_in, input_weight, middle_weight, output_weight).T
        answers.append(
            lax.all_to_all(result.reshape(features, experts, width), "lon", split_axis=1, concat_axis=1, tiled=True)
        )
    returned = jnp.concatenate(answers, axis=2)
    return combine(targets, returned.reshape(features, -1).T, current).reshape(column_state.shape)


def solution(mesh):
    in_specs = (
        P(None, None, "lat", "lon"),
        P(None, None, "lat", "lon"),
        P(None, "lat", "lon"),
        P("lat", "lon", None),
        P("lon", None, None),
        P("lon", None, None, None),
        P("lon", None, None),
    )
    out_specs = P(None, None, "lat", "lon")
    return jax.shard_map(local, mesh=mesh, in_specs=in_specs, out_specs=out_specs, check_vma=False)
```

```python
import jax
import jax.numpy as jnp
from jax import lax
from jax.experimental import pallas as pl
from jax.experimental.pallas import tpu as pltpu
from jax.sharding import PartitionSpec as P


def neighbours(axis, periodic):
    count = lax.axis_size(axis)
    forward = [(i, i + 1) for i in range(count - 1)]
    if periodic:
        forward.append((count - 1, 0))
    backward = [(target, source) for source, target in forward]
    return forward, backward


FB = 32

def keep_edges(block_ref, top_ref, bottom_ref, ends_ref):
    feats, rows, cols = block_ref.shape
    for f in range(feats):
        top_ref[f] = block_ref[f, 0:1, :]
        bottom_ref[f] = block_ref[f, rows - 1:rows, :]
    lane = lax.broadcasted_iota(jnp.int32, (2, cols), 1)
    which = lax.broadcasted_iota(jnp.int32, (2, cols), 0)
    pick = (lane == which * (cols - 1)).astype(jnp.float32)
    ends_ref[...] = lax.dot_general(
        pick, block_ref[...].reshape(feats * rows, cols), (((1,), (1,)), ((), ())),
        precision=lax.Precision.HIGHEST, preferred_element_type=jnp.float32,
    )


def sweep_kernel(q_ref, hn_ref, hs_ref, he_ref, hw_ref, u_ref, v_ref, k_ref, o_ref, *edge_refs):
    rows, cols = q_ref.shape[1], q_ref.shape[2]
    row = lax.broadcasted_iota(jnp.int32, (rows, cols), 0)
    lane = lax.broadcasted_iota(jnp.int32, (rows, cols), 1)
    he = he_ref[0]
    hw = hw_ref[0]
    for f in range(FB):
        q = q_ref[f]
        north = jnp.where(row == rows - 1, jnp.broadcast_to(hn_ref[f], (rows, cols)), pltpu.roll(q, rows - 1, 0))
        south = jnp.where(row == 0, jnp.broadcast_to(hs_ref[f], (rows, cols)), pltpu.roll(q, 1, 0))
        east = jnp.where(lane == cols - 1, jnp.broadcast_to(he[:, f:f + 1], (rows, cols)), pltpu.roll(q, cols - 1, 1))
        west = jnp.where(lane == 0, jnp.broadcast_to(hw[:, f:f + 1], (rows, cols)), pltpu.roll(q, 1, 1))
        u = u_ref[f]
        v = v_ref[f]
        k = k_ref[f]
        o_ref[f] = (q - 0.5 * u * (east - west) - 0.5 * v * (north - south)
                    + k * (east + west + north + south - 4.0 * q))
    if edge_refs:
        keep_edges(o_ref, *edge_refs)


def sweep(q, halos, u, v, k, emit_edges):
    feats, rows, cols = q.shape
    levels = u.shape[0]
    nb = feats // FB
    per = levels // FB
    big = pl.BlockSpec((FB, rows, cols), lambda i: (i, 0, 0))
    field = pl.BlockSpec((FB, rows, cols), lambda i: (i % per, 0, 0))
    edge_row = pl.BlockSpec((FB, 1, cols), lambda i: (i, 0, 0))
    edge_col = pl.BlockSpec((1, rows, FB), lambda i: (i, 0, 0))
    out_specs, out_shape = [big], [jax.ShapeDtypeStruct(q.shape, q.dtype)]
    if emit_edges:
        out_specs += [edge_row, edge_row, pl.BlockSpec((2, FB * rows), lambda i: (0, i))]
        out_shape += [
            jax.ShapeDtypeStruct((feats, 1, cols), jnp.float32),
            jax.ShapeDtypeStruct((feats, 1, cols), jnp.float32),
            jax.ShapeDtypeStruct((2, feats * rows), jnp.float32),
        ]
    return pl.pallas_call(
        sweep_kernel,
        grid=(nb,),
        in_specs=[big, edge_row, edge_row, edge_col, edge_col, field, field, field],
        out_specs=out_specs,
        out_shape=out_shape,
        cost_estimate=pl.CostEstimate(flops=20 * q.size, bytes_accessed=8 * q.size + 12 * u.size, transcendentals=0),
    )(q, *halos, u, v, k)


def columns_of(edge):
    feats, rows = edge.shape
    return jnp.swapaxes(edge.reshape(feats // FB, FB, rows), 1, 2)


def exchange(top, bottom, ends, feats, rows):
    lat_forward, lat_backward = neighbours("lat", False)
    lon_forward, lon_backward = neighbours("lon", True)
    hn = lax.ppermute(top, "lat", lat_backward)
    hs = lax.ppermute(bottom, "lat", lat_forward)
    he = lax.ppermute(columns_of(ends[0].reshape(feats, rows)), "lon", lon_backward)
    hw = lax.ppermute(columns_of(ends[1].reshape(feats, rows)), "lon", lon_forward)
    return hn, hs, he, hw


def edges(x):
    feats, rows, cols = x.shape
    lane = lax.broadcasted_iota(jnp.int32, (cols, 2), 0)
    which = lax.broadcasted_iota(jnp.int32, (cols, 2), 1)
    pick = (lane == which * (cols - 1)).astype(jnp.float32)
    ends = jnp.dot(x.reshape(feats * rows, cols), pick, precision=lax.Precision.HIGHEST)
    return x[:, :1, :], x[:, rows - 1:, :], ends.T


def positions(targets_all, experts):
    count = targets_all.shape[0]
    block = 128
    onehot = (targets_all[:, None] == jnp.arange(experts, dtype=jnp.int32)[None, :]).astype(
        jnp.bfloat16
    )
    blocks = onehot.reshape(count // block, block, experts)
    rows = jnp.arange(block, dtype=jnp.int32)
    before = (rows[:, None] > rows[None, :]).astype(jnp.bfloat16)
    within = jnp.einsum("ij,bje->bie", before, blocks, preferred_element_type=jnp.float32)
    totals = jnp.sum(blocks.astype(jnp.float32), axis=1)
    offsets = jnp.cumsum(totals, axis=0) - totals
    ranks = within + offsets[:, None, :]
    position = jnp.sum(ranks * blocks.astype(jnp.float32), axis=2)
    return position.reshape(count).astype(jnp.int32)


ROWS = 1024
HALF = 128


def silu(t):
    return t * (0.5 * jnp.tanh(0.5 * t) + 0.5)


def layers(x, w_first, w_middle, w_last):
    hidden = silu(jnp.dot(x, w_first, preferred_element_type=jnp.float32)).astype(jnp.bfloat16)
    for layer_index in range(w_middle.shape[0]):
        hidden = silu(
            jnp.dot(hidden, w_middle[layer_index], preferred_element_type=jnp.float32)
        ).astype(jnp.bfloat16)
    return jnp.dot(hidden, w_last, preferred_element_type=jnp.float32).astype(jnp.bfloat16)


def network_kernel(nonzero_ref, x_hbm, first_ref, middle_ref, last_ref, o_hbm, buf, res, lsem, ssem, source_ref, used_ref):
    block = pl.program_id(0)
    blocks = pl.num_programs(0)
    per = ROWS // HALF
    groups = source_ref.shape[0]

    @pl.when(block == 0)
    def _():
        def nonempty(g, used):
            @pl.when(nonzero_ref[g] > 0)
            def _():
                source_ref[used] = g

            return used + nonzero_ref[g]

        used = lax.fori_loop(0, groups, nonempty, 0)
        used_ref[0] = used

        def empty(g, at):
            @pl.when(nonzero_ref[g] == 0)
            def _():
                source_ref[at] = g

            return at + 1 - nonzero_ref[g]

        lax.fori_loop(0, groups, empty, used)

    active = (used_ref[0] * HALF + ROWS - 1) // ROWS
    slot = block % 2

    def loads(index, into):
        return [
            pltpu.make_async_copy(
                x_hbm.at[pl.ds(source_ref[index * per + j] * HALF, HALF)],
                buf.at[into, pl.ds(j * HALF, HALF)],
                lsem.at[into, j],
            )
            for j in range(per)
        ]

    def stores(index, outof):
        return [
            pltpu.make_async_copy(
                res.at[outof, pl.ds(j * HALF, HALF)],
                o_hbm.at[pl.ds(source_ref[index * per + j] * HALF, HALF)],
                ssem.at[outof, j],
            )
            for j in range(per)
        ]

    @pl.when((block == 0) & (active > 0))
    def _():
        for copy in loads(0, 0):
            copy.start()

    @pl.when(block + 1 < active)
    def _():
        for copy in loads(block + 1, 1 - slot):
            copy.start()

    @pl.when(block >= 2)
    def _():
        for copy in stores(block - 2, slot):
            copy.wait()

    @pl.when(block < active)
    def _():
        for copy in loads(block, slot):
            copy.wait()
        res[slot] = layers(buf[slot], first_ref[...], middle_ref[...], last_ref[...])

    @pl.when(block >= active)
    def _():
        res[slot] = jnp.zeros(res.shape[1:], res.dtype)

    for copy in stores(block, slot):
        copy.start()

    @pl.when(block == blocks - 1)
    def _():
        for copy in stores(block - 1, 1 - slot):
            copy.wait()
        for copy in stores(block, slot):
            copy.wait()


def network(rows_in, input_weight, middle_weight, output_weight):
    count, feats = rows_in.shape
    groups = count // HALF
    hid = input_weight.shape[1]
    first = input_weight[0].T
    middle = jnp.swapaxes(middle_weight[0], 1, 2)
    last = output_weight[0].T
    grouped = rows_in.reshape(groups, HALF, feats)
    nonzero = jnp.any(grouped != 0, axis=(1, 2)).astype(jnp.int32)
    mats = 2 * (hid * feats * 2 + middle_weight.shape[1] * hid * hid)
    per = ROWS // HALF
    return pl.pallas_call(
        network_kernel,
        grid_spec=pltpu.PrefetchScalarGridSpec(
            num_scalar_prefetch=1,
            grid=(count // ROWS,),
            in_specs=[
                pl.BlockSpec(memory_space=pl.ANY),
                pl.BlockSpec(first.shape, lambda i, n: (0, 0)),
                pl.BlockSpec(middle.shape, lambda i, n: (0, 0, 0)),
                pl.BlockSpec(last.shape, lambda i, n: (0, 0)),
            ],
            out_specs=pl.BlockSpec(memory_space=pl.ANY),
            scratch_shapes=[
                pltpu.VMEM((2, ROWS, feats), jnp.bfloat16),
                pltpu.VMEM((2, ROWS, feats), jnp.bfloat16),
                pltpu.SemaphoreType.DMA((2, per)),
                pltpu.SemaphoreType.DMA((2, per)),
                pltpu.SMEM((groups,), jnp.int32),
                pltpu.SMEM((1,), jnp.int32),
            ],
        ),
        out_shape=jax.ShapeDtypeStruct((count, feats), jnp.bfloat16),
        cost_estimate=pl.CostEstimate(
            flops=mats * count,
            bytes_accessed=4 * count * feats + 2 * (mats // 2),
            transcendentals=(1 + middle_weight.shape[1]) * hid * count,
        ),
    )(nonzero, rows_in, first, middle, last)


UNROLL = 32


def pack_kernel(t_ref, cur_ref, o_ref, rows, full):
    feats, lat_cells, lon_cells = cur_ref.shape
    for r in range(lat_cells):
        rows[r * lon_cells:(r + 1) * lon_cells, :] = cur_ref[:, r, :].T
    full[...] = jnp.zeros(full.shape, full.dtype)

    def body(i, carry):
        for u in range(UNROLL):
            c = i * UNROLL + u
            full[pl.ds(t_ref[c], 1), :] = rows[pl.ds(c, 1), :]
        return carry

    lax.fori_loop(0, rows.shape[0] // UNROLL, body, 0)
    o_ref[...] = full[...].astype(o_ref.dtype)


def pack(targets, current, slots):
    feats, lat_cells, lon_cells = current.shape
    count = lat_cells * lon_cells
    return pl.pallas_call(
        pack_kernel,
        grid_spec=pltpu.PrefetchScalarGridSpec(
            num_scalar_prefetch=1,
            grid=(1,),
            in_specs=[pl.BlockSpec(current.shape, lambda i, t: (0, 0, 0))],
            out_specs=pl.BlockSpec((slots, feats), lambda i, t: (0, 0)),
            scratch_shapes=[pltpu.VMEM((count, feats), jnp.float32), pltpu.VMEM((slots, feats), jnp.float32)],
        ),
        out_shape=jax.ShapeDtypeStruct((slots, feats), jnp.bfloat16),
    )(targets, current)


def combine_kernel(t_ref, ret_ref, cur_ref, o_ref, full, tend):
    feats, lat_cells, lon_cells = cur_ref.shape
    full[...] = ret_ref[...].astype(jnp.float32)

    def body(i, carry):
        for u in range(UNROLL):
            c = i * UNROLL + u
            tend[pl.ds(c, 1), :] = full[pl.ds(t_ref[c], 1), :]
        return carry

    lax.fori_loop(0, tend.shape[0] // UNROLL, body, 0)
    for r in range(lat_cells):
        o_ref[:, r, :] = cur_ref[:, r, :] + tend[r * lon_cells:(r + 1) * lon_cells, :].T


def combine(targets, returned_rows, current):
    feats, lat_cells, lon_cells = current.shape
    slots = returned_rows.shape[0]
    return pl.pallas_call(
        combine_kernel,
        grid_spec=pltpu.PrefetchScalarGridSpec(
            num_scalar_prefetch=1,
            grid=(1,),
            in_specs=[
                pl.BlockSpec((slots, feats), lambda i, t: (0, 0)),
                pl.BlockSpec(current.shape, lambda i, t: (0, 0, 0)),
            ],
            out_specs=pl.BlockSpec(current.shape, lambda i, t: (0, 0, 0)),
            scratch_shapes=[
                pltpu.VMEM((slots, feats), jnp.float32),
                pltpu.VMEM((lat_cells * lon_cells, feats), jnp.float32),
            ],
        ),
        out_shape=jax.ShapeDtypeStruct(current.shape, jnp.float32),
    )(targets, returned_rows, current)


def local(
    column_state, wind_speed, diffusivity, batch_index, input_weight, middle_weight, output_weight
):
    num_vars, levels, lat_cells, lon_cells = column_state.shape
    features = num_vars * levels
    current = column_state.reshape(features, lat_cells, lon_cells)
    sides = edges(current)
    for sweep_index in range(2):
        halos = exchange(*sides, features, lat_cells)
        current, *sides = sweep(current, halos, wind_speed[0], wind_speed[1], diffusivity, sweep_index == 0)
    column_count = lat_cells * lon_cells
    experts = lax.axis_size("lon")
    capacity = 2 * column_count // experts
    targets_all = batch_index.reshape(column_count)
    position = positions(targets_all, experts)
    targets = targets_all * capacity + position
    packed = pack(targets, current, experts * capacity).T.reshape(features, experts, capacity)
    chunks = 2
    width = capacity // chunks
    answers = []
    for chunk in range(chunks):
        part = packed[:, :, chunk * width:(chunk + 1) * width]
        received = lax.all_to_all(part, "lon", split_axis=1, concat_axis=1, tiled=True)
        rows_in = received.reshape(features, experts * width).T
        result = network(rows_in, input_weight, middle_weight, output_weight).T
        answers.append(
            lax.all_to_all(result.reshape(features, experts, width), "lon", split_axis=1, concat_axis=1, tiled=True)
        )
    returned = jnp.concatenate(answers, axis=2)
    return combine(targets, returned.reshape(features, -1).T, current).reshape(column_state.shape)


def solution(mesh):
    in_specs = (
        P(None, None, "lat", "lon"),
        P(None, None, "lat", "lon"),
        P(None, "lat", "lon"),
        P("lat", "lon", None),
        P("lon", None, None),
        P("lon", None, None, None),
        P("lon", None, None),
    )
    out_specs = P(None, None, "lat", "lon")
    return jax.shard_map(local, mesh=mesh, in_specs=in_specs, out_specs=out_specs, check_vma=False)
```

```python
import jax
import jax.numpy as jnp
from jax import lax
from jax.experimental import pallas as pl
from jax.experimental.pallas import tpu as pltpu
from jax.sharding import PartitionSpec as P


def neighbours(axis, periodic):
    count = lax.axis_size(axis)
    forward = [(i, i + 1) for i in range(count - 1)]
    if periodic:
        forward.append((count - 1, 0))
    backward = [(target, source) for source, target in forward]
    return forward, backward


FB = 32

def keep_edges(block_ref, top_ref, bottom_ref, ends_ref):
    feats, rows, cols = block_ref.shape
    for f in range(feats):
        top_ref[f] = block_ref[f, 0:1, :]
        bottom_ref[f] = block_ref[f, rows - 1:rows, :]
    lane = lax.broadcasted_iota(jnp.int32, (2, cols), 1)
    which = lax.broadcasted_iota(jnp.int32, (2, cols), 0)
    pick = (lane == which * (cols - 1)).astype(jnp.float32)
    ends_ref[...] = lax.dot_general(
        pick, block_ref[...].reshape(feats * rows, cols), (((1,), (1,)), ((), ())),
        precision=lax.Precision.HIGHEST, preferred_element_type=jnp.float32,
    )


def sweep_kernel(q_ref, hn_ref, hs_ref, he_ref, hw_ref, u_ref, v_ref, k_ref, o_ref, *edge_refs):
    rows, cols = q_ref.shape[1], q_ref.shape[2]
    row = lax.broadcasted_iota(jnp.int32, (rows, cols), 0)
    lane = lax.broadcasted_iota(jnp.int32, (rows, cols), 1)
    he = he_ref[0]
    hw = hw_ref[0]
    for f in range(FB):
        q = q_ref[f]
        north = jnp.where(row == rows - 1, jnp.broadcast_to(hn_ref[f], (rows, cols)), pltpu.roll(q, rows - 1, 0))
        south = jnp.where(row == 0, jnp.broadcast_to(hs_ref[f], (rows, cols)), pltpu.roll(q, 1, 0))
        east = jnp.where(lane == cols - 1, jnp.broadcast_to(he[:, f:f + 1], (rows, cols)), pltpu.roll(q, cols - 1, 1))
        west = jnp.where(lane == 0, jnp.broadcast_to(hw[:, f:f + 1], (rows, cols)), pltpu.roll(q, 1, 1))
        u = u_ref[f]
        v = v_ref[f]
        k = k_ref[f]
        o_ref[f] = (q - 0.5 * u * (east - west) - 0.5 * v * (north - south)
                    + k * (east + west + north + south - 4.0 * q))
    if edge_refs:
        keep_edges(o_ref, *edge_refs)


def sweep(q, halos, u, v, k, emit_edges):
    feats, rows, cols = q.shape
    levels = u.shape[0]
    nb = feats // FB
    per = levels // FB
    big = pl.BlockSpec((FB, rows, cols), lambda i: (i, 0, 0))
    field = pl.BlockSpec((FB, rows, cols), lambda i: (i % per, 0, 0))
    edge_row = pl.BlockSpec((FB, 1, cols), lambda i: (i, 0, 0))
    edge_col = pl.BlockSpec((1, rows, FB), lambda i: (i, 0, 0))
    out_specs, out_shape = [big], [jax.ShapeDtypeStruct(q.shape, q.dtype)]
    if emit_edges:
        out_specs += [edge_row, edge_row, pl.BlockSpec((2, FB * rows), lambda i: (0, i))]
        out_shape += [
            jax.ShapeDtypeStruct((feats, 1, cols), jnp.float32),
            jax.ShapeDtypeStruct((feats, 1, cols), jnp.float32),
            jax.ShapeDtypeStruct((2, feats * rows), jnp.float32),
        ]
    return pl.pallas_call(
        sweep_kernel,
        grid=(nb,),
        in_specs=[big, edge_row, edge_row, edge_col, edge_col, field, field, field],
        out_specs=out_specs,
        out_shape=out_shape,
        cost_estimate=pl.CostEstimate(flops=20 * q.size, bytes_accessed=8 * q.size + 12 * u.size, transcendentals=0),
    )(q, *halos, u, v, k)


def columns_of(edge):
    feats, rows = edge.shape
    return jnp.swapaxes(edge.reshape(feats // FB, FB, rows), 1, 2)


def exchange(top, bottom, ends, feats, rows):
    lat_forward, lat_backward = neighbours("lat", False)
    lon_forward, lon_backward = neighbours("lon", True)
    hn = lax.ppermute(top, "lat", lat_backward)
    hs = lax.ppermute(bottom, "lat", lat_forward)
    he = lax.ppermute(columns_of(ends[0].reshape(feats, rows)), "lon", lon_backward)
    hw = lax.ppermute(columns_of(ends[1].reshape(feats, rows)), "lon", lon_forward)
    return hn, hs, he, hw


def edges(x):
    feats, rows, cols = x.shape
    lane = lax.broadcasted_iota(jnp.int32, (cols, 2), 0)
    which = lax.broadcasted_iota(jnp.int32, (cols, 2), 1)
    pick = (lane == which * (cols - 1)).astype(jnp.float32)
    ends = jnp.dot(x.reshape(feats * rows, cols), pick, precision=lax.Precision.HIGHEST)
    ends_t, top, bottom = lax.optimization_barrier((ends.T, x[:, :1, :], x[:, rows - 1:, :]))
    return top, bottom, ends_t


def positions(targets_all, experts):
    count = targets_all.shape[0]
    block = 128
    onehot = (targets_all[:, None] == jnp.arange(experts, dtype=jnp.int32)[None, :]).astype(
        jnp.bfloat16
    )
    blocks = onehot.reshape(count // block, block, experts)
    rows = jnp.arange(block, dtype=jnp.int32)
    before = (rows[:, None] > rows[None, :]).astype(jnp.bfloat16)
    within = jnp.einsum("ij,bje->bie", before, blocks, preferred_element_type=jnp.float32)
    totals = jnp.sum(blocks.astype(jnp.float32), axis=1)
    offsets = jnp.cumsum(totals, axis=0) - totals
    ranks = within + offsets[:, None, :]
    position = jnp.sum(ranks * blocks.astype(jnp.float32), axis=2)
    return position.reshape(count).astype(jnp.int32)


ROWS = 1024
HALF = 128


def silu(t):
    return t * (0.5 * jnp.tanh(0.5 * t) + 0.5)


def layers(x, w_first, w_middle, w_last):
    hidden = silu(jnp.dot(x, w_first, preferred_element_type=jnp.float32)).astype(jnp.bfloat16)
    for layer_index in range(w_middle.shape[0]):
        hidden = silu(
            jnp.dot(hidden, w_middle[layer_index], preferred_element_type=jnp.float32)
        ).astype(jnp.bfloat16)
    return jnp.dot(hidden, w_last, preferred_element_type=jnp.float32).astype(jnp.bfloat16)


def network_kernel(nonzero_ref, x_hbm, first_ref, middle_ref, last_ref, o_hbm, buf, res, lsem, ssem, source_ref, used_ref):
    block = pl.program_id(0)
    blocks = pl.num_programs(0)
    per = ROWS // HALF
    groups = source_ref.shape[0]

    @pl.when(block == 0)
    def _():
        def nonempty(g, used):
            @pl.when(nonzero_ref[g] > 0)
            def _():
                source_ref[used] = g

            return used + nonzero_ref[g]

        used = lax.fori_loop(0, groups, nonempty, 0)
        used_ref[0] = used

        def empty(g, at):
            @pl.when(nonzero_ref[g] == 0)
            def _():
                source_ref[at] = g

            return at + 1 - nonzero_ref[g]

        lax.fori_loop(0, groups, empty, used)

    active = (used_ref[0] * HALF + ROWS - 1) // ROWS
    slot = block % 2

    def loads(index, into):
        return [
            pltpu.make_async_copy(
                x_hbm.at[pl.ds(source_ref[index * per + j] * HALF, HALF)],
                buf.at[into, pl.ds(j * HALF, HALF)],
                lsem.at[into, j],
            )
            for j in range(per)
        ]

    def stores(index, outof):
        return [
            pltpu.make_async_copy(
                res.at[outof, pl.ds(j * HALF, HALF)],
                o_hbm.at[pl.ds(source_ref[index * per + j] * HALF, HALF)],
                ssem.at[outof, j],
            )
            for j in range(per)
        ]

    @pl.when((block == 0) & (active > 0))
    def _():
        for copy in loads(0, 0):
            copy.start()

    @pl.when(block + 1 < active)
    def _():
        for copy in loads(block + 1, 1 - slot):
            copy.start()

    @pl.when(block >= 2)
    def _():
        for copy in stores(block - 2, slot):
            copy.wait()

    @pl.when(block < active)
    def _():
        for copy in loads(block, slot):
            copy.wait()
        res[slot] = layers(buf[slot], first_ref[...], middle_ref[...], last_ref[...])

    @pl.when(block >= active)
    def _():
        res[slot] = jnp.zeros(res.shape[1:], res.dtype)

    for copy in stores(block, slot):
        copy.start()

    @pl.when(block == blocks - 1)
    def _():
        for copy in stores(block - 1, 1 - slot):
            copy.wait()
        for copy in stores(block, slot):
            copy.wait()


def network(rows_in, input_weight, middle_weight, output_weight):
    count, feats = rows_in.shape
    groups = count // HALF
    hid = input_weight.shape[1]
    first = input_weight[0].T
    middle = jnp.swapaxes(middle_weight[0], 1, 2)
    last = output_weight[0].T
    grouped = rows_in.reshape(groups, HALF, feats)
    nonzero = jnp.any(grouped != 0, axis=(1, 2)).astype(jnp.int32)
    mats = 2 * (hid * feats * 2 + middle_weight.shape[1] * hid * hid)
    per = ROWS // HALF
    return pl.pallas_call(
        network_kernel,
        grid_spec=pltpu.PrefetchScalarGridSpec(
            num_scalar_prefetch=1,
            grid=(count // ROWS,),
            in_specs=[
                pl.BlockSpec(memory_space=pl.ANY),
                pl.BlockSpec(first.shape, lambda i, n: (0, 0)),
                pl.BlockSpec(middle.shape, lambda i, n: (0, 0, 0)),
                pl.BlockSpec(last.shape, lambda i, n: (0, 0)),
            ],
            out_specs=pl.BlockSpec(memory_space=pl.ANY),
            scratch_shapes=[
                pltpu.VMEM((2, ROWS, feats), jnp.bfloat16),
                pltpu.VMEM((2, ROWS, feats), jnp.bfloat16),
                pltpu.SemaphoreType.DMA((2, per)),
                pltpu.SemaphoreType.DMA((2, per)),
                pltpu.SMEM((groups,), jnp.int32),
                pltpu.SMEM((1,), jnp.int32),
            ],
        ),
        out_shape=jax.ShapeDtypeStruct((count, feats), jnp.bfloat16),
        cost_estimate=pl.CostEstimate(
            flops=mats * count,
            bytes_accessed=4 * count * feats + 2 * (mats // 2),
            transcendentals=(1 + middle_weight.shape[1]) * hid * count,
        ),
    )(nonzero, rows_in, first, middle, last)


UNROLL = 32


def pack_kernel(t_ref, cur_ref, o_ref, rows, full):
    feats, lat_cells, lon_cells = cur_ref.shape
    for r in range(lat_cells):
        rows[r * lon_cells:(r + 1) * lon_cells, :] = cur_ref[:, r, :].T
    full[...] = jnp.zeros(full.shape, full.dtype)

    def body(i, carry):
        for u in range(UNROLL):
            c = i * UNROLL + u
            full[pl.ds(t_ref[c], 1), :] = rows[pl.ds(c, 1), :]
        return carry

    lax.fori_loop(0, rows.shape[0] // UNROLL, body, 0)
    o_ref[...] = full[...].astype(o_ref.dtype)


def pack(targets, current, slots):
    feats, lat_cells, lon_cells = current.shape
    count = lat_cells * lon_cells
    return pl.pallas_call(
        pack_kernel,
        grid_spec=pltpu.PrefetchScalarGridSpec(
            num_scalar_prefetch=1,
            grid=(1,),
            in_specs=[pl.BlockSpec(current.shape, lambda i, t: (0, 0, 0))],
            out_specs=pl.BlockSpec((slots, feats), lambda i, t: (0, 0)),
            scratch_shapes=[pltpu.VMEM((count, feats), jnp.float32), pltpu.VMEM((slots, feats), jnp.float32)],
        ),
        out_shape=jax.ShapeDtypeStruct((slots, feats), jnp.bfloat16),
    )(targets, current)


def combine_kernel(t_ref, ret_ref, cur_ref, o_ref, full, tend):
    feats, lat_cells, lon_cells = cur_ref.shape
    full[...] = ret_ref[...].astype(jnp.float32)

    def body(i, carry):
        for u in range(UNROLL):
            c = i * UNROLL + u
            tend[pl.ds(c, 1), :] = full[pl.ds(t_ref[c], 1), :]
        return carry

    lax.fori_loop(0, tend.shape[0] // UNROLL, body, 0)
    for r in range(lat_cells):
        o_ref[:, r, :] = cur_ref[:, r, :] + tend[r * lon_cells:(r + 1) * lon_cells, :].T


def combine(targets, returned_rows, current):
    feats, lat_cells, lon_cells = current.shape
    slots = returned_rows.shape[0]
    return pl.pallas_call(
        combine_kernel,
        grid_spec=pltpu.PrefetchScalarGridSpec(
            num_scalar_prefetch=1,
            grid=(1,),
            in_specs=[
                pl.BlockSpec((slots, feats), lambda i, t: (0, 0)),
                pl.BlockSpec(current.shape, lambda i, t: (0, 0, 0)),
            ],
            out_specs=pl.BlockSpec(current.shape, lambda i, t: (0, 0, 0)),
            scratch_shapes=[
                pltpu.VMEM((slots, feats), jnp.float32),
                pltpu.VMEM((lat_cells * lon_cells, feats), jnp.float32),
            ],
        ),
        out_shape=jax.ShapeDtypeStruct(current.shape, jnp.float32),
    )(targets, returned_rows, current)


def local(
    column_state, wind_speed, diffusivity, batch_index, input_weight, middle_weight, output_weight
):
    num_vars, levels, lat_cells, lon_cells = column_state.shape
    features = num_vars * levels
    current = column_state.reshape(features, lat_cells, lon_cells)
    sides = edges(current)
    for sweep_index in range(2):
        halos = exchange(*sides, features, lat_cells)
        current, *sides = sweep(current, halos, wind_speed[0], wind_speed[1], diffusivity, sweep_index == 0)
    column_count = lat_cells * lon_cells
    experts = lax.axis_size("lon")
    capacity = 2 * column_count // experts
    targets_all = batch_index.reshape(column_count)
    position = positions(targets_all, experts)
    targets = targets_all * capacity + position
    packed = pack(targets, current, experts * capacity).T.reshape(features, experts, capacity)
    chunks = 1
    width = capacity // chunks
    answers = []
    for chunk in range(chunks):
        part = packed[:, :, chunk * width:(chunk + 1) * width]
        received = lax.all_to_all(part, "lon", split_axis=1, concat_axis=1, tiled=True)
        rows_in = received.reshape(features, experts * width).T
        result = network(rows_in, input_weight, middle_weight, output_weight).T
        answers.append(
            lax.all_to_all(result.reshape(features, experts, width), "lon", split_axis=1, concat_axis=1, tiled=True)
        )
    returned = jnp.concatenate(answers, axis=2)
    return combine(targets, returned.reshape(features, -1).T, current).reshape(column_state.shape)


def solution(mesh):
    in_specs = (
        P(None, None, "lat", "lon"),
        P(None, None, "lat", "lon"),
        P(None, "lat", "lon"),
        P("lat", "lon", None),
        P("lon", None, None),
        P("lon", None, None, None),
        P("lon", None, None),
    )
    out_specs = P(None, None, "lat", "lon")
    return jax.shard_map(local, mesh=mesh, in_specs=in_specs, out_specs=out_specs, check_vma=False)
```

```python
import jax
import jax.numpy as jnp
from jax import lax
from jax.experimental import pallas as pl
from jax.experimental.pallas import tpu as pltpu
from jax.sharding import PartitionSpec as P


def neighbours(axis, periodic):
    count = lax.axis_size(axis)
    forward = [(i, i + 1) for i in range(count - 1)]
    if periodic:
        forward.append((count - 1, 0))
    backward = [(target, source) for source, target in forward]
    return forward, backward


FB = 32

def keep_edges(block_ref, top_ref, bottom_ref, ends_ref):
    feats, rows, cols = block_ref.shape
    for f in range(feats):
        top_ref[f] = block_ref[f, 0:1, :]
        bottom_ref[f] = block_ref[f, rows - 1:rows, :]
    lane = lax.broadcasted_iota(jnp.int32, (2, cols), 1)
    which = lax.broadcasted_iota(jnp.int32, (2, cols), 0)
    pick = (lane == which * (cols - 1)).astype(jnp.float32)
    ends_ref[...] = lax.dot_general(
        pick, block_ref[...].reshape(feats * rows, cols), (((1,), (1,)), ((), ())),
        precision=lax.Precision.HIGHEST, preferred_element_type=jnp.float32,
    )


def sweep_kernel(q_ref, hn_ref, hs_ref, he_ref, hw_ref, u_ref, v_ref, k_ref, o_ref, *edge_refs):
    rows, cols = q_ref.shape[1], q_ref.shape[2]
    row = lax.broadcasted_iota(jnp.int32, (rows, cols), 0)
    lane = lax.broadcasted_iota(jnp.int32, (rows, cols), 1)
    he = he_ref[0]
    hw = hw_ref[0]
    for f in range(FB):
        q = q_ref[f]
        north = jnp.where(row == rows - 1, jnp.broadcast_to(hn_ref[f], (rows, cols)), pltpu.roll(q, rows - 1, 0))
        south = jnp.where(row == 0, jnp.broadcast_to(hs_ref[f], (rows, cols)), pltpu.roll(q, 1, 0))
        east = jnp.where(lane == cols - 1, jnp.broadcast_to(he[:, f:f + 1], (rows, cols)), pltpu.roll(q, cols - 1, 1))
        west = jnp.where(lane == 0, jnp.broadcast_to(hw[:, f:f + 1], (rows, cols)), pltpu.roll(q, 1, 1))
        u = u_ref[f]
        v = v_ref[f]
        k = k_ref[f]
        o_ref[f] = (q - 0.5 * u * (east - west) - 0.5 * v * (north - south)
                    + k * (east + west + north + south - 4.0 * q))
    if edge_refs:
        keep_edges(o_ref, *edge_refs)


def sweep(q, halos, u, v, k, emit_edges):
    feats, rows, cols = q.shape
    levels = u.shape[0]
    nb = feats // FB
    per = levels // FB
    big = pl.BlockSpec((FB, rows, cols), lambda i: (i, 0, 0))
    field = pl.BlockSpec((FB, rows, cols), lambda i: (i % per, 0, 0))
    edge_row = pl.BlockSpec((FB, 1, cols), lambda i: (i, 0, 0))
    edge_col = pl.BlockSpec((1, rows, FB), lambda i: (i, 0, 0))
    out_specs, out_shape = [big], [jax.ShapeDtypeStruct(q.shape, q.dtype)]
    if emit_edges:
        out_specs += [edge_row, edge_row, pl.BlockSpec((2, FB * rows), lambda i: (0, i))]
        out_shape += [
            jax.ShapeDtypeStruct((feats, 1, cols), jnp.float32),
            jax.ShapeDtypeStruct((feats, 1, cols), jnp.float32),
            jax.ShapeDtypeStruct((2, feats * rows), jnp.float32),
        ]
    return pl.pallas_call(
        sweep_kernel,
        grid=(nb,),
        in_specs=[big, edge_row, edge_row, edge_col, edge_col, field, field, field],
        out_specs=out_specs,
        out_shape=out_shape,
        cost_estimate=pl.CostEstimate(flops=20 * q.size, bytes_accessed=8 * q.size + 12 * u.size, transcendentals=0),
    )(q, *halos, u, v, k)


def columns_of(edge):
    feats, rows = edge.shape
    return jnp.swapaxes(edge.reshape(feats // FB, FB, rows), 1, 2)


def exchange(top, bottom, ends, feats, rows):
    lat_forward, lat_backward = neighbours("lat", False)
    lon_forward, lon_backward = neighbours("lon", True)
    hn = lax.ppermute(top, "lat", lat_backward)
    hs = lax.ppermute(bottom, "lat", lat_forward)
    he = lax.ppermute(columns_of(ends[0].reshape(feats, rows)), "lon", lon_backward)
    hw = lax.ppermute(columns_of(ends[1].reshape(feats, rows)), "lon", lon_forward)
    return hn, hs, he, hw


def edges(x):
    feats, rows, cols = x.shape
    lane = lax.broadcasted_iota(jnp.int32, (cols, 2), 0)
    which = lax.broadcasted_iota(jnp.int32, (cols, 2), 1)
    pick = (lane == which * (cols - 1)).astype(jnp.float32)
    ends = jnp.dot(x.reshape(feats * rows, cols), pick, precision=lax.Precision.HIGHEST)
    ends_t, top, bottom = lax.optimization_barrier((ends.T, x[:, :1, :], x[:, rows - 1:, :]))
    return top, bottom, ends_t


def positions(targets_all, experts):
    count = targets_all.shape[0]
    block = 128
    onehot = (targets_all[:, None] == jnp.arange(experts, dtype=jnp.int32)[None, :]).astype(
        jnp.bfloat16
    )
    blocks = onehot.reshape(count // block, block, experts)
    rows = jnp.arange(block, dtype=jnp.int32)
    before = (rows[:, None] > rows[None, :]).astype(jnp.bfloat16)
    within = jnp.einsum("ij,bje->bie", before, blocks, preferred_element_type=jnp.float32)
    totals = jnp.sum(blocks.astype(jnp.float32), axis=1)
    offsets = jnp.cumsum(totals, axis=0) - totals
    ranks = within + offsets[:, None, :]
    position = jnp.sum(ranks * blocks.astype(jnp.float32), axis=2)
    return position.reshape(count).astype(jnp.int32)


ROWS = 2048
HALF = 128


def silu(t):
    return t * (0.5 * jnp.tanh(0.5 * t) + 0.5)


def layers(x, w_first, w_middle, w_last):
    hidden = silu(jnp.dot(x, w_first, preferred_element_type=jnp.float32)).astype(jnp.bfloat16)
    for layer_index in range(w_middle.shape[0]):
        hidden = silu(
            jnp.dot(hidden, w_middle[layer_index], preferred_element_type=jnp.float32)
        ).astype(jnp.bfloat16)
    return jnp.dot(hidden, w_last, preferred_element_type=jnp.float32).astype(jnp.bfloat16)


def network_kernel(nonzero_ref, x_hbm, first_ref, middle_ref, last_ref, o_hbm, buf, res, lsem, ssem, source_ref, used_ref):
    block = pl.program_id(0)
    blocks = pl.num_programs(0)
    per = ROWS // HALF
    groups = source_ref.shape[0]

    @pl.when(block == 0)
    def _():
        def nonempty(g, used):
            @pl.when(nonzero_ref[g] > 0)
            def _():
                source_ref[used] = g

            return used + nonzero_ref[g]

        used = lax.fori_loop(0, groups, nonempty, 0)
        used_ref[0] = used

        def empty(g, at):
            @pl.when(nonzero_ref[g] == 0)
            def _():
                source_ref[at] = g

            return at + 1 - nonzero_ref[g]

        lax.fori_loop(0, groups, empty, used)

    active = (used_ref[0] * HALF + ROWS - 1) // ROWS
    slot = block % 2

    def loads(index, into):
        return [
            pltpu.make_async_copy(
                x_hbm.at[pl.ds(source_ref[index * per + j] * HALF, HALF)],
                buf.at[into, pl.ds(j * HALF, HALF)],
                lsem.at[into, j],
            )
            for j in range(per)
        ]

    def stores(index, outof):
        return [
            pltpu.make_async_copy(
                res.at[outof, pl.ds(j * HALF, HALF)],
                o_hbm.at[pl.ds(source_ref[index * per + j] * HALF, HALF)],
                ssem.at[outof, j],
            )
            for j in range(per)
        ]

    @pl.when((block == 0) & (active > 0))
    def _():
        for copy in loads(0, 0):
            copy.start()

    @pl.when(block + 1 < active)
    def _():
        for copy in loads(block + 1, 1 - slot):
            copy.start()

    @pl.when(block >= 2)
    def _():
        for copy in stores(block - 2, slot):
            copy.wait()

    @pl.when(block < active)
    def _():
        for copy in loads(block, slot):
            copy.wait()
        res[slot] = layers(buf[slot], first_ref[...], middle_ref[...], last_ref[...])

    @pl.when(block >= active)
    def _():
        res[slot] = jnp.zeros(res.shape[1:], res.dtype)

    for copy in stores(block, slot):
        copy.start()

    @pl.when(block == blocks - 1)
    def _():
        for copy in stores(block - 1, 1 - slot):
            copy.wait()
        for copy in stores(block, slot):
            copy.wait()


def network(rows_in, input_weight, middle_weight, output_weight):
    count, feats = rows_in.shape
    groups = count // HALF
    hid = input_weight.shape[1]
    first = input_weight[0].T
    middle = jnp.swapaxes(middle_weight[0], 1, 2)
    last = output_weight[0].T
    grouped = rows_in.reshape(groups, HALF, feats)
    nonzero = jnp.any(grouped != 0, axis=(1, 2)).astype(jnp.int32)
    mats = 2 * (hid * feats * 2 + middle_weight.shape[1] * hid * hid)
    per = ROWS // HALF
    return pl.pallas_call(
        network_kernel,
        grid_spec=pltpu.PrefetchScalarGridSpec(
            num_scalar_prefetch=1,
            grid=(count // ROWS,),
            in_specs=[
                pl.BlockSpec(memory_space=pl.ANY),
                pl.BlockSpec(first.shape, lambda i, n: (0, 0)),
                pl.BlockSpec(middle.shape, lambda i, n: (0, 0, 0)),
                pl.BlockSpec(last.shape, lambda i, n: (0, 0)),
            ],
            out_specs=pl.BlockSpec(memory_space=pl.ANY),
            scratch_shapes=[
                pltpu.VMEM((2, ROWS, feats), jnp.bfloat16),
                pltpu.VMEM((2, ROWS, feats), jnp.bfloat16),
                pltpu.SemaphoreType.DMA((2, per)),
                pltpu.SemaphoreType.DMA((2, per)),
                pltpu.SMEM((groups,), jnp.int32),
                pltpu.SMEM((1,), jnp.int32),
            ],
        ),
        out_shape=jax.ShapeDtypeStruct((count, feats), jnp.bfloat16),
        cost_estimate=pl.CostEstimate(
            flops=mats * count,
            bytes_accessed=4 * count * feats + 2 * (mats // 2),
            transcendentals=(1 + middle_weight.shape[1]) * hid * count,
        ),
    )(nonzero, rows_in, first, middle, last)


UNROLL = 32


def pack_kernel(t_ref, cur_ref, o_ref, rows, full):
    feats, lat_cells, lon_cells = cur_ref.shape
    for r in range(lat_cells):
        rows[r * lon_cells:(r + 1) * lon_cells, :] = cur_ref[:, r, :].T
    full[...] = jnp.zeros(full.shape, full.dtype)

    def body(i, carry):
        for u in range(UNROLL):
            c = i * UNROLL + u
            full[pl.ds(t_ref[c], 1), :] = rows[pl.ds(c, 1), :]
        return carry

    lax.fori_loop(0, rows.shape[0] // UNROLL, body, 0)
    o_ref[...] = full[...].astype(o_ref.dtype)


def pack(targets, current, slots):
    feats, lat_cells, lon_cells = current.shape
    count = lat_cells * lon_cells
    return pl.pallas_call(
        pack_kernel,
        grid_spec=pltpu.PrefetchScalarGridSpec(
            num_scalar_prefetch=1,
            grid=(1,),
            in_specs=[pl.BlockSpec(current.shape, lambda i, t: (0, 0, 0))],
            out_specs=pl.BlockSpec((slots, feats), lambda i, t: (0, 0)),
            scratch_shapes=[pltpu.VMEM((count, feats), jnp.float32), pltpu.VMEM((slots, feats), jnp.float32)],
        ),
        out_shape=jax.ShapeDtypeStruct((slots, feats), jnp.bfloat16),
    )(targets, current)


def combine_kernel(t_ref, ret_ref, cur_ref, o_ref, full, tend):
    feats, lat_cells, lon_cells = cur_ref.shape
    full[...] = ret_ref[...].astype(jnp.float32)

    def body(i, carry):
        for u in range(UNROLL):
            c = i * UNROLL + u
            tend[pl.ds(c, 1), :] = full[pl.ds(t_ref[c], 1), :]
        return carry

    lax.fori_loop(0, tend.shape[0] // UNROLL, body, 0)
    for r in range(lat_cells):
        o_ref[:, r, :] = cur_ref[:, r, :] + tend[r * lon_cells:(r + 1) * lon_cells, :].T


def combine(targets, returned_rows, current):
    feats, lat_cells, lon_cells = current.shape
    slots = returned_rows.shape[0]
    return pl.pallas_call(
        combine_kernel,
        grid_spec=pltpu.PrefetchScalarGridSpec(
            num_scalar_prefetch=1,
            grid=(1,),
            in_specs=[
                pl.BlockSpec((slots, feats), lambda i, t: (0, 0)),
                pl.BlockSpec(current.shape, lambda i, t: (0, 0, 0)),
            ],
            out_specs=pl.BlockSpec(current.shape, lambda i, t: (0, 0, 0)),
            scratch_shapes=[
                pltpu.VMEM((slots, feats), jnp.float32),
                pltpu.VMEM((lat_cells * lon_cells, feats), jnp.float32),
            ],
        ),
        out_shape=jax.ShapeDtypeStruct(current.shape, jnp.float32),
    )(targets, returned_rows, current)


def local(
    column_state, wind_speed, diffusivity, batch_index, input_weight, middle_weight, output_weight
):
    num_vars, levels, lat_cells, lon_cells = column_state.shape
    features = num_vars * levels
    current = column_state.reshape(features, lat_cells, lon_cells)
    sides = edges(current)
    for sweep_index in range(2):
        halos = exchange(*sides, features, lat_cells)
        current, *sides = sweep(current, halos, wind_speed[0], wind_speed[1], diffusivity, sweep_index == 0)
    column_count = lat_cells * lon_cells
    experts = lax.axis_size("lon")
    capacity = 2 * column_count // experts
    targets_all = batch_index.reshape(column_count)
    position = positions(targets_all, experts)
    targets = targets_all * capacity + position
    packed = pack(targets, current, experts * capacity).T.reshape(features, experts, capacity)
    chunks = 1
    width = capacity // chunks
    answers = []
    for chunk in range(chunks):
        part = packed[:, :, chunk * width:(chunk + 1) * width]
        received = lax.all_to_all(part, "lon", split_axis=1, concat_axis=1, tiled=True)
        rows_in = received.reshape(features, experts * width).T
        result = network(rows_in, input_weight, middle_weight, output_weight).T
        answers.append(
            lax.all_to_all(result.reshape(features, experts, width), "lon", split_axis=1, concat_axis=1, tiled=True)
        )
    returned = jnp.concatenate(answers, axis=2)
    return combine(targets, returned.reshape(features, -1).T, current).reshape(column_state.shape)


def solution(mesh):
    in_specs = (
        P(None, None, "lat", "lon"),
        P(None, None, "lat", "lon"),
        P(None, "lat", "lon"),
        P("lat", "lon", None),
        P("lon", None, None),
        P("lon", None, None, None),
        P("lon", None, None),
    )
    out_specs = P(None, None, "lat", "lon")
    return jax.shard_map(local, mesh=mesh, in_specs=in_specs, out_specs=out_specs, check_vma=False)
```

```python
import jax
import jax.numpy as jnp
from jax import lax
from jax.experimental import pallas as pl
from jax.experimental.pallas import tpu as pltpu
from jax.sharding import PartitionSpec as P


def neighbours(axis, periodic):
    count = lax.axis_size(axis)
    forward = [(i, i + 1) for i in range(count - 1)]
    if periodic:
        forward.append((count - 1, 0))
    backward = [(target, source) for source, target in forward]
    return forward, backward


FB = 32

def keep_edges(block_ref, top_ref, bottom_ref, ends_ref):
    feats, rows, cols = block_ref.shape
    for f in range(feats):
        top_ref[f] = block_ref[f, 0:1, :]
        bottom_ref[f] = block_ref[f, rows - 1:rows, :]
    lane = lax.broadcasted_iota(jnp.int32, (2, cols), 1)
    which = lax.broadcasted_iota(jnp.int32, (2, cols), 0)
    pick = (lane == which * (cols - 1)).astype(jnp.float32)
    ends_ref[...] = lax.dot_general(
        pick, block_ref[...].reshape(feats * rows, cols), (((1,), (1,)), ((), ())),
        precision=lax.Precision.HIGHEST, preferred_element_type=jnp.float32,
    )


def sweep_kernel(q_ref, hn_ref, hs_ref, he_ref, hw_ref, u_ref, v_ref, k_ref, o_ref, *edge_refs):
    rows, cols = q_ref.shape[1], q_ref.shape[2]
    row = lax.broadcasted_iota(jnp.int32, (rows, cols), 0)
    lane = lax.broadcasted_iota(jnp.int32, (rows, cols), 1)
    he = he_ref[0]
    hw = hw_ref[0]
    for f in range(FB):
        q = q_ref[f]
        north = jnp.where(row == rows - 1, jnp.broadcast_to(hn_ref[f], (rows, cols)), pltpu.roll(q, rows - 1, 0))
        south = jnp.where(row == 0, jnp.broadcast_to(hs_ref[f], (rows, cols)), pltpu.roll(q, 1, 0))
        east = jnp.where(lane == cols - 1, jnp.broadcast_to(he[:, f:f + 1], (rows, cols)), pltpu.roll(q, cols - 1, 1))
        west = jnp.where(lane == 0, jnp.broadcast_to(hw[:, f:f + 1], (rows, cols)), pltpu.roll(q, 1, 1))
        u = u_ref[f]
        v = v_ref[f]
        k = k_ref[f]
        o_ref[f] = (q - 0.5 * u * (east - west) - 0.5 * v * (north - south)
                    + k * (east + west + north + south - 4.0 * q))
    if edge_refs:
        keep_edges(o_ref, *edge_refs)


def sweep(q, halos, u, v, k, emit_edges):
    feats, rows, cols = q.shape
    levels = u.shape[0]
    nb = feats // FB
    per = levels // FB
    big = pl.BlockSpec((FB, rows, cols), lambda i: (i, 0, 0))
    field = pl.BlockSpec((FB, rows, cols), lambda i: (i % per, 0, 0))
    edge_row = pl.BlockSpec((FB, 1, cols), lambda i: (i, 0, 0))
    edge_col = pl.BlockSpec((1, rows, FB), lambda i: (i, 0, 0))
    out_specs, out_shape = [big], [jax.ShapeDtypeStruct(q.shape, q.dtype)]
    if emit_edges:
        out_specs += [edge_row, edge_row, pl.BlockSpec((2, FB * rows), lambda i: (0, i))]
        out_shape += [
            jax.ShapeDtypeStruct((feats, 1, cols), jnp.float32),
            jax.ShapeDtypeStruct((feats, 1, cols), jnp.float32),
            jax.ShapeDtypeStruct((2, feats * rows), jnp.float32),
        ]
    return pl.pallas_call(
        sweep_kernel,
        grid=(nb,),
        in_specs=[big, edge_row, edge_row, edge_col, edge_col, field, field, field],
        out_specs=out_specs,
        out_shape=out_shape,
        cost_estimate=pl.CostEstimate(flops=20 * q.size, bytes_accessed=8 * q.size + 12 * u.size, transcendentals=0),
    )(q, *halos, u, v, k)


def columns_of(edge):
    feats, rows = edge.shape
    return jnp.swapaxes(edge.reshape(feats // FB, FB, rows), 1, 2)


def exchange(top, bottom, ends, feats, rows):
    lat_forward, lat_backward = neighbours("lat", False)
    lon_forward, lon_backward = neighbours("lon", True)
    hn = lax.ppermute(top, "lat", lat_backward)
    hs = lax.ppermute(bottom, "lat", lat_forward)
    he = lax.ppermute(columns_of(ends[0].reshape(feats, rows)), "lon", lon_backward)
    hw = lax.ppermute(columns_of(ends[1].reshape(feats, rows)), "lon", lon_forward)
    return hn, hs, he, hw


def edges(x):
    feats, rows, cols = x.shape
    lane = lax.broadcasted_iota(jnp.int32, (cols, 2), 0)
    which = lax.broadcasted_iota(jnp.int32, (cols, 2), 1)
    pick = (lane == which * (cols - 1)).astype(jnp.float32)
    ends = jnp.dot(x.reshape(feats * rows, cols), pick, precision=lax.Precision.HIGHEST)
    ends_t, top, bottom = lax.optimization_barrier((ends.T, x[:, :1, :], x[:, rows - 1:, :]))
    return top, bottom, ends_t


def positions(targets_all, experts):
    count = targets_all.shape[0]
    block = 128
    onehot = (targets_all[:, None] == jnp.arange(experts, dtype=jnp.int32)[None, :]).astype(
        jnp.bfloat16
    )
    blocks = onehot.reshape(count // block, block, experts)
    rows = jnp.arange(block, dtype=jnp.int32)
    before = (rows[:, None] > rows[None, :]).astype(jnp.bfloat16)
    within = jnp.einsum("ij,bje->bie", before, blocks, preferred_element_type=jnp.float32)
    totals = jnp.sum(blocks.astype(jnp.float32), axis=1)
    offsets = jnp.cumsum(totals, axis=0) - totals
    ranks = within + offsets[:, None, :]
    position = jnp.sum(ranks * blocks.astype(jnp.float32), axis=2)
    return position.reshape(count).astype(jnp.int32)


ROWS = 1024
HALF = 256


def silu(t):
    return t * (0.5 * jnp.tanh(0.5 * t) + 0.5)


def layers(x, w_first, w_middle, w_last):
    hidden = silu(jnp.dot(x, w_first, preferred_element_type=jnp.float32)).astype(jnp.bfloat16)
    for layer_index in range(w_middle.shape[0]):
        hidden = silu(
            jnp.dot(hidden, w_middle[layer_index], preferred_element_type=jnp.float32)
        ).astype(jnp.bfloat16)
    return jnp.dot(hidden, w_last, preferred_element_type=jnp.float32).astype(jnp.bfloat16)


def network_kernel(nonzero_ref, x_hbm, first_ref, middle_ref, last_ref, o_hbm, buf, res, lsem, ssem, source_ref, used_ref):
    block = pl.program_id(0)
    blocks = pl.num_programs(0)
    per = ROWS // HALF
    groups = source_ref.shape[0]

    @pl.when(block == 0)
    def _():
        def nonempty(g, used):
            @pl.when(nonzero_ref[g] > 0)
            def _():
                source_ref[used] = g

            return used + nonzero_ref[g]

        used = lax.fori_loop(0, groups, nonempty, 0)
        used_ref[0] = used

        def empty(g, at):
            @pl.when(nonzero_ref[g] == 0)
            def _():
                source_ref[at] = g

            return at + 1 - nonzero_ref[g]

        lax.fori_loop(0, groups, empty, used)

    active = (used_ref[0] * HALF + ROWS - 1) // ROWS
    slot = block % 2

    def loads(index, into):
        return [
            pltpu.make_async_copy(
                x_hbm.at[pl.ds(source_ref[index * per + j] * HALF, HALF)],
                buf.at[into, pl.ds(j * HALF, HALF)],
                lsem.at[into, j],
            )
            for j in range(per)
        ]

    def stores(index, outof):
        return [
            pltpu.make_async_copy(
                res.at[outof, pl.ds(j * HALF, HALF)],
                o_hbm.at[pl.ds(source_ref[index * per + j] * HALF, HALF)],
                ssem.at[outof, j],
            )
            for j in range(per)
        ]

    @pl.when((block == 0) & (active > 0))
    def _():
        for copy in loads(0, 0):
            copy.start()

    @pl.when(block + 1 < active)
    def _():
        for copy in loads(block + 1, 1 - slot):
            copy.start()

    @pl.when(block >= 2)
    def _():
        for copy in stores(block - 2, slot):
            copy.wait()

    @pl.when(block < active)
    def _():
        for copy in loads(block, slot):
            copy.wait()
        res[slot] = layers(buf[slot], first_ref[...], middle_ref[...], last_ref[...])

    @pl.when(block >= active)
    def _():
        res[slot] = jnp.zeros(res.shape[1:], res.dtype)

    for copy in stores(block, slot):
        copy.start()

    @pl.when(block == blocks - 1)
    def _():
        for copy in stores(block - 1, 1 - slot):
            copy.wait()
        for copy in stores(block, slot):
            copy.wait()


def network(rows_in, input_weight, middle_weight, output_weight):
    count, feats = rows_in.shape
    groups = count // HALF
    hid = input_weight.shape[1]
    first = input_weight[0].T
    middle = jnp.swapaxes(middle_weight[0], 1, 2)
    last = output_weight[0].T
    grouped = rows_in.reshape(groups, HALF, feats)
    nonzero = jnp.any(grouped != 0, axis=(1, 2)).astype(jnp.int32)
    mats = 2 * (hid * feats * 2 + middle_weight.shape[1] * hid * hid)
    per = ROWS // HALF
    return pl.pallas_call(
        network_kernel,
        grid_spec=pltpu.PrefetchScalarGridSpec(
            num_scalar_prefetch=1,
            grid=(count // ROWS,),
            in_specs=[
                pl.BlockSpec(memory_space=pl.ANY),
                pl.BlockSpec(first.shape, lambda i, n: (0, 0)),
                pl.BlockSpec(middle.shape, lambda i, n: (0, 0, 0)),
                pl.BlockSpec(last.shape, lambda i, n: (0, 0)),
            ],
            out_specs=pl.BlockSpec(memory_space=pl.ANY),
            scratch_shapes=[
                pltpu.VMEM((2, ROWS, feats), jnp.bfloat16),
                pltpu.VMEM((2, ROWS, feats), jnp.bfloat16),
                pltpu.SemaphoreType.DMA((2, per)),
                pltpu.SemaphoreType.DMA((2, per)),
                pltpu.SMEM((groups,), jnp.int32),
                pltpu.SMEM((1,), jnp.int32),
            ],
        ),
        out_shape=jax.ShapeDtypeStruct((count, feats), jnp.bfloat16),
        cost_estimate=pl.CostEstimate(
            flops=mats * count,
            bytes_accessed=4 * count * feats + 2 * (mats // 2),
            transcendentals=(1 + middle_weight.shape[1]) * hid * count,
        ),
    )(nonzero, rows_in, first, middle, last)


UNROLL = 32


def pack_kernel(t_ref, cur_ref, o_ref, rows, full):
    feats, lat_cells, lon_cells = cur_ref.shape
    for r in range(lat_cells):
        rows[r * lon_cells:(r + 1) * lon_cells, :] = cur_ref[:, r, :].T
    full[...] = jnp.zeros(full.shape, full.dtype)

    def body(i, carry):
        for u in range(UNROLL):
            c = i * UNROLL + u
            full[pl.ds(t_ref[c], 1), :] = rows[pl.ds(c, 1), :]
        return carry

    lax.fori_loop(0, rows.shape[0] // UNROLL, body, 0)
    o_ref[...] = full[...].astype(o_ref.dtype)


def pack(targets, current, slots):
    feats, lat_cells, lon_cells = current.shape
    count = lat_cells * lon_cells
    return pl.pallas_call(
        pack_kernel,
        grid_spec=pltpu.PrefetchScalarGridSpec(
            num_scalar_prefetch=1,
            grid=(1,),
            in_specs=[pl.BlockSpec(current.shape, lambda i, t: (0, 0, 0))],
            out_specs=pl.BlockSpec((slots, feats), lambda i, t: (0, 0)),
            scratch_shapes=[pltpu.VMEM((count, feats), jnp.float32), pltpu.VMEM((slots, feats), jnp.float32)],
        ),
        out_shape=jax.ShapeDtypeStruct((slots, feats), jnp.bfloat16),
    )(targets, current)


def combine_kernel(t_ref, ret_ref, cur_ref, o_ref, full, tend):
    feats, lat_cells, lon_cells = cur_ref.shape
    full[...] = ret_ref[...].astype(jnp.float32)

    def body(i, carry):
        for u in range(UNROLL):
            c = i * UNROLL + u
            tend[pl.ds(c, 1), :] = full[pl.ds(t_ref[c], 1), :]
        return carry

    lax.fori_loop(0, tend.shape[0] // UNROLL, body, 0)
    for r in range(lat_cells):
        o_ref[:, r, :] = cur_ref[:, r, :] + tend[r * lon_cells:(r + 1) * lon_cells, :].T


def combine(targets, returned_rows, current):
    feats, lat_cells, lon_cells = current.shape
    slots = returned_rows.shape[0]
    return pl.pallas_call(
        combine_kernel,
        grid_spec=pltpu.PrefetchScalarGridSpec(
            num_scalar_prefetch=1,
            grid=(1,),
            in_specs=[
                pl.BlockSpec((slots, feats), lambda i, t: (0, 0)),
                pl.BlockSpec(current.shape, lambda i, t: (0, 0, 0)),
            ],
            out_specs=pl.BlockSpec(current.shape, lambda i, t: (0, 0, 0)),
            scratch_shapes=[
                pltpu.VMEM((slots, feats), jnp.float32),
                pltpu.VMEM((lat_cells * lon_cells, feats), jnp.float32),
            ],
        ),
        out_shape=jax.ShapeDtypeStruct(current.shape, jnp.float32),
    )(targets, returned_rows, current)


def local(
    column_state, wind_speed, diffusivity, batch_index, input_weight, middle_weight, output_weight
):
    num_vars, levels, lat_cells, lon_cells = column_state.shape
    features = num_vars * levels
    current = column_state.reshape(features, lat_cells, lon_cells)
    sides = edges(current)
    for sweep_index in range(2):
        halos = exchange(*sides, features, lat_cells)
        current, *sides = sweep(current, halos, wind_speed[0], wind_speed[1], diffusivity, sweep_index == 0)
    column_count = lat_cells * lon_cells
    experts = lax.axis_size("lon")
    capacity = 2 * column_count // experts
    targets_all = batch_index.reshape(column_count)
    position = positions(targets_all, experts)
    targets = targets_all * capacity + position
    packed = pack(targets, current, experts * capacity).T.reshape(features, experts, capacity)
    chunks = 1
    width = capacity // chunks
    answers = []
    for chunk in range(chunks):
        part = packed[:, :, chunk * width:(chunk + 1) * width]
        received = lax.all_to_all(part, "lon", split_axis=1, concat_axis=1, tiled=True)
        rows_in = received.reshape(features, experts * width).T
        result = network(rows_in, input_weight, middle_weight, output_weight).T
        answers.append(
            lax.all_to_all(result.reshape(features, experts, width), "lon", split_axis=1, concat_axis=1, tiled=True)
        )
    returned = jnp.concatenate(answers, axis=2)
    return combine(targets, returned.reshape(features, -1).T, current).reshape(column_state.shape)


def solution(mesh):
    in_specs = (
        P(None, None, "lat", "lon"),
        P(None, None, "lat", "lon"),
        P(None, "lat", "lon"),
        P("lat", "lon", None),
        P("lon", None, None),
        P("lon", None, None, None),
        P("lon", None, None),
    )
    out_specs = P(None, None, "lat", "lon")
    return jax.shard_map(local, mesh=mesh, in_specs=in_specs, out_specs=out_specs, check_vma=False)
```

```python
import jax
import jax.numpy as jnp
from jax import lax
from jax.experimental import pallas as pl
from jax.experimental.pallas import tpu as pltpu
from jax.sharding import PartitionSpec as P


def neighbours(axis, periodic):
    count = lax.axis_size(axis)
    forward = [(i, i + 1) for i in range(count - 1)]
    if periodic:
        forward.append((count - 1, 0))
    backward = [(target, source) for source, target in forward]
    return forward, backward


FB = 32

def keep_edges(block_ref, top_ref, bottom_ref, ends_ref):
    feats, rows, cols = block_ref.shape
    for f in range(feats):
        top_ref[f] = block_ref[f, 0:1, :]
        bottom_ref[f] = block_ref[f, rows - 1:rows, :]
    lane = lax.broadcasted_iota(jnp.int32, (2, cols), 1)
    which = lax.broadcasted_iota(jnp.int32, (2, cols), 0)
    pick = (lane == which * (cols - 1)).astype(jnp.float32)
    ends_ref[...] = lax.dot_general(
        pick, block_ref[...].reshape(feats * rows, cols), (((1,), (1,)), ((), ())),
        precision=lax.Precision.HIGHEST, preferred_element_type=jnp.float32,
    )


def sweep_kernel(q_ref, hn_ref, hs_ref, he_ref, hw_ref, u_ref, v_ref, k_ref, o_ref, *edge_refs):
    rows, cols = q_ref.shape[1], q_ref.shape[2]
    row = lax.broadcasted_iota(jnp.int32, (rows, cols), 0)
    lane = lax.broadcasted_iota(jnp.int32, (rows, cols), 1)
    he = he_ref[0]
    hw = hw_ref[0]
    for f in range(FB):
        q = q_ref[f]
        north = jnp.where(row == rows - 1, jnp.broadcast_to(hn_ref[f], (rows, cols)), pltpu.roll(q, rows - 1, 0))
        south = jnp.where(row == 0, jnp.broadcast_to(hs_ref[f], (rows, cols)), pltpu.roll(q, 1, 0))
        east = jnp.where(lane == cols - 1, jnp.broadcast_to(he[:, f:f + 1], (rows, cols)), pltpu.roll(q, cols - 1, 1))
        west = jnp.where(lane == 0, jnp.broadcast_to(hw[:, f:f + 1], (rows, cols)), pltpu.roll(q, 1, 1))
        u = u_ref[f]
        v = v_ref[f]
        k = k_ref[f]
        o_ref[f] = (q - 0.5 * u * (east - west) - 0.5 * v * (north - south)
                    + k * (east + west + north + south - 4.0 * q))
    if edge_refs:
        keep_edges(o_ref, *edge_refs)


def sweep(q, halos, u, v, k, emit_edges):
    feats, rows, cols = q.shape
    levels = u.shape[0]
    nb = feats // FB
    per = levels // FB
    big = pl.BlockSpec((FB, rows, cols), lambda i: (i, 0, 0))
    field = pl.BlockSpec((FB, rows, cols), lambda i: (i % per, 0, 0))
    edge_row = pl.BlockSpec((FB, 1, cols), lambda i: (i, 0, 0))
    edge_col = pl.BlockSpec((1, rows, FB), lambda i: (i, 0, 0))
    out_specs, out_shape = [big], [jax.ShapeDtypeStruct(q.shape, q.dtype)]
    if emit_edges:
        out_specs += [edge_row, edge_row, pl.BlockSpec((2, FB * rows), lambda i: (0, i))]
        out_shape += [
            jax.ShapeDtypeStruct((feats, 1, cols), jnp.float32),
            jax.ShapeDtypeStruct((feats, 1, cols), jnp.float32),
            jax.ShapeDtypeStruct((2, feats * rows), jnp.float32),
        ]
    return pl.pallas_call(
        sweep_kernel,
        grid=(nb,),
        in_specs=[big, edge_row, edge_row, edge_col, edge_col, field, field, field],
        out_specs=out_specs,
        out_shape=out_shape,
        cost_estimate=pl.CostEstimate(flops=20 * q.size, bytes_accessed=8 * q.size + 12 * u.size, transcendentals=0),
    )(q, *halos, u, v, k)


def columns_of(edge):
    feats, rows = edge.shape
    return jnp.swapaxes(edge.reshape(feats // FB, FB, rows), 1, 2)


def exchange(top, bottom, ends, feats, rows):
    lat_forward, lat_backward = neighbours("lat", False)
    lon_forward, lon_backward = neighbours("lon", True)
    hn = lax.ppermute(top, "lat", lat_backward)
    hs = lax.ppermute(bottom, "lat", lat_forward)
    he = lax.ppermute(columns_of(ends[0].reshape(feats, rows)), "lon", lon_backward)
    hw = lax.ppermute(columns_of(ends[1].reshape(feats, rows)), "lon", lon_forward)
    return hn, hs, he, hw


def edges(x):
    feats, rows, cols = x.shape
    lane = lax.broadcasted_iota(jnp.int32, (cols, 2), 0)
    which = lax.broadcasted_iota(jnp.int32, (cols, 2), 1)
    pick = (lane == which * (cols - 1)).astype(jnp.float32)
    ends = jnp.dot(x.reshape(feats * rows, cols), pick, precision=lax.Precision.HIGHEST)
    ends_t, top, bottom = lax.optimization_barrier((ends.T, x[:, :1, :], x[:, rows - 1:, :]))
    return top, bottom, ends_t


def positions(targets_all, experts):
    count = targets_all.shape[0]
    block = 128
    onehot = (targets_all[:, None] == jnp.arange(experts, dtype=jnp.int32)[None, :]).astype(
        jnp.bfloat16
    )
    blocks = onehot.reshape(count // block, block, experts)
    rows = jnp.arange(block, dtype=jnp.int32)
    before = (rows[:, None] > rows[None, :]).astype(jnp.bfloat16)
    within = jnp.einsum("ij,bje->bie", before, blocks, preferred_element_type=jnp.float32)
    totals = jnp.sum(blocks.astype(jnp.float32), axis=1)
    offsets = jnp.cumsum(totals, axis=0) - totals
    ranks = within + offsets[:, None, :]
    position = jnp.sum(ranks * blocks.astype(jnp.float32), axis=2)
    return position.reshape(count).astype(jnp.int32)


ROWS = 1024
HALF = 128


def silu(t):
    return t * (0.5 * jnp.tanh(0.5 * t) + 0.5)


def layers(x, w_first, w_middle, w_last):
    hidden = silu(jnp.dot(x, w_first, preferred_element_type=jnp.float32)).astype(jnp.bfloat16)
    for layer_index in range(w_middle.shape[0]):
        hidden = silu(
            jnp.dot(hidden, w_middle[layer_index], preferred_element_type=jnp.float32)
        ).astype(jnp.bfloat16)
    return jnp.dot(hidden, w_last, preferred_element_type=jnp.float32).astype(jnp.bfloat16)


def network_kernel(nonzero_ref, x_hbm, first_ref, middle_ref, last_ref, o_hbm, buf, res, lsem, ssem, source_ref, used_ref):
    block = pl.program_id(0)
    blocks = pl.num_programs(0)
    per = ROWS // HALF
    groups = source_ref.shape[0]

    @pl.when(block == 0)
    def _():
        def nonempty(g, used):
            @pl.when(nonzero_ref[g] > 0)
            def _():
                source_ref[used] = g

            return used + nonzero_ref[g]

        used = lax.fori_loop(0, groups, nonempty, 0)
        used_ref[0] = used

        def empty(g, at):
            @pl.when(nonzero_ref[g] == 0)
            def _():
                source_ref[at] = g

            return at + 1 - nonzero_ref[g]

        lax.fori_loop(0, groups, empty, used)

    active = (used_ref[0] * HALF + ROWS - 1) // ROWS
    slot = block % 2

    def loads(index, into):
        return [
            pltpu.make_async_copy(
                x_hbm.at[pl.ds(source_ref[index * per + j] * HALF, HALF)],
                buf.at[into, pl.ds(j * HALF, HALF)],
                lsem.at[into, j],
            )
            for j in range(per)
        ]

    def stores(index, outof):
        return [
            pltpu.make_async_copy(
                res.at[outof, pl.ds(j * HALF, HALF)],
                o_hbm.at[pl.ds(source_ref[index * per + j] * HALF, HALF)],
                ssem.at[outof, j],
            )
            for j in range(per)
        ]

    @pl.when((block == 0) & (active > 0))
    def _():
        for copy in loads(0, 0):
            copy.start()

    @pl.when(block + 1 < active)
    def _():
        for copy in loads(block + 1, 1 - slot):
            copy.start()

    @pl.when(block >= 2)
    def _():
        for copy in stores(block - 2, slot):
            copy.wait()

    @pl.when(block < active)
    def _():
        for copy in loads(block, slot):
            copy.wait()
        res[slot] = layers(buf[slot], first_ref[...], middle_ref[...], last_ref[...])

    @pl.when(block >= active)
    def _():
        res[slot] = jnp.zeros(res.shape[1:], res.dtype)

    for copy in stores(block, slot):
        copy.start()

    @pl.when(block == blocks - 1)
    def _():
        for copy in stores(block - 1, 1 - slot):
            copy.wait()
        for copy in stores(block, slot):
            copy.wait()


def network(rows_in, input_weight, middle_weight, output_weight):
    count, feats = rows_in.shape
    groups = count // HALF
    hid = input_weight.shape[1]
    first = input_weight[0].T
    middle = jnp.swapaxes(middle_weight[0], 1, 2)
    last = output_weight[0].T
    grouped = rows_in.reshape(groups, HALF, feats)
    nonzero = jnp.any(grouped != 0, axis=(1, 2)).astype(jnp.int32)
    mats = 2 * (hid * feats * 2 + middle_weight.shape[1] * hid * hid)
    per = ROWS // HALF
    return pl.pallas_call(
        network_kernel,
        grid_spec=pltpu.PrefetchScalarGridSpec(
            num_scalar_prefetch=1,
            grid=(count // ROWS,),
            in_specs=[
                pl.BlockSpec(memory_space=pl.ANY),
                pl.BlockSpec(first.shape, lambda i, n: (0, 0)),
                pl.BlockSpec(middle.shape, lambda i, n: (0, 0, 0)),
                pl.BlockSpec(last.shape, lambda i, n: (0, 0)),
            ],
            out_specs=pl.BlockSpec(memory_space=pl.ANY),
            scratch_shapes=[
                pltpu.VMEM((2, ROWS, feats), jnp.bfloat16),
                pltpu.VMEM((2, ROWS, feats), jnp.bfloat16),
                pltpu.SemaphoreType.DMA((2, per)),
                pltpu.SemaphoreType.DMA((2, per)),
                pltpu.SMEM((groups,), jnp.int32),
                pltpu.SMEM((1,), jnp.int32),
            ],
        ),
        out_shape=jax.ShapeDtypeStruct((count, feats), jnp.bfloat16),
        cost_estimate=pl.CostEstimate(
            flops=mats * count,
            bytes_accessed=4 * count * feats + 2 * (mats // 2),
            transcendentals=(1 + middle_weight.shape[1]) * hid * count,
        ),
    )(nonzero, rows_in, first, middle, last)


UNROLL = 64


def pack_kernel(t_ref, cur_ref, o_ref, rows, full):
    feats, lat_cells, lon_cells = cur_ref.shape
    for r in range(lat_cells):
        rows[r * lon_cells:(r + 1) * lon_cells, :] = cur_ref[:, r, :].T
    full[...] = jnp.zeros(full.shape, full.dtype)

    def body(i, carry):
        for u in range(UNROLL):
            c = i * UNROLL + u
            full[pl.ds(t_ref[c], 1), :] = rows[pl.ds(c, 1), :]
        return carry

    lax.fori_loop(0, rows.shape[0] // UNROLL, body, 0)
    o_ref[...] = full[...].astype(o_ref.dtype)


def pack(targets, current, slots):
    feats, lat_cells, lon_cells = current.shape
    count = lat_cells * lon_cells
    return pl.pallas_call(
        pack_kernel,
        grid_spec=pltpu.PrefetchScalarGridSpec(
            num_scalar_prefetch=1,
            grid=(1,),
            in_specs=[pl.BlockSpec(current.shape, lambda i, t: (0, 0, 0))],
            out_specs=pl.BlockSpec((slots, feats), lambda i, t: (0, 0)),
            scratch_shapes=[pltpu.VMEM((count, feats), jnp.float32), pltpu.VMEM((slots, feats), jnp.float32)],
        ),
        out_shape=jax.ShapeDtypeStruct((slots, feats), jnp.bfloat16),
    )(targets, current)


def combine_kernel(t_ref, ret_ref, cur_ref, o_ref, full, tend):
    feats, lat_cells, lon_cells = cur_ref.shape
    full[...] = ret_ref[...].astype(jnp.float32)

    def body(i, carry):
        for u in range(UNROLL):
            c = i * UNROLL + u
            tend[pl.ds(c, 1), :] = full[pl.ds(t_ref[c], 1), :]
        return carry

    lax.fori_loop(0, tend.shape[0] // UNROLL, body, 0)
    for r in range(lat_cells):
        o_ref[:, r, :] = cur_ref[:, r, :] + tend[r * lon_cells:(r + 1) * lon_cells, :].T


def combine(targets, returned_rows, current):
    feats, lat_cells, lon_cells = current.shape
    slots = returned_rows.shape[0]
    return pl.pallas_call(
        combine_kernel,
        grid_spec=pltpu.PrefetchScalarGridSpec(
            num_scalar_prefetch=1,
            grid=(1,),
            in_specs=[
                pl.BlockSpec((slots, feats), lambda i, t: (0, 0)),
                pl.BlockSpec(current.shape, lambda i, t: (0, 0, 0)),
            ],
            out_specs=pl.BlockSpec(current.shape, lambda i, t: (0, 0, 0)),
            scratch_shapes=[
                pltpu.VMEM((slots, feats), jnp.float32),
                pltpu.VMEM((lat_cells * lon_cells, feats), jnp.float32),
            ],
        ),
        out_shape=jax.ShapeDtypeStruct(current.shape, jnp.float32),
    )(targets, returned_rows, current)


def local(
    column_state, wind_speed, diffusivity, batch_index, input_weight, middle_weight, output_weight
):
    num_vars, levels, lat_cells, lon_cells = column_state.shape
    features = num_vars * levels
    current = column_state.reshape(features, lat_cells, lon_cells)
    sides = edges(current)
    for sweep_index in range(2):
        halos = exchange(*sides, features, lat_cells)
        current, *sides = sweep(current, halos, wind_speed[0], wind_speed[1], diffusivity, sweep_index == 0)
    column_count = lat_cells * lon_cells
    experts = lax.axis_size("lon")
    capacity = 2 * column_count // experts
    targets_all = batch_index.reshape(column_count)
    position = positions(targets_all, experts)
    targets = targets_all * capacity + position
    packed = pack(targets, current, experts * capacity).T.reshape(features, experts, capacity)
    chunks = 1
    width = capacity // chunks
    answers = []
    for chunk in range(chunks):
        part = packed[:, :, chunk * width:(chunk + 1) * width]
        received = lax.all_to_all(part, "lon", split_axis=1, concat_axis=1, tiled=True)
        rows_in = received.reshape(features, experts * width).T
        result = network(rows_in, input_weight, middle_weight, output_weight).T
        answers.append(
            lax.all_to_all(result.reshape(features, experts, width), "lon", split_axis=1, concat_axis=1, tiled=True)
        )
    returned = jnp.concatenate(answers, axis=2)
    return combine(targets, returned.reshape(features, -1).T, current).reshape(column_state.shape)


def solution(mesh):
    in_specs = (
        P(None, None, "lat", "lon"),
        P(None, None, "lat", "lon"),
        P(None, "lat", "lon"),
        P("lat", "lon", None),
        P("lon", None, None),
        P("lon", None, None, None),
        P("lon", None, None),
    )
    out_specs = P(None, None, "lat", "lon")
    return jax.shard_map(local, mesh=mesh, in_specs=in_specs, out_specs=out_specs, check_vma=False)
```

```python
import jax
import jax.numpy as jnp
from jax import lax
from jax.experimental import pallas as pl
from jax.experimental.pallas import tpu as pltpu
from jax.sharding import PartitionSpec as P


def neighbours(axis, periodic):
    count = lax.axis_size(axis)
    forward = [(i, i + 1) for i in range(count - 1)]
    if periodic:
        forward.append((count - 1, 0))
    backward = [(target, source) for source, target in forward]
    return forward, backward


FB = 32

def keep_edges(block_ref, top_ref, bottom_ref, ends_ref):
    feats, rows, cols = block_ref.shape
    for f in range(feats):
        top_ref[f] = block_ref[f, 0:1, :]
        bottom_ref[f] = block_ref[f, rows - 1:rows, :]
    lane = lax.broadcasted_iota(jnp.int32, (2, cols), 1)
    which = lax.broadcasted_iota(jnp.int32, (2, cols), 0)
    pick = (lane == which * (cols - 1)).astype(jnp.float32)
    ends_ref[...] = lax.dot_general(
        pick, block_ref[...].reshape(feats * rows, cols), (((1,), (1,)), ((), ())),
        precision=lax.Precision.HIGHEST, preferred_element_type=jnp.float32,
    )


def sweep_kernel(q_ref, hn_ref, hs_ref, he_ref, hw_ref, u_ref, v_ref, k_ref, o_ref, *edge_refs):
    rows, cols = q_ref.shape[1], q_ref.shape[2]
    row = lax.broadcasted_iota(jnp.int32, (rows, cols), 0)
    lane = lax.broadcasted_iota(jnp.int32, (rows, cols), 1)
    he = he_ref[0]
    hw = hw_ref[0]
    for f in range(FB):
        q = q_ref[f]
        north = jnp.where(row == rows - 1, jnp.broadcast_to(hn_ref[f], (rows, cols)), pltpu.roll(q, rows - 1, 0))
        south = jnp.where(row == 0, jnp.broadcast_to(hs_ref[f], (rows, cols)), pltpu.roll(q, 1, 0))
        east = jnp.where(lane == cols - 1, jnp.broadcast_to(he[:, f:f + 1], (rows, cols)), pltpu.roll(q, cols - 1, 1))
        west = jnp.where(lane == 0, jnp.broadcast_to(hw[:, f:f + 1], (rows, cols)), pltpu.roll(q, 1, 1))
        u = u_ref[f]
        v = v_ref[f]
        k = k_ref[f]
        o_ref[f] = (q - 0.5 * u * (east - west) - 0.5 * v * (north - south)
                    + k * (east + west + north + south - 4.0 * q))
    if edge_refs:
        keep_edges(o_ref, *edge_refs)


def sweep(q, halos, u, v, k, emit_edges):
    feats, rows, cols = q.shape
    levels = u.shape[0]
    nb = feats // FB
    per = levels // FB
    big = pl.BlockSpec((FB, rows, cols), lambda i: (i, 0, 0))
    field = pl.BlockSpec((FB, rows, cols), lambda i: (i % per, 0, 0))
    edge_row = pl.BlockSpec((FB, 1, cols), lambda i: (i, 0, 0))
    edge_col = pl.BlockSpec((1, rows, FB), lambda i: (i, 0, 0))
    out_specs, out_shape = [big], [jax.ShapeDtypeStruct(q.shape, q.dtype)]
    if emit_edges:
        out_specs += [edge_row, edge_row, pl.BlockSpec((2, FB * rows), lambda i: (0, i))]
        out_shape += [
            jax.ShapeDtypeStruct((feats, 1, cols), jnp.float32),
            jax.ShapeDtypeStruct((feats, 1, cols), jnp.float32),
            jax.ShapeDtypeStruct((2, feats * rows), jnp.float32),
        ]
    return pl.pallas_call(
        sweep_kernel,
        grid=(nb,),
        in_specs=[big, edge_row, edge_row, edge_col, edge_col, field, field, field],
        out_specs=out_specs,
        out_shape=out_shape,
        cost_estimate=pl.CostEstimate(flops=20 * q.size, bytes_accessed=8 * q.size + 12 * u.size, transcendentals=0),
    )(q, *halos, u, v, k)


def columns_of(edge):
    feats, rows = edge.shape
    return jnp.swapaxes(edge.reshape(feats // FB, FB, rows), 1, 2)


def exchange(top, bottom, ends, feats, rows):
    lat_forward, lat_backward = neighbours("lat", False)
    lon_forward, lon_backward = neighbours("lon", True)
    hn = lax.ppermute(top, "lat", lat_backward)
    hs = lax.ppermute(bottom, "lat", lat_forward)
    he = lax.ppermute(columns_of(ends[0].reshape(feats, rows)), "lon", lon_backward)
    hw = lax.ppermute(columns_of(ends[1].reshape(feats, rows)), "lon", lon_forward)
    return hn, hs, he, hw


def edges(x):
    feats, rows, cols = x.shape
    lane = lax.broadcasted_iota(jnp.int32, (cols, 2), 0)
    which = lax.broadcasted_iota(jnp.int32, (cols, 2), 1)
    pick = (lane == which * (cols - 1)).astype(jnp.float32)
    ends = jnp.dot(x.reshape(feats * rows, cols), pick, precision=lax.Precision.HIGHEST)
    ends_t, top, bottom = lax.optimization_barrier((ends.T, x[:, :1, :], x[:, rows - 1:, :]))
    return top, bottom, ends_t


def positions(targets_all, experts):
    count = targets_all.shape[0]
    block = 128
    onehot = (targets_all[:, None] == jnp.arange(experts, dtype=jnp.int32)[None, :]).astype(
        jnp.bfloat16
    )
    blocks = onehot.reshape(count // block, block, experts)
    rows = jnp.arange(block, dtype=jnp.int32)
    before = (rows[:, None] > rows[None, :]).astype(jnp.bfloat16)
    within = jnp.einsum("ij,bje->bie", before, blocks, preferred_element_type=jnp.float32)
    totals = jnp.sum(blocks.astype(jnp.float32), axis=1)
    offsets = jnp.cumsum(totals, axis=0) - totals
    ranks = within + offsets[:, None, :]
    position = jnp.sum(ranks * blocks.astype(jnp.float32), axis=2)
    return position.reshape(count).astype(jnp.int32)


ROWS = 1024
HALF = 128


def silu(t):
    return t * (0.5 * jnp.tanh(0.5 * t) + 0.5)


def layers(x, w_first, w_middle, w_last):
    hidden = silu(jnp.dot(x, w_first, preferred_element_type=jnp.float32)).astype(jnp.bfloat16)
    for layer_index in range(w_middle.shape[0]):
        hidden = silu(
            jnp.dot(hidden, w_middle[layer_index], preferred_element_type=jnp.float32)
        ).astype(jnp.bfloat16)
    return jnp.dot(hidden, w_last, preferred_element_type=jnp.float32).astype(jnp.bfloat16)


def network_kernel(nonzero_ref, x_hbm, first_ref, middle_ref, last_ref, o_hbm, buf, res, lsem, ssem, source_ref, used_ref):
    block = pl.program_id(0)
    blocks = pl.num_programs(0)
    per = ROWS // HALF
    groups = source_ref.shape[0]

    @pl.when(block == 0)
    def _():
        def nonempty(g, used):
            @pl.when(nonzero_ref[g] > 0)
            def _():
                source_ref[used] = g

            return used + nonzero_ref[g]

        used = lax.fori_loop(0, groups, nonempty, 0)
        used_ref[0] = used

        def empty(g, at):
            @pl.when(nonzero_ref[g] == 0)
            def _():
                source_ref[at] = g

            return at + 1 - nonzero_ref[g]

        lax.fori_loop(0, groups, empty, used)

    active = (used_ref[0] * HALF + ROWS - 1) // ROWS
    slot = block % 2

    def loads(index, into):
        return [
            pltpu.make_async_copy(
                x_hbm.at[pl.ds(source_ref[index * per + j] * HALF, HALF)],
                buf.at[into, pl.ds(j * HALF, HALF)],
                lsem.at[into, j],
            )
            for j in range(per)
        ]

    def stores(index, outof):
        return [
            pltpu.make_async_copy(
                res.at[outof, pl.ds(j * HALF, HALF)],
                o_hbm.at[pl.ds(source_ref[index * per + j] * HALF, HALF)],
                ssem.at[outof, j],
            )
            for j in range(per)
        ]

    @pl.when((block == 0) & (active > 0))
    def _():
        for copy in loads(0, 0):
            copy.start()

    @pl.when(block + 1 < active)
    def _():
        for copy in loads(block + 1, 1 - slot):
            copy.start()

    @pl.when(block >= 2)
    def _():
        for copy in stores(block - 2, slot):
            copy.wait()

    @pl.when(block < active)
    def _():
        for copy in loads(block, slot):
            copy.wait()
        res[slot] = layers(buf[slot], first_ref[...], middle_ref[...], last_ref[...])

    @pl.when(block >= active)
    def _():
        res[slot] = jnp.zeros(res.shape[1:], res.dtype)

    for copy in stores(block, slot):
        copy.start()

    @pl.when(block == blocks - 1)
    def _():
        for copy in stores(block - 1, 1 - slot):
            copy.wait()
        for copy in stores(block, slot):
            copy.wait()


def network(rows_in, input_weight, middle_weight, output_weight):
    count, feats = rows_in.shape
    groups = count // HALF
    hid = input_weight.shape[1]
    first = input_weight[0].T
    middle = jnp.swapaxes(middle_weight[0], 1, 2)
    last = output_weight[0].T
    grouped = rows_in.reshape(groups, HALF, feats)
    nonzero = jnp.any(grouped != 0, axis=(1, 2)).astype(jnp.int32)
    mats = 2 * (hid * feats * 2 + middle_weight.shape[1] * hid * hid)
    per = ROWS // HALF
    return pl.pallas_call(
        network_kernel,
        grid_spec=pltpu.PrefetchScalarGridSpec(
            num_scalar_prefetch=1,
            grid=(count // ROWS,),
            in_specs=[
                pl.BlockSpec(memory_space=pl.ANY),
                pl.BlockSpec(first.shape, lambda i, n: (0, 0)),
                pl.BlockSpec(middle.shape, lambda i, n: (0, 0, 0)),
                pl.BlockSpec(last.shape, lambda i, n: (0, 0)),
            ],
            out_specs=pl.BlockSpec(memory_space=pl.ANY),
            scratch_shapes=[
                pltpu.VMEM((2, ROWS, feats), jnp.bfloat16),
                pltpu.VMEM((2, ROWS, feats), jnp.bfloat16),
                pltpu.SemaphoreType.DMA((2, per)),
                pltpu.SemaphoreType.DMA((2, per)),
                pltpu.SMEM((groups,), jnp.int32),
                pltpu.SMEM((1,), jnp.int32),
            ],
        ),
        out_shape=jax.ShapeDtypeStruct((count, feats), jnp.bfloat16),
        cost_estimate=pl.CostEstimate(
            flops=mats * count,
            bytes_accessed=4 * count * feats + 2 * (mats // 2),
            transcendentals=(1 + middle_weight.shape[1]) * hid * count,
        ),
    )(nonzero, rows_in, first, middle, last)


UNROLL = 128


def pack_kernel(t_ref, cur_ref, o_ref, rows, full):
    feats, lat_cells, lon_cells = cur_ref.shape
    for r in range(lat_cells):
        rows[r * lon_cells:(r + 1) * lon_cells, :] = cur_ref[:, r, :].T
    full[...] = jnp.zeros(full.shape, full.dtype)

    def body(i, carry):
        for u in range(UNROLL):
            c = i * UNROLL + u
            full[pl.ds(t_ref[c], 1), :] = rows[pl.ds(c, 1), :]
        return carry

    lax.fori_loop(0, rows.shape[0] // UNROLL, body, 0)
    o_ref[...] = full[...].astype(o_ref.dtype)


def pack(targets, current, slots):
    feats, lat_cells, lon_cells = current.shape
    count = lat_cells * lon_cells
    return pl.pallas_call(
        pack_kernel,
        grid_spec=pltpu.PrefetchScalarGridSpec(
            num_scalar_prefetch=1,
            grid=(1,),
            in_specs=[pl.BlockSpec(current.shape, lambda i, t: (0, 0, 0))],
            out_specs=pl.BlockSpec((slots, feats), lambda i, t: (0, 0)),
            scratch_shapes=[pltpu.VMEM((count, feats), jnp.float32), pltpu.VMEM((slots, feats), jnp.float32)],
        ),
        out_shape=jax.ShapeDtypeStruct((slots, feats), jnp.bfloat16),
    )(targets, current)


def combine_kernel(t_ref, ret_ref, cur_ref, o_ref, full, tend):
    feats, lat_cells, lon_cells = cur_ref.shape
    full[...] = ret_ref[...].astype(jnp.float32)

    def body(i, carry):
        for u in range(UNROLL):
            c = i * UNROLL + u
            tend[pl.ds(c, 1), :] = full[pl.ds(t_ref[c], 1), :]
        return carry

    lax.fori_loop(0, tend.shape[0] // UNROLL, body, 0)
    for r in range(lat_cells):
        o_ref[:, r, :] = cur_ref[:, r, :] + tend[r * lon_cells:(r + 1) * lon_cells, :].T


def combine(targets, returned_rows, current):
    feats, lat_cells, lon_cells = current.shape
    slots = returned_rows.shape[0]
    return pl.pallas_call(
        combine_kernel,
        grid_spec=pltpu.PrefetchScalarGridSpec(
            num_scalar_prefetch=1,
            grid=(1,),
            in_specs=[
                pl.BlockSpec((slots, feats), lambda i, t: (0, 0)),
                pl.BlockSpec(current.shape, lambda i, t: (0, 0, 0)),
            ],
            out_specs=pl.BlockSpec(current.shape, lambda i, t: (0, 0, 0)),
            scratch_shapes=[
                pltpu.VMEM((slots, feats), jnp.float32),
                pltpu.VMEM((lat_cells * lon_cells, feats), jnp.float32),
            ],
        ),
        out_shape=jax.ShapeDtypeStruct(current.shape, jnp.float32),
    )(targets, returned_rows, current)


def local(
    column_state, wind_speed, diffusivity, batch_index, input_weight, middle_weight, output_weight
):
    num_vars, levels, lat_cells, lon_cells = column_state.shape
    features = num_vars * levels
    current = column_state.reshape(features, lat_cells, lon_cells)
    sides = edges(current)
    for sweep_index in range(2):
        halos = exchange(*sides, features, lat_cells)
        current, *sides = sweep(current, halos, wind_speed[0], wind_speed[1], diffusivity, sweep_index == 0)
    column_count = lat_cells * lon_cells
    experts = lax.axis_size("lon")
    capacity = 2 * column_count // experts
    targets_all = batch_index.reshape(column_count)
    position = positions(targets_all, experts)
    targets = targets_all * capacity + position
    packed = pack(targets, current, experts * capacity).T.reshape(features, experts, capacity)
    chunks = 1
    width = capacity // chunks
    answers = []
    for chunk in range(chunks):
        part = packed[:, :, chunk * width:(chunk + 1) * width]
        received = lax.all_to_all(part, "lon", split_axis=1, concat_axis=1, tiled=True)
        rows_in = received.reshape(features, experts * width).T
        result = network(rows_in, input_weight, middle_weight, output_weight).T
        answers.append(
            lax.all_to_all(result.reshape(features, experts, width), "lon", split_axis=1, concat_axis=1, tiled=True)
        )
    returned = jnp.concatenate(answers, axis=2)
    return combine(targets, returned.reshape(features, -1).T, current).reshape(column_state.shape)


def solution(mesh):
    in_specs = (
        P(None, None, "lat", "lon"),
        P(None, None, "lat", "lon"),
        P(None, "lat", "lon"),
        P("lat", "lon", None),
        P("lon", None, None),
        P("lon", None, None, None),
        P("lon", None, None),
    )
    out_specs = P(None, None, "lat", "lon")
    return jax.shard_map(local, mesh=mesh, in_specs=in_specs, out_specs=out_specs, check_vma=False)
```
